256 devices in a mesh: ctx: 32 (over z, x), kvh: 8 (over y, core).
Axes of the slice: x: 4, y: 4, z: 8, core: 2. Of those that a mesh axis runs over, the one named last changes fastest.
Arguments:
- queries: bfloat16 [12288, 8192], P(('ctx', 'kvh')), may hold values from -150 to 150
- keys: bfloat16 [12288, 1024], P(('ctx', 'kvh')), may hold values from -6 to 6
- values: bfloat16 [12288, 1024], P(('ctx', 'kvh')), may hold values from -6 to 6
- doc_ids: int32 [12288], P('ctx'), may hold values from 0 to 7, never falling along the last dimension, each value on 1 to 6528 neighbouring positions
- block_keep: int32 [96, 96], P('ctx'), may hold values 0 or 1
Outputs:
- attended: bfloat16 [12288, 8192], P(('ctx', 'kvh'))
The draws below stay inside these ranges and needn't reach their ends.
Inputs may be any that keep to these rules, and one draw needn't show every extreme that they name: `doc_ids`: never falls along the sequence; every document holds 1 to 6528 tokens and one holds exactly 6528.
All inputs are finite; a program needn't handle non-finite values. No bound on the sum of `block_keep` on one device may be relied on, other than what follows from the above.
Results may differ from the reference program's by a relative error of at most 0.004.
Values may be sent and summed in bfloat16 or wider, within the bound.
No kernel may reach another device: no remote copies, remote signals or barrier semaphores. Data moves between devices by JAX's collectives and lax.ppermute only.
A program may use at most 64 MiB of HBM per device.

```python
import math
import jax
import jax.numpy as jnp
import numpy as np
from jax import lax

HD = 128
QPK = 8
KVH = 8
HQ = 64
TOK_DEV = 384
BLOCK = 128
TOKENS = 12288
NBLK = 96
DOCS = 8
DOC_MOST = 6528
N_CTX = 32


def shared_keys(key):
    return jax.random.truncated_normal(jax.random.fold_in(key, 11), -6.0, 6.0, (TOKENS, KVH * HD), jnp.float32)


def draw_keys(key, part):
    drawn = shared_keys(key)
    return drawn.astype(jnp.bfloat16)


def draw_queries(key, part):
    drawn = jax.random.truncated_normal(jax.random.fold_in(key, 13), -6.0, 6.0, (TOKENS, HQ * HD), jnp.float32)
    return drawn.astype(jnp.bfloat16)


def with_ends(array, rng, low, high):
    index_at = [jax.random.randint(jax.random.fold_in(rng, axis), (), 0, length) for axis, length in enumerate(array.shape)]
    longest = array.shape.index(max(array.shape))
    neighbour = index_at[:longest] + [(index_at[longest] + 1) % array.shape[longest]] + index_at[longest + 1:]
    return array.at[tuple(index_at)].set(low).at[tuple(neighbour)].set(high)


def shard_levels(own_key, shape, cuts, low, top_value):
    loudness, own = 1.0, jax.random.fold_in(own_key, 6)
    for position, blocks in cuts:
        heights = jnp.exp(jax.random.uniform(jax.random.fold_in(own, position), (blocks,), jnp.float32, low / len(cuts), top_value / len(cuts)))
        loudness = loudness * jnp.repeat(heights, shape[position] // blocks).reshape([-1 if axis == position else 1 for axis in range(len(shape))])
    return loudness


def length_profile(amount, total, most, skew):
    loads = [(1 << 20) // math.isqrt(standing ** skew) + 1 for standing in range(2, amount + 1)]
    spare, counts = total - most - (amount - 1), [1] * (amount - 1)
    while spare > 0:
        movable = [i for i in range(amount - 1) if counts[i] < most]
        mass, remaining = sum([loads[i] for i in movable]), spare
        for i in movable:
            addition = min(most - counts[i], max(1, remaining * loads[i] // mass), spare)
            counts[i] = counts[i] + addition
            spare = spare - addition
    return np.array([most] + counts)


def uneven(stream_key, amount, total, bound, lean):
    if amount == 2:
        one = jax.random.randint(stream_key, (), max(1, total - bound), min(bound, total - 1) + 1)
        return jnp.stack([one, total - one])
    tallies = jnp.asarray(length_profile(amount, total, bound, lean), jnp.int32)
    pairs = (amount - 1) // 2
    source_of, taker = tallies[1:1 + 2 * pairs:2], tallies[2:2 + 2 * pairs:2]
    slack = jnp.minimum(source_of - 1, bound - taker)
    passed = jax.random.randint(jax.random.fold_in(stream_key, 1), (pairs,), 0, 1 << 20) % (slack + 1)
    tallies = tallies.at[1:1 + 2 * pairs:2].set(source_of - passed).at[2:2 + 2 * pairs:2].set(taker + passed)
    return tallies[jax.random.permutation(jax.random.fold_in(stream_key, 2), amount)]


def gaussian(key, shape, width, limit, split=(), kind=jnp.bfloat16):
    array = jax.random.normal(key, shape, jnp.float32) * width
    if len(split) > 0:
        array = shard_levels(key, shape, split, -0.22, 0.18) * array
    return jnp.clip(array, min=-limit, max=limit).astype(kind)


def setup_inputs(seed: int = 0) -> dict:
    key_list = jax.random.split(jax.random.key(seed), 6)
    return {
        "queries": draw_queries(jax.random.fold_in(key_list[5], 71), 0),
        "keys": draw_keys(jax.random.fold_in(key_list[5], 71), 0),
        "values": gaussian(key_list[2], (TOKENS, KVH * HD), 1.0, 6.0, ((0, 256),)),
        "doc_ids": jnp.searchsorted(jnp.cumsum(uneven(key_list[3], DOCS, TOKENS, DOC_MOST, 0)), jnp.arange(TOKENS), side="right").astype(jnp.int32),
        "block_keep": with_ends((jax.random.randint(key_list[4], (NBLK, NBLK), 0, 2) < 1).astype(jnp.int32), jax.random.fold_in(key_list[4], 1), 0, 1),
    }


def reference(queries, keys, values, doc_ids, block_keep):
    tokens = queries.shape[0]
    window = (N_CTX // 2) * TOK_DEV
    q_rows = min(256, tokens)
    key_len = min(window + q_rows, tokens)
    blocks_here = q_rows // BLOCK
    key_blocks = key_len // BLOCK
    query_all = queries.reshape(tokens, KVH, QPK, HD)
    keys_all = keys.reshape(tokens, KVH, HD)
    values_all = values.reshape(tokens, KVH, HD)
    scale = HD ** -0.5

    def one_block(block_index):
        first_row = block_index * q_rows
        key_first = jnp.clip(first_row - window, 0, tokens - key_len).astype(jnp.int32)
        query_blk = lax.dynamic_slice_in_dim(query_all, first_row, q_rows, 0).astype(jnp.float32)
        key_blk = lax.dynamic_slice_in_dim(keys_all, key_first, key_len, 0).astype(jnp.float32)
        value_blk = lax.dynamic_slice_in_dim(values_all, key_first, key_len, 0).astype(jnp.float32)
        query_pos = first_row + jnp.arange(q_rows, dtype=jnp.int32)
        key_pos = key_first + jnp.arange(key_len, dtype=jnp.int32)
        query_doc = lax.dynamic_slice_in_dim(doc_ids, first_row, q_rows, 0)
        key_doc = lax.dynamic_slice_in_dim(doc_ids, key_first, key_len, 0)
        keep_rows = lax.dynamic_slice(block_keep, ((first_row // BLOCK).astype(jnp.int32), (key_first // BLOCK).astype(jnp.int32)), (blocks_here, key_blocks))
        keep_full = jnp.repeat(jnp.repeat(keep_rows, BLOCK, axis=0), BLOCK, axis=1) == 1
        earlier = (key_pos[None, :] < query_pos[:, None]) & (query_pos[:, None] - key_pos[None, :] < window)
        earlier = earlier & (query_doc[:, None] == key_doc[None, :]) & keep_full
        allowed = (key_pos[None, :] == query_pos[:, None]) | earlier
        scores = jnp.einsum('tgqd,kgd->tgqk', query_blk, key_blk) * scale
        mask_full = allowed[:, None, None, :]
        scores = jnp.where(mask_full, scores, -jnp.inf)
        row_max = jnp.max(scores, axis=-1, keepdims=True)
        weights = jnp.where(mask_full, jnp.exp(scores - row_max), 0.0)
        total = jnp.sum(weights, axis=-1)
        rounded = lax.optimization_barrier(weights.astype(jnp.bfloat16)).astype(jnp.float32)
        summed = jnp.einsum('tgqk,kgd->tgqd', rounded, value_blk)
        return (summed / total[..., None]).astype(jnp.bfloat16)

    outputs = lax.map(one_block, jnp.arange(tokens // q_rows, dtype=jnp.int32))
    return outputs.reshape(tokens, KVH * QPK * HD)
```

```python
import functools

import jax
import jax.numpy as jnp
from jax import lax
from jax.experimental import pallas as pl
from jax.experimental.pallas import tpu as pltpu
from jax.sharding import PartitionSpec as P

HD = 128
BLOCK = 128


def attn_kernel(
    kb_tab, kind_tab, cnt_tab, keep_tab, base_ref,
    qdoc_ref, kdoc_ref, q_ref, k_ref, v_ref,
    o_ref,
    m_sc, l_sc, acc_sc,
    *, heads, window,
):
    qbl = pl.program_id(0)
    qpos0 = base_ref[0] + qbl * BLOCK
    scale = HD ** (-0.5)
    rows = qpos0 + lax.broadcasted_iota(jnp.int32, (BLOCK, BLOCK), 0)
    qd = qdoc_ref[...]

    m_sc[...] = jnp.full(m_sc.shape, -1e30, jnp.float32)
    l_sc[...] = jnp.zeros(l_sc.shape, jnp.float32)
    acc_sc[...] = jnp.zeros(acc_sc.shape, jnp.float32)

    def absorb(kb, masked):
        start = pl.multiple_of(kb * BLOCK, BLOCK)
        k = k_ref[pl.ds(start, BLOCK), :]
        v = v_ref[pl.ds(start, BLOCK), :]
        if masked:
            cols = kb * BLOCK + lax.broadcasted_iota(jnp.int32, (BLOCK, BLOCK), 1)
            kd = kdoc_ref[pl.ds(kb, 1), :]
            keep = keep_tab[qbl, kb]
            earlier = (
                (cols < rows)
                & (rows - cols < window)
                & (qd == kd)
                & (keep != 0)
            )
            allowed = (cols == rows) | earlier
        for h in range(heads):
            qh = q_ref[:, h * HD:(h + 1) * HD]
            s = lax.dot_general(
                qh, k, (((1,), (1,)), ((), ())), preferred_element_type=jnp.float32
            ) * scale
            if masked:
                s = jnp.where(allowed, s, -1e30)
            m_prev = m_sc[h]
            m_new = jnp.maximum(m_prev, jnp.max(s, axis=1, keepdims=True))
            alpha = jnp.exp(m_prev - m_new)
            p = jnp.exp(s - m_new)
            l_sc[h] = alpha * l_sc[h] + jnp.sum(p, axis=1, keepdims=True)
            acc_sc[h] = acc_sc[h] * alpha + jnp.dot(
                p.astype(jnp.bfloat16), v, preferred_element_type=jnp.float32
            )
            m_sc[h] = m_new

    def body(n, carry):
        kb = kb_tab[qbl, n]
        kind = kind_tab[qbl, n]

        @pl.when(kind == 0)
        def _():
            absorb(kb, False)

        @pl.when(kind != 0)
        def _():
            absorb(kb, True)

        return carry

    lax.fori_loop(0, cnt_tab[qbl], body, 0)

    for h in range(heads):
        o_ref[:, h * HD:(h + 1) * HD] = (acc_sc[h] / l_sc[h]).astype(o_ref.dtype)


def block_tables(doc_all, keep_rows, first_blk, window):
    nkb = doc_all.shape[0] // BLOCK
    nqb = keep_rows.shape[0]
    nwin = window // BLOCK
    doc_blocks = doc_all.reshape(nkb, BLOCK)
    doc_first = doc_blocks[:, 0]
    doc_last = doc_blocks[:, -1]
    qb = first_blk + jnp.arange(nqb, dtype=jnp.int32)
    kb = qb[:, None] - jnp.arange(nwin + 1, dtype=jnp.int32)[None, :]
    kbc = jnp.clip(kb, 0, nkb - 1)
    keep = jnp.take_along_axis(keep_rows, kbc, axis=1)
    diag = kb == qb[:, None]
    needed = (kb >= 0) & (
        diag | ((keep == 1) & (doc_last[kbc] == doc_first[qb][:, None]))
    )
    full = (
        (~diag)
        & (kb > qb[:, None] - nwin)
        & (doc_first[kbc] == doc_last[qb][:, None])
        & (keep == 1)
    )
    order = jnp.argsort(jnp.where(needed, 0, 1), axis=1, stable=True)
    kb_tab = jnp.take_along_axis(kbc, order, axis=1).astype(jnp.int32)
    kind_tab = jnp.take_along_axis(jnp.where(full, 0, 1), order, axis=1).astype(jnp.int32)
    cnt = jnp.sum(needed, axis=1).astype(jnp.int32)
    return kb_tab, kind_tab, cnt, doc_blocks


def attention(q_local, k_all, v_all, doc_all, doc_q, keep_rows, first_row, window):
    rows_here = q_local.shape[0]
    heads = q_local.shape[1] // HD
    nqb = rows_here // BLOCK
    nk = k_all.shape[0]
    first_blk = first_row // BLOCK
    kb_tab, kind_tab, cnt, doc_blocks = block_tables(doc_all, keep_rows, first_blk, window)
    base = jnp.reshape(first_row, (1,)).astype(jnp.int32)
    kernel = functools.partial(attn_kernel, heads=heads, window=window)
    grid_spec = pltpu.PrefetchScalarGridSpec(
        num_scalar_prefetch=5,
        grid=(nqb,),
        in_specs=[
            pl.BlockSpec((BLOCK, 1), lambda i, *_: (i, 0)),
            pl.BlockSpec((nk // BLOCK, BLOCK), lambda i, *_: (0, 0)),
            pl.BlockSpec((BLOCK, heads * HD), lambda i, *_: (i, 0)),
            pl.BlockSpec((nk, HD), lambda i, *_: (0, 0)),
            pl.BlockSpec((nk, HD), lambda i, *_: (0, 0)),
        ],
        out_specs=pl.BlockSpec((BLOCK, heads * HD), lambda i, *_: (i, 0)),
        scratch_shapes=[
            pltpu.VMEM((heads, BLOCK, 1), jnp.float32),
            pltpu.VMEM((heads, BLOCK, 1), jnp.float32),
            pltpu.VMEM((heads, BLOCK, HD), jnp.float32),
        ],
    )
    return pl.pallas_call(
        kernel,
        grid_spec=grid_spec,
        out_shape=jax.ShapeDtypeStruct((rows_here, heads * HD), q_local.dtype),
    )(
        kb_tab, kind_tab, cnt, keep_rows.astype(jnp.int32), base,
        doc_q.reshape(rows_here, 1), doc_blocks, q_local, k_all, v_all,
    )


def local(queries, keys, values, doc_ids, block_keep):
    query_local = lax.all_to_all(queries, "kvh", split_axis=1, concat_axis=0, tiled=True)
    key_local = lax.all_to_all(keys, "kvh", split_axis=1, concat_axis=0, tiled=True)
    value_local = lax.all_to_all(values, "kvh", split_axis=1, concat_axis=0, tiled=True)
    rows_here = query_local.shape[0]
    window = (lax.axis_size("ctx") // 2) * rows_here
    first_row = lax.axis_index("ctx") * rows_here
    k_all = lax.all_gather(key_local, "ctx", axis=0, tiled=True)
    v_all = lax.all_gather(value_local, "ctx", axis=0, tiled=True)
    doc_all = lax.all_gather(doc_ids, "ctx", axis=0, tiled=True)
    outputs = attention(
        query_local, k_all, v_all, doc_all, doc_ids, block_keep, first_row, window
    )
    return lax.all_to_all(outputs, "kvh", split_axis=0, concat_axis=1, tiled=True)


def solution(mesh):
    return jax.shard_map(
        local,
        mesh=mesh,
        in_specs=(
            P(("ctx", "kvh"), None),
            P(("ctx", "kvh"), None),
            P(("ctx", "kvh"), None),
            P("ctx"),
            P("ctx", None),
        ),
        out_specs=P(("ctx", "kvh"), None),
        check_vma=False,
    )
```

```python
import functools

import jax
import jax.numpy as jnp
from jax import lax
from jax.experimental import pallas as pl
from jax.experimental.pallas import tpu as pltpu
from jax.sharding import PartitionSpec as P

HD = 128
BLOCK = 128


def attn_kernel(
    tab_ref, cnt_ref, keep_ref, base_ref,
    qds_ref, q_ref, k_ref, v_ref,
    o_ref,
    m_sc, l_sc, acc_sc,
    *, heads, window,
):
    qbl = pl.program_id(0)
    qpos0 = base_ref[0] + qbl * BLOCK
    scale = HD ** (-0.5)
    width = heads * BLOCK
    qpos = qpos0 + lax.broadcasted_iota(jnp.int32, (BLOCK, BLOCK), 1)
    krel = lax.broadcasted_iota(jnp.int32, (BLOCK, BLOCK), 0)
    qds = qds_ref[pl.ds(qbl, 1), :]
    qmat = q_ref[...].reshape(width, HD)

    m_sc[...] = jnp.full(m_sc.shape, -1e30, jnp.float32)
    l_sc[...] = jnp.zeros(l_sc.shape, jnp.float32)
    acc_sc[...] = jnp.zeros(acc_sc.shape, jnp.float32)

    def absorb(kb, masked):
        start = pl.multiple_of(kb * BLOCK, BLOCK)
        k = k_ref[pl.ds(start, BLOCK), :]
        v = v_ref[pl.ds(start, BLOCK), :]
        s = lax.dot_general(
            k, qmat, (((1,), (1,)), ((), ())), preferred_element_type=jnp.float32
        ) * scale
        if masked:
            kpos = kb * BLOCK + krel
            keep = keep_ref[qbl, kb]
            earlier = (
                (kpos < qpos)
                & (qpos - kpos < window)
                & (kpos >= qds)
                & (keep != 0)
            )
            allowed = (kpos == qpos) | earlier
            s = jnp.where(jnp.tile(allowed, (1, heads)), s, -1e30)
        m_prev = m_sc[...]
        m_new = jnp.maximum(m_prev, jnp.max(s, axis=0, keepdims=True))
        alpha = jnp.exp(m_prev - m_new)
        p = jnp.exp(s - m_new)
        l_sc[...] = alpha * l_sc[...] + jnp.sum(p, axis=0, keepdims=True)
        acc_sc[...] = acc_sc[...] * alpha + lax.dot_general(
            v, p.astype(jnp.bfloat16), (((0,), (0,)), ((), ())),
            preferred_element_type=jnp.float32,
        )
        m_sc[...] = m_new

    def body(n, carry):
        entry = tab_ref[qbl, n]
        kb = entry & 255
        kind = entry >> 8

        @pl.when(kind == 0)
        def _():
            absorb(kb, False)

        @pl.when(kind != 0)
        def _():
            absorb(kb, True)

        return carry

    lax.fori_loop(0, cnt_ref[qbl], body, 0)

    out = acc_sc[...] / l_sc[...]
    for h in range(heads):
        o_ref[:, h * HD:(h + 1) * HD] = out[:, h * BLOCK:(h + 1) * BLOCK].T.astype(o_ref.dtype)


def block_tables(doc_start_q, keep_rows, first_blk, nkb, window):
    nqb = keep_rows.shape[0]
    nwin = window // BLOCK
    ds_blocks = doc_start_q.reshape(nqb, BLOCK)
    ds_first = ds_blocks[:, :1]
    ds_last = ds_blocks[:, -1:]
    qb = first_blk + jnp.arange(nqb, dtype=jnp.int32)[:, None]
    kb = jnp.arange(nkb, dtype=jnp.int32)[None, :]
    diag = kb == qb
    inwin = (kb <= qb) & (kb >= qb - nwin)
    keep = keep_rows == 1
    needed = inwin & (diag | (keep & (kb * BLOCK + BLOCK - 1 >= ds_first)))
    full = needed & (~diag) & (kb > qb - nwin) & (kb * BLOCK >= ds_last) & keep
    sort_key = jnp.where(needed, jnp.where(diag, 0, 1), 2).astype(jnp.int32)
    payload = (kb + 256 * jnp.where(full, 0, 1)).astype(jnp.int32)
    payload = jnp.broadcast_to(payload, sort_key.shape)
    _, tab = lax.sort((sort_key, payload), dimension=1, is_stable=True, num_keys=1)
    cnt = jnp.sum(needed, axis=1).astype(jnp.int32)
    return tab, cnt, ds_blocks


def attention(q_local, k_all, v_all, doc_start_q, keep_rows, first_row, window):
    rows_here = q_local.shape[0]
    heads = q_local.shape[1] // HD
    nqb = rows_here // BLOCK
    nk = k_all.shape[0]
    first_blk = first_row // BLOCK
    tab, cnt, ds_blocks = block_tables(doc_start_q, keep_rows, first_blk, nk // BLOCK, window)
    base = jnp.reshape(first_row, (1,)).astype(jnp.int32)
    q_t = jnp.transpose(q_local.reshape(rows_here, heads, HD), (1, 0, 2))
    kernel = functools.partial(attn_kernel, heads=heads, window=window)
    grid_spec = pltpu.PrefetchScalarGridSpec(
        num_scalar_prefetch=4,
        grid=(nqb,),
        in_specs=[
            pl.BlockSpec((nqb, BLOCK), lambda i, *_: (0, 0)),
            pl.BlockSpec((heads, BLOCK, HD), lambda i, *_: (0, i, 0)),
            pl.BlockSpec((nk, HD), lambda i, *_: (0, 0)),
            pl.BlockSpec((nk, HD), lambda i, *_: (0, 0)),
        ],
        out_specs=pl.BlockSpec((BLOCK, heads * HD), lambda i, *_: (i, 0)),
        scratch_shapes=[
            pltpu.VMEM((1, heads * BLOCK), jnp.float32),
            pltpu.VMEM((1, heads * BLOCK), jnp.float32),
            pltpu.VMEM((HD, heads * BLOCK), jnp.float32),
        ],
    )
    return pl.pallas_call(
        kernel,
        grid_spec=grid_spec,
        out_shape=jax.ShapeDtypeStruct((rows_here, heads * HD), q_local.dtype),
    )(tab, cnt, keep_rows.astype(jnp.int32), base, ds_blocks, q_t, k_all, v_all)


def doc_starts(doc_all, doc_q):
    docs = jnp.arange(8, dtype=jnp.int32)
    start = jnp.sum((doc_all[None, :] < docs[:, None]).astype(jnp.int32), axis=1)
    onehot = doc_q[:, None] == docs[None, :]
    return jnp.sum(jnp.where(onehot, start[None, :], 0), axis=1).astype(jnp.int32)


def local(queries, keys, values, doc_ids, block_keep):
    query_local = lax.all_to_all(queries, "kvh", split_axis=1, concat_axis=0, tiled=True)
    key_local = lax.all_to_all(keys, "kvh", split_axis=1, concat_axis=0, tiled=True)
    value_local = lax.all_to_all(values, "kvh", split_axis=1, concat_axis=0, tiled=True)
    rows_here = query_local.shape[0]
    window = (lax.axis_size("ctx") // 2) * rows_here
    first_row = lax.axis_index("ctx") * rows_here
    k_all = lax.all_gather(key_local, "ctx", axis=0, tiled=True)
    v_all = lax.all_gather(value_local, "ctx", axis=0, tiled=True)
    doc_all = lax.all_gather(doc_ids, "ctx", axis=0, tiled=True)
    outputs = attention(
        query_local, k_all, v_all, doc_starts(doc_all, doc_ids), block_keep, first_row, window
    )
    return lax.all_to_all(outputs, "kvh", split_axis=0, concat_axis=1, tiled=True)


def solution(mesh):
    return jax.shard_map(
        local,
        mesh=mesh,
        in_specs=(
            P(("ctx", "kvh"), None),
            P(("ctx", "kvh"), None),
            P(("ctx", "kvh"), None),
            P("ctx"),
            P("ctx", None),
        ),
        out_specs=P(("ctx", "kvh"), None),
        check_vma=False,
    )
```

```python
import functools

import jax
import jax.numpy as jnp
from jax import lax
from jax.experimental import pallas as pl
from jax.experimental.pallas import tpu as pltpu
from jax.sharding import PartitionSpec as P

HD = 128
BLOCK = 128


def attn_kernel(
    tab_ref, cnt_ref, keep_ref, base_ref,
    qds_ref, q_ref, kv_ref,
    o_ref,
    m_sc, l_sc, acc_sc,
    *, heads, window,
):
    qbl = pl.program_id(0)
    qpos0 = base_ref[0] + qbl * BLOCK
    scale = HD ** (-0.5)
    width = heads * BLOCK
    qpos = qpos0 + lax.broadcasted_iota(jnp.int32, (BLOCK, BLOCK), 1)
    krel = lax.broadcasted_iota(jnp.int32, (BLOCK, BLOCK), 0)
    qds = qds_ref[pl.ds(qbl, 1), :]
    qmat = q_ref[...].reshape(width, HD)

    m_sc[...] = jnp.full(m_sc.shape, -1e30, jnp.float32)
    l_sc[...] = jnp.zeros(l_sc.shape, jnp.float32)
    acc_sc[...] = jnp.zeros(acc_sc.shape, jnp.float32)

    def absorb(kb, masked):
        start = pl.multiple_of(kb * BLOCK, BLOCK)
        k = kv_ref[pl.ds(start, BLOCK), :HD]
        v = kv_ref[pl.ds(start, BLOCK), HD:]
        s = lax.dot_general(
            k, qmat, (((1,), (1,)), ((), ())), preferred_element_type=jnp.float32
        ) * scale
        if masked:
            kpos = kb * BLOCK + krel
            keep = keep_ref[qbl, kb]
            earlier = (
                (kpos < qpos)
                & (qpos - kpos < window)
                & (kpos >= qds)
                & (keep != 0)
            )
            allowed = (kpos == qpos) | earlier
            s = jnp.where(jnp.tile(allowed, (1, heads)), s, -1e30)
        m_prev = m_sc[...]
        m_new = jnp.maximum(m_prev, jnp.max(s, axis=0, keepdims=True))
        alpha = jnp.exp(m_prev - m_new)
        p = jnp.exp(s - m_new)
        l_sc[...] = alpha * l_sc[...] + jnp.sum(p, axis=0, keepdims=True)
        acc_sc[...] = acc_sc[...] * alpha + lax.dot_general(
            v, p.astype(jnp.bfloat16), (((0,), (0,)), ((), ())),
            preferred_element_type=jnp.float32,
        )
        m_sc[...] = m_new

    def body(n, carry):
        entry = tab_ref[qbl, n]
        kb = entry & 255
        kind = entry >> 8

        @pl.when(kind == 0)
        def _():
            absorb(kb, False)

        @pl.when(kind != 0)
        def _():
            absorb(kb, True)

        return carry

    lax.fori_loop(0, cnt_ref[qbl], body, 0)

    out = acc_sc[...] / l_sc[...]
    for h in range(heads):
        o_ref[:, h * HD:(h + 1) * HD] = out[:, h * BLOCK:(h + 1) * BLOCK].T.astype(o_ref.dtype)


def block_tables(doc_start_q, keep_rows, first_blk, nkb, window):
    nqb = keep_rows.shape[0]
    nwin = window // BLOCK
    ds_blocks = doc_start_q.reshape(nqb, BLOCK)
    ds_first = ds_blocks[:, :1]
    ds_last = ds_blocks[:, -1:]
    qb = first_blk + jnp.arange(nqb, dtype=jnp.int32)[:, None]
    kb = jnp.arange(nkb, dtype=jnp.int32)[None, :]
    diag = kb == qb
    inwin = (kb <= qb) & (kb >= qb - nwin)
    keep = keep_rows == 1
    needed = inwin & (diag | (keep & (kb * BLOCK + BLOCK - 1 >= ds_first)))
    full = needed & (~diag) & (kb > qb - nwin) & (kb * BLOCK >= ds_last) & keep
    sort_key = jnp.where(needed, jnp.where(diag, 0, 1), 2).astype(jnp.int32)
    payload = (kb + 256 * jnp.where(full, 0, 1)).astype(jnp.int32)
    payload = jnp.broadcast_to(payload, sort_key.shape)
    _, tab = lax.sort((sort_key, payload), dimension=1, is_stable=True, num_keys=1)
    cnt = jnp.sum(needed, axis=1).astype(jnp.int32)
    return tab, cnt, ds_blocks


def attention(q_local, kv_all, doc_start_q, keep_rows, first_row, window):
    rows_here = q_local.shape[0]
    heads = q_local.shape[1] // HD
    nqb = rows_here // BLOCK
    nk = kv_all.shape[0]
    first_blk = first_row // BLOCK
    tab, cnt, ds_blocks = block_tables(doc_start_q, keep_rows, first_blk, nk // BLOCK, window)
    base = jnp.reshape(first_row, (1,)).astype(jnp.int32)
    q_t = jnp.transpose(q_local.reshape(rows_here, heads, HD), (1, 0, 2))
    kernel = functools.partial(attn_kernel, heads=heads, window=window)
    grid_spec = pltpu.PrefetchScalarGridSpec(
        num_scalar_prefetch=4,
        grid=(nqb,),
        in_specs=[
            pl.BlockSpec((nqb, BLOCK), lambda i, *_: (0, 0)),
            pl.BlockSpec((heads, BLOCK, HD), lambda i, *_: (0, i, 0)),
            pl.BlockSpec((nk, 2 * HD), lambda i, *_: (0, 0)),
        ],
        out_specs=pl.BlockSpec((BLOCK, heads * HD), lambda i, *_: (i, 0)),
        scratch_shapes=[
            pltpu.VMEM((1, heads * BLOCK), jnp.float32),
            pltpu.VMEM((1, heads * BLOCK), jnp.float32),
            pltpu.VMEM((HD, heads * BLOCK), jnp.float32),
        ],
    )
    return pl.pallas_call(
        kernel,
        grid_spec=grid_spec,
        out_shape=jax.ShapeDtypeStruct((rows_here, heads * HD), q_local.dtype),
    )(tab, cnt, keep_rows.astype(jnp.int32), base, ds_blocks, q_t, kv_all)


def doc_starts(doc_ids, first_row):
    docs = jnp.arange(8, dtype=jnp.int32)
    below_local = jnp.sum((doc_ids[None, :] < docs[:, None]).astype(jnp.int32), axis=1)
    start = lax.psum(below_local, "ctx")
    onehot = doc_ids[:, None] == docs[None, :]
    return jnp.sum(jnp.where(onehot, start[None, :], 0), axis=1).astype(jnp.int32)


def local(queries, keys, values, doc_ids, block_keep):
    query_local = lax.all_to_all(queries, "kvh", split_axis=1, concat_axis=0, tiled=True)
    kv = jnp.concatenate(
        [keys.reshape(keys.shape[0], -1, HD), values.reshape(values.shape[0], -1, HD)], axis=2
    ).reshape(keys.shape[0], -1)
    kv_local = lax.all_to_all(kv, "kvh", split_axis=1, concat_axis=0, tiled=True)
    rows_here = query_local.shape[0]
    window = (lax.axis_size("ctx") // 2) * rows_here
    first_row = lax.axis_index("ctx") * rows_here
    kv_all = lax.all_gather(kv_local, "ctx", axis=0, tiled=True)
    outputs = attention(
        query_local, kv_all, doc_starts(doc_ids, first_row), block_keep, first_row, window
    )
    return lax.all_to_all(outputs, "kvh", split_axis=0, concat_axis=1, tiled=True)


def solution(mesh):
    return jax.shard_map(
        local,
        mesh=mesh,
        in_specs=(
            P(("ctx", "kvh"), None),
            P(("ctx", "kvh"), None),
            P(("ctx", "kvh"), None),
            P("ctx"),
            P("ctx", None),
        ),
        out_specs=P(("ctx", "kvh"), None),
        check_vma=False,
    )
```

```python
import functools

import jax
import jax.numpy as jnp
from jax import lax
from jax.experimental import pallas as pl
from jax.experimental.pallas import tpu as pltpu
from jax.sharding import PartitionSpec as P

HD = 128
BLOCK = 128
NX = 4


def attn_kernel(
    tab_ref, cnt_ref, keep_ref, base_ref,
    qds_ref, q_ref, kv_ref,
    o_ref,
    m_sc, l_sc, acc_sc,
    *, heads, window,
):
    qbl = pl.program_id(0)
    qpos0 = base_ref[0] + qbl * BLOCK
    scale = HD ** (-0.5)
    width = heads * BLOCK
    qpos = qpos0 + lax.broadcasted_iota(jnp.int32, (BLOCK, BLOCK), 1)
    krel = lax.broadcasted_iota(jnp.int32, (BLOCK, BLOCK), 0)
    qds = qds_ref[pl.ds(qbl, 1), :]
    qmat = q_ref[...].reshape(width, HD)

    m_sc[...] = jnp.full(m_sc.shape, -1e30, jnp.float32)
    l_sc[...] = jnp.zeros(l_sc.shape, jnp.float32)
    acc_sc[...] = jnp.zeros(acc_sc.shape, jnp.float32)

    def absorb(kb, row_blk, masked):
        start = pl.multiple_of(row_blk * BLOCK, BLOCK)
        k = kv_ref[pl.ds(start, BLOCK), :HD]
        v = kv_ref[pl.ds(start, BLOCK), HD:]
        s = lax.dot_general(
            k, qmat, (((1,), (1,)), ((), ())), preferred_element_type=jnp.float32
        ) * scale
        if masked:
            kpos = kb * BLOCK + krel
            keep = keep_ref[qbl, kb]
            earlier = (
                (kpos < qpos)
                & (qpos - kpos < window)
                & (kpos >= qds)
                & (keep != 0)
            )
            allowed = (kpos == qpos) | earlier
            s = jnp.where(jnp.tile(allowed, (1, heads)), s, -1e30)
        m_prev = m_sc[...]
        m_new = jnp.maximum(m_prev, jnp.max(s, axis=0, keepdims=True))
        alpha = jnp.exp(m_prev - m_new)
        p = jnp.exp(s - m_new)
        l_sc[...] = alpha * l_sc[...] + jnp.sum(p, axis=0, keepdims=True)
        acc_sc[...] = acc_sc[...] * alpha + lax.dot_general(
            v, p.astype(jnp.bfloat16), (((0,), (0,)), ((), ())),
            preferred_element_type=jnp.float32,
        )
        m_sc[...] = m_new

    def body(n, carry):
        entry = tab_ref[qbl, n]
        kb = entry & 255
        row_blk = (entry >> 8) & 255
        kind = entry >> 16

        @pl.when(kind == 0)
        def _():
            absorb(kb, row_blk, False)

        @pl.when(kind != 0)
        def _():
            absorb(kb, row_blk, True)

        return carry

    lax.fori_loop(0, cnt_ref[qbl], body, 0)

    out = acc_sc[...] / l_sc[...]
    for h in range(heads):
        o_ref[:, h * HD:(h + 1) * HD] = out[:, h * BLOCK:(h + 1) * BLOCK].T.astype(o_ref.dtype)


def block_tables(doc_start_q, keep_rows, first_blk, nkb, window, slot_of, n_rows_blk):
    nqb = keep_rows.shape[0]
    nwin = window // BLOCK
    ds_blocks = doc_start_q.reshape(nqb, BLOCK)
    ds_first = ds_blocks[:, :1]
    ds_last = ds_blocks[:, -1:]
    qb = first_blk + jnp.arange(nqb, dtype=jnp.int32)[:, None]
    kb = jnp.arange(nkb, dtype=jnp.int32)[None, :]
    diag = kb == qb
    inwin = (kb <= qb) & (kb >= qb - nwin)
    keep = keep_rows == 1
    needed = inwin & (diag | (keep & (kb * BLOCK + BLOCK - 1 >= ds_first)))
    full = needed & (~diag) & (kb > qb - nwin) & (kb * BLOCK >= ds_last) & keep
    sort_key = jnp.where(needed, jnp.where(diag, 0, 1), 2).astype(jnp.int32)
    row_blk = jnp.clip(slot_of(kb), 0, n_rows_blk - 1)
    payload = (kb + 256 * row_blk + 65536 * jnp.where(full, 0, 1)).astype(jnp.int32)
    payload = jnp.broadcast_to(payload, sort_key.shape)
    _, tab = lax.sort((sort_key, payload), dimension=1, is_stable=True, num_keys=1)
    cnt = jnp.sum(needed, axis=1).astype(jnp.int32)
    return tab, cnt, ds_blocks


def attention(q_local, kv_all, doc_start_q, keep_rows, first_row, window, nkb, slot_of):
    rows_here = q_local.shape[0]
    heads = q_local.shape[1] // HD
    nqb = rows_here // BLOCK
    nk = kv_all.shape[0]
    first_blk = first_row // BLOCK
    tab, cnt, ds_blocks = block_tables(
        doc_start_q, keep_rows, first_blk, nkb, window, slot_of, nk // BLOCK
    )
    base = jnp.reshape(first_row, (1,)).astype(jnp.int32)
    q_t = jnp.transpose(q_local.reshape(rows_here, heads, HD), (1, 0, 2))
    kernel = functools.partial(attn_kernel, heads=heads, window=window)
    grid_spec = pltpu.PrefetchScalarGridSpec(
        num_scalar_prefetch=4,
        grid=(nqb,),
        in_specs=[
            pl.BlockSpec((nqb, BLOCK), lambda i, *_: (0, 0)),
            pl.BlockSpec((heads, BLOCK, HD), lambda i, *_: (0, i, 0)),
            pl.BlockSpec((nk, 2 * HD), lambda i, *_: (0, 0)),
        ],
        out_specs=pl.BlockSpec((BLOCK, heads * HD), lambda i, *_: (i, 0)),
        scratch_shapes=[
            pltpu.VMEM((1, heads * BLOCK), jnp.float32),
            pltpu.VMEM((1, heads * BLOCK), jnp.float32),
            pltpu.VMEM((HD, heads * BLOCK), jnp.float32),
        ],
    )
    return pl.pallas_call(
        kernel,
        grid_spec=grid_spec,
        out_shape=jax.ShapeDtypeStruct((rows_here, heads * HD), q_local.dtype),
    )(tab, cnt, keep_rows.astype(jnp.int32), base, ds_blocks, q_t, kv_all)


def doc_starts(doc_ids, first_row):
    docs = jnp.arange(8, dtype=jnp.int32)
    below_local = jnp.sum((doc_ids[None, :] < docs[:, None]).astype(jnp.int32), axis=1)
    start = lax.psum(below_local, "ctx")
    onehot = doc_ids[:, None] == docs[None, :]
    return jnp.sum(jnp.where(onehot, start[None, :], 0), axis=1).astype(jnp.int32)


def shift(x, pairs):
    return lax.ppermute(x, "ctx", pairs)


def local(queries, keys, values, doc_ids, block_keep):
    query_local = lax.all_to_all(queries, "kvh", split_axis=1, concat_axis=0, tiled=True)
    kv = jnp.concatenate(
        [keys.reshape(keys.shape[0], -1, HD), values.reshape(values.shape[0], -1, HD)], axis=2
    ).reshape(keys.shape[0], -1)
    kv_local = lax.all_to_all(kv, "kvh", split_axis=1, concat_axis=0, tiled=True)
    rows_here = query_local.shape[0]
    per_dev = rows_here // BLOCK
    n_ctx = lax.axis_size("ctx")
    nx = NX
    nz = n_ctx // nx
    reach = n_ctx // 2 // nx
    window = (n_ctx // 2) * rows_here
    ctx = lax.axis_index("ctx")
    first_row = ctx * rows_here

    col = [kv_local]
    z_pairs = [(c, (c + nx) % n_ctx) for c in range(n_ctx)]
    for _ in range(reach):
        col.append(shift(col[-1], z_pairs))
    mids, firsts, lasts = [], [], []
    for d in range(1, nx):
        pairs = [(z * nx + x, z * nx + (x + d) % nx) for z in range(nz) for x in range(nx)]
        for a in range(1, reach):
            mids.append(shift(col[a], pairs))
        first_pairs = [(z * nx + x, z * nx + x + d) for z in range(nz) for x in range(nx - d)]
        last_pairs = [(z * nx + x, z * nx + x + d - nx) for z in range(nz) for x in range(nx - d, nx)]
        firsts.append(shift(col[0], first_pairs))
        lasts.append(shift(col[reach], last_pairs))
    kv_buf = jnp.concatenate(col + mids + firsts + lasts, axis=0)

    zq, xq = ctx // nx, ctx % nx
    n_mid = reach - 1

    def slot_of(kb):
        cp = kb // per_dev
        a = zq - cp // nx
        d = (xq - cp % nx) % nx
        slot = jnp.where(
            d == 0,
            a,
            jnp.where(
                a == 0,
                reach + 1 + (nx - 1) * n_mid + (d - 1),
                jnp.where(
                    a == reach,
                    reach + 1 + (nx - 1) * n_mid + (nx - 1) + (d - 1),
                    reach + 1 + (d - 1) * n_mid + (a - 1),
                ),
            ),
        )
        return slot * per_dev + kb % per_dev

    outputs = attention(
        query_local, kv_buf, doc_starts(doc_ids, first_row), block_keep, first_row, window,
        n_ctx * per_dev, slot_of,
    )
    return lax.all_to_all(outputs, "kvh", split_axis=0, concat_axis=1, tiled=True)


def solution(mesh):
    return jax.shard_map(
        local,
        mesh=mesh,
        in_specs=(
            P(("ctx", "kvh"), None),
            P(("ctx", "kvh"), None),
            P(("ctx", "kvh"), None),
            P("ctx"),
            P("ctx", None),
        ),
        out_specs=P(("ctx", "kvh"), None),
        check_vma=False,
    )
```

```python
import functools

import jax
import jax.numpy as jnp
from jax import lax
from jax.experimental import pallas as pl
from jax.experimental.pallas import tpu as pltpu
from jax.sharding import PartitionSpec as P

HD = 128
BLOCK = 128
NX = 4
N_DOC_IDS = 8


def attn_kernel(
    tab_ref, cnt_ref, keep_ref, base_ref,
    qds_ref, q_ref, kv_ref,
    o_ref,
    m_sc, l_sc, acc_sc,
    *, heads, window,
):
    qbl = pl.program_id(0)
    qpos0 = base_ref[0] + qbl * BLOCK
    scale = HD ** (-0.5)
    width = heads * BLOCK
    qpos = qpos0 + lax.broadcasted_iota(jnp.int32, (BLOCK, BLOCK), 1)
    krel = lax.broadcasted_iota(jnp.int32, (BLOCK, BLOCK), 0)
    qds = qds_ref[pl.ds(qbl, 1), :]
    qmat = q_ref[...].reshape(width, HD)

    m_sc[...] = jnp.full(m_sc.shape, -1e30, jnp.float32)
    l_sc[...] = jnp.zeros(l_sc.shape, jnp.float32)
    acc_sc[...] = jnp.zeros(acc_sc.shape, jnp.float32)

    def absorb(kb, row_blk, masked):
        start = pl.multiple_of(row_blk * 16, 16)
        k = kv_ref[pl.ds(start, BLOCK), :HD]
        v = kv_ref[pl.ds(start, BLOCK), HD:]
        s = lax.dot_general(
            k, qmat, (((1,), (1,)), ((), ())), preferred_element_type=jnp.float32
        ) * scale
        if masked:
            kpos = kb * BLOCK + krel
            keep = keep_ref[qbl, kb]
            earlier = (
                (kpos < qpos)
                & (qpos - kpos < window)
                & (kpos >= qds)
                & (keep != 0)
            )
            allowed = (kpos == qpos) | earlier
            s = jnp.where(jnp.tile(allowed, (1, heads)), s, -1e30)
        m_prev = m_sc[...]
        m_new = jnp.maximum(m_prev, jnp.max(s, axis=0, keepdims=True))
        alpha = jnp.exp(m_prev - m_new)
        p = jnp.exp(s - m_new)
        l_sc[...] = alpha * l_sc[...] + jnp.sum(p, axis=0, keepdims=True)
        acc_sc[...] = acc_sc[...] * alpha + lax.dot_general(
            v, p.astype(jnp.bfloat16), (((0,), (0,)), ((), ())),
            preferred_element_type=jnp.float32,
        )
        m_sc[...] = m_new

    def body(n, carry):
        entry = tab_ref[qbl, n]
        kb = entry & 255
        row_blk = (entry >> 8) & 4095
        kind = entry >> 20

        @pl.when(kind == 0)
        def _():
            absorb(kb, row_blk, False)

        @pl.when(kind != 0)
        def _():
            absorb(kb, row_blk, True)

        return carry

    lax.fori_loop(0, cnt_ref[qbl], body, 0)

    out = acc_sc[...] / l_sc[...]
    for h in range(heads):
        o_ref[:, h * HD:(h + 1) * HD] = out[:, h * BLOCK:(h + 1) * BLOCK].T.astype(o_ref.dtype)


def block_tables(doc_start_q, keep_rows, first_blk, nkb, window, slot_of, n_rows_blk):
    nqb = keep_rows.shape[0]
    nwin = window // BLOCK
    ds_blocks = doc_start_q.reshape(nqb, BLOCK)
    ds_first = ds_blocks[:, :1]
    ds_last = ds_blocks[:, -1:]
    qb = first_blk + jnp.arange(nqb, dtype=jnp.int32)[:, None]
    kb = jnp.arange(nkb, dtype=jnp.int32)[None, :]
    diag = kb == qb
    inwin = (kb <= qb) & (kb >= qb - nwin)
    keep = keep_rows == 1
    needed = inwin & (diag | (keep & (kb * BLOCK + BLOCK - 1 >= ds_first)))
    full = needed & (~diag) & (kb > qb - nwin) & (kb * BLOCK >= ds_last) & keep
    sort_key = jnp.where(needed, jnp.where(diag, 0, 1), 2).astype(jnp.int32)
    row_blk = jnp.clip(slot_of(kb), 0, n_rows_blk - 1)
    payload = (kb + 256 * row_blk + (1 << 20) * jnp.where(full, 0, 1)).astype(jnp.int32)
    payload = jnp.broadcast_to(payload, sort_key.shape)
    _, tab = lax.sort((sort_key, payload), dimension=1, is_stable=True, num_keys=1)
    cnt = jnp.sum(needed, axis=1).astype(jnp.int32)
    return tab, cnt, ds_blocks


def attention(q_local, kv_all, doc_start_q, keep_rows, first_row, window, nkb, slot_of):
    rows_here = q_local.shape[0]
    heads = q_local.shape[1] // HD
    nqb = rows_here // BLOCK
    nk = kv_all.shape[0]
    first_blk = first_row // BLOCK
    tab, cnt, ds_blocks = block_tables(
        doc_start_q, keep_rows, first_blk, nkb, window, slot_of, (nk - BLOCK) // 16
    )
    base = jnp.reshape(first_row, (1,)).astype(jnp.int32)
    q_t = jnp.transpose(q_local.reshape(rows_here, heads, HD), (1, 0, 2))
    kernel = functools.partial(attn_kernel, heads=heads, window=window)
    grid_spec = pltpu.PrefetchScalarGridSpec(
        num_scalar_prefetch=4,
        grid=(nqb,),
        in_specs=[
            pl.BlockSpec((nqb, BLOCK), lambda i, *_: (0, 0)),
            pl.BlockSpec((heads, BLOCK, HD), lambda i, *_: (0, i, 0)),
            pl.BlockSpec((nk, 2 * HD), lambda i, *_: (0, 0)),
        ],
        out_specs=pl.BlockSpec((BLOCK, heads * HD), lambda i, *_: (i, 0)),
        scratch_shapes=[
            pltpu.VMEM((1, heads * BLOCK), jnp.float32),
            pltpu.VMEM((1, heads * BLOCK), jnp.float32),
            pltpu.VMEM((HD, heads * BLOCK), jnp.float32),
        ],
    )
    return pl.pallas_call(
        kernel,
        grid_spec=grid_spec,
        out_shape=jax.ShapeDtypeStruct((rows_here, heads * HD), q_local.dtype),
    )(tab, cnt, keep_rows.astype(jnp.int32), base, ds_blocks, q_t, kv_all)


def shift(x, pairs):
    return lax.ppermute(x, "ctx", pairs)


def local(queries, keys, values, doc_ids, block_keep):
    query_local = lax.all_to_all(queries, "kvh", split_axis=1, concat_axis=0, tiled=True)
    kv = jnp.concatenate(
        [keys.reshape(keys.shape[0], -1, HD), values.reshape(values.shape[0], -1, HD)], axis=2
    ).reshape(keys.shape[0], -1)
    kv_local = lax.all_to_all(kv, "kvh", split_axis=1, concat_axis=0, tiled=True)
    rows_here = query_local.shape[0]
    per_dev = rows_here // BLOCK
    n_ctx = lax.axis_size("ctx")
    nx = NX
    nz = n_ctx // nx
    reach = n_ctx // 2 // nx
    window = (n_ctx // 2) * rows_here
    ctx = lax.axis_index("ctx")
    first_row = ctx * rows_here
    zq, xq = ctx // nx, ctx % nx

    docs = jnp.arange(N_DOC_IDS, dtype=jnp.int32)
    below = jnp.sum((doc_ids[None, :] < docs[:, None]).astype(jnp.int32), axis=1)
    tail = jnp.zeros((16, kv_local.shape[1]), jnp.float32)
    tail = tail.at[0, :N_DOC_IDS].set((below // 32).astype(jnp.float32))
    tail = tail.at[1, :N_DOC_IDS].set((below % 32).astype(jnp.float32))
    piece = jnp.concatenate([kv_local, tail.astype(kv_local.dtype)], axis=0)
    prow = piece.shape[0]

    def z_pairs(k):
        return [(c, (c + k * nx) % n_ctx) for c in range(n_ctx)]

    col1 = shift(piece, z_pairs(1))
    col_far = shift(piece, z_pairs(reach))
    pair23 = shift(jnp.concatenate([piece, col1], axis=0), z_pairs(2))
    col = [piece, col1, pair23[:prow], pair23[prow:], col_far]
    recv = []
    for d in range(1, nx):
        pairs = [(z * nx + x, z * nx + (x + d) % nx) for z in range(nz) for x in range(nx)]
        extra = jnp.where(xq + d < nx, col[0], col[reach])
        recv.append(shift(jnp.concatenate(col[1:reach] + [extra], axis=0), pairs))
    kv_buf = jnp.concatenate(col + recv, axis=0)

    n_slots = reach + 1 + (nx - 1) * reach
    slot_ids = jnp.arange(n_slots, dtype=jnp.int32)
    own_a = jnp.minimum(slot_ids, reach)
    rel = slot_ids - (reach + 1)
    d_s = rel // reach + 1
    a_s = rel % reach + 1
    x_src = (xq - d_s) % nx
    extra_ctx = jnp.where(xq >= d_s, zq * nx + xq - d_s, (zq - reach) * nx + x_src)
    slot_ctx = jnp.where(
        slot_ids <= reach,
        ctx - own_a * nx,
        jnp.where(a_s == reach, extra_ctx, (zq - a_s) * nx + x_src),
    )
    tails = kv_buf.reshape(n_slots, prow, -1)[:, rows_here:rows_here + 2, :N_DOC_IDS]
    tails = tails.astype(jnp.int32)
    below_all = tails[:, 0, :] * 32 + tails[:, 1, :]
    below_all = jnp.where((slot_ctx >= 0)[:, None], below_all, 0)
    floor_row = jnp.maximum(ctx - reach * nx, 0) * rows_here
    below_sum = jnp.sum(below_all, axis=0)
    onehot = doc_ids[:, None] == docs[None, :]
    doc_start = floor_row + jnp.sum(jnp.where(onehot, below_sum[None, :], 0), axis=1)

    def slot_of(kb):
        cp = kb // per_dev
        a = zq - cp // nx
        d = (xq - cp % nx) % nx
        slot = jnp.where(
            d == 0,
            a,
            jnp.where(
                (a == 0) | (a == reach),
                reach + 1 + (d - 1) * reach + (reach - 1),
                reach + 1 + (d - 1) * reach + (a - 1),
            ),
        )
        return (slot * prow + (kb % per_dev) * BLOCK) // 16

    outputs = attention(
        query_local, kv_buf, doc_start.astype(jnp.int32), block_keep, first_row, window,
        n_ctx * per_dev, slot_of,
    )
    return lax.all_to_all(outputs, "kvh", split_axis=0, concat_axis=1, tiled=True)


def solution(mesh):
    return jax.shard_map(
        local,
        mesh=mesh,
        in_specs=(
            P(("ctx", "kvh"), None),
            P(("ctx", "kvh"), None),
            P(("ctx", "kvh"), None),
            P("ctx"),
            P("ctx", None),
        ),
        out_specs=P(("ctx", "kvh"), None),
        check_vma=False,
    )
```

```python
import functools

import jax
import jax.numpy as jnp
from jax import lax
from jax.experimental import pallas as pl
from jax.experimental.pallas import tpu as pltpu
from jax.sharding import PartitionSpec as P

HD = 128
BLOCK = 128
NX = 4
N_DOC_IDS = 8


def attn_kernel(
    tab_ref, cnt_ref, keep_ref, base_ref,
    qds_ref, q_ref, kv_ref,
    o_ref,
    m_sc, l_sc, acc_sc,
    *, heads, window,
):
    qbl = pl.program_id(0)
    qpos0 = base_ref[0] + qbl * BLOCK
    scale = HD ** (-0.5)
    width = heads * BLOCK
    qpos = qpos0 + lax.broadcasted_iota(jnp.int32, (BLOCK, BLOCK), 1)
    krel = lax.broadcasted_iota(jnp.int32, (BLOCK, BLOCK), 0)
    qds = qds_ref[pl.ds(qbl, 1), :]
    qmat = q_ref[...].reshape(width, HD)

    m_sc[...] = jnp.full(m_sc.shape, -1e30, jnp.float32)
    l_sc[...] = jnp.zeros(l_sc.shape, jnp.float32)
    acc_sc[...] = jnp.zeros(acc_sc.shape, jnp.float32)

    def absorb(kb, row_blk, masked):
        start = pl.multiple_of(row_blk * 16, 16)
        k = kv_ref[pl.ds(start, BLOCK), :HD]
        v = kv_ref[pl.ds(start, BLOCK), HD:]
        s = lax.dot_general(
            k, qmat, (((1,), (1,)), ((), ())), preferred_element_type=jnp.float32
        ) * scale
        if masked:
            kpos = kb * BLOCK + krel
            keep = keep_ref[qbl, kb]
            earlier = (
                (kpos < qpos)
                & (qpos - kpos < window)
                & (kpos >= qds)
                & (keep != 0)
            )
            allowed = (kpos == qpos) | earlier
            s = jnp.where(jnp.tile(allowed, (1, heads)), s, -1e30)
        m_prev = m_sc[...]
        m_new = jnp.maximum(m_prev, jnp.max(s, axis=0, keepdims=True))
        alpha = jnp.exp(m_prev - m_new)
        p = jnp.exp(s - m_new)
        l_sc[...] = alpha * l_sc[...] + jnp.sum(p, axis=0, keepdims=True)
        acc_sc[...] = acc_sc[...] * alpha + lax.dot_general(
            v, p.astype(jnp.bfloat16), (((0,), (0,)), ((), ())),
            preferred_element_type=jnp.float32,
        )
        m_sc[...] = m_new

    def body(n, carry):
        entry = tab_ref[qbl, n]
        kb = entry & 255
        row_blk = (entry >> 8) & 4095
        kind = entry >> 20

        @pl.when(kind == 0)
        def _():
            absorb(kb, row_blk, False)

        @pl.when(kind != 0)
        def _():
            absorb(kb, row_blk, True)

        return carry

    lax.fori_loop(0, cnt_ref[qbl], body, 0)

    out = acc_sc[...] / l_sc[...]
    for h in range(heads):
        o_ref[:, h * HD:(h + 1) * HD] = out[:, h * BLOCK:(h + 1) * BLOCK].T.astype(o_ref.dtype)


def block_tables(doc_start_q, keep_rows, first_blk, nkb, window, slot_of, n_rows_blk):
    nqb = keep_rows.shape[0]
    nwin = window // BLOCK
    ds_blocks = doc_start_q.reshape(nqb, BLOCK)
    ds_first = ds_blocks[:, :1]
    ds_last = ds_blocks[:, -1:]
    qb = first_blk + jnp.arange(nqb, dtype=jnp.int32)[:, None]
    kb = jnp.arange(nkb, dtype=jnp.int32)[None, :]
    diag = kb == qb
    inwin = (kb <= qb) & (kb >= qb - nwin)
    keep = keep_rows == 1
    needed = inwin & (diag | (keep & (kb * BLOCK + BLOCK - 1 >= ds_first)))
    full = needed & (~diag) & (kb > qb - nwin) & (kb * BLOCK >= ds_last) & keep
    sort_key = jnp.where(needed, jnp.where(diag, 0, 1), 2).astype(jnp.int32)
    row_blk = jnp.clip(slot_of(kb), 0, n_rows_blk - 1)
    payload = (kb + 256 * row_blk + (1 << 20) * jnp.where(full, 0, 1)).astype(jnp.int32)
    payload = jnp.broadcast_to(payload, sort_key.shape)
    _, tab = lax.sort((sort_key, payload), dimension=1, is_stable=True, num_keys=1)
    cnt = jnp.sum(needed, axis=1).astype(jnp.int32)
    return tab, cnt, ds_blocks


def attention(q_local, kv_all, doc_start_q, keep_rows, first_row, window, nkb, slot_of):
    rows_here = q_local.shape[0]
    heads = q_local.shape[1] // HD
    nqb = rows_here // BLOCK
    nk = kv_all.shape[0]
    first_blk = first_row // BLOCK
    tab, cnt, ds_blocks = block_tables(
        doc_start_q, keep_rows, first_blk, nkb, window, slot_of, (nk - BLOCK) // 16 + 1
    )
    base = jnp.reshape(first_row, (1,)).astype(jnp.int32)
    q_t = jnp.transpose(q_local.reshape(rows_here, heads, HD), (1, 0, 2))
    kernel = functools.partial(attn_kernel, heads=heads, window=window)
    grid_spec = pltpu.PrefetchScalarGridSpec(
        num_scalar_prefetch=4,
        grid=(nqb,),
        in_specs=[
            pl.BlockSpec((nqb, BLOCK), lambda i, *_: (0, 0)),
            pl.BlockSpec((heads, BLOCK, HD), lambda i, *_: (0, i, 0)),
            pl.BlockSpec((nk, 2 * HD), lambda i, *_: (0, 0)),
        ],
        out_specs=pl.BlockSpec((BLOCK, heads * HD), lambda i, *_: (i, 0)),
        scratch_shapes=[
            pltpu.VMEM((1, heads * BLOCK), jnp.float32),
            pltpu.VMEM((1, heads * BLOCK), jnp.float32),
            pltpu.VMEM((HD, heads * BLOCK), jnp.float32),
        ],
    )
    return pl.pallas_call(
        kernel,
        grid_spec=grid_spec,
        out_shape=jax.ShapeDtypeStruct((rows_here, heads * HD), q_local.dtype),
    )(tab, cnt, keep_rows.astype(jnp.int32), base, ds_blocks, q_t, kv_all)


def shift(x, pairs):
    return lax.ppermute(x, "ctx", pairs)


def local(queries, keys, values, doc_ids, block_keep):
    rows_in = keys.shape[0]
    groups = keys.shape[1] // HD
    qkv = jnp.concatenate(
        [
            queries.reshape(rows_in, groups, -1),
            keys.reshape(rows_in, groups, HD),
            values.reshape(rows_in, groups, HD),
        ],
        axis=2,
    ).reshape(rows_in, -1)
    qkv_local = lax.all_to_all(qkv, "kvh", split_axis=1, concat_axis=0, tiled=True)
    q_width = queries.shape[1] // groups
    query_local = qkv_local[:, :q_width]
    kv_local = qkv_local[:, q_width:]
    rows_here = query_local.shape[0]
    per_dev = rows_here // BLOCK
    n_ctx = lax.axis_size("ctx")
    nx = NX
    nz = n_ctx // nx
    reach = n_ctx // 2 // nx
    window = (n_ctx // 2) * rows_here
    ctx = lax.axis_index("ctx")
    first_row = ctx * rows_here
    zq, xq = ctx // nx, ctx % nx

    docs = jnp.arange(N_DOC_IDS, dtype=jnp.int32)
    below = jnp.sum((doc_ids[None, :] < docs[:, None]).astype(jnp.int32), axis=1)
    tail = jnp.zeros((16, kv_local.shape[1]), jnp.float32)
    tail = tail.at[0, :N_DOC_IDS].set((below // 32).astype(jnp.float32))
    tail = tail.at[1, :N_DOC_IDS].set((below % 32).astype(jnp.float32))
    piece = jnp.concatenate([kv_local, tail.astype(kv_local.dtype)], axis=0)
    prow = piece.shape[0]

    def z_pairs(k):
        return [(c, (c + k * nx) % n_ctx) for c in range(n_ctx)]

    col1 = shift(piece, z_pairs(1))
    col_far = shift(piece, z_pairs(reach))
    pair23 = shift(jnp.concatenate([piece, col1], axis=0), z_pairs(2))
    col = [piece, col1, pair23[:prow], pair23[prow:], col_far]
    recv = []
    for d in range(1, nx):
        pairs = [(z * nx + x, z * nx + (x + d) % nx) for z in range(nz) for x in range(nx)]
        extra = jnp.where(xq + d < nx, col[0], col[reach])
        recv.append(shift(jnp.concatenate(col[1:reach] + [extra], axis=0), pairs))
    kv_buf = jnp.concatenate(col + recv, axis=0)

    n_slots = reach + 1 + (nx - 1) * reach
    slot_ids = jnp.arange(n_slots, dtype=jnp.int32)
    own_a = jnp.minimum(slot_ids, reach)
    rel = slot_ids - (reach + 1)
    d_s = rel // reach + 1
    a_s = rel % reach + 1
    x_src = (xq - d_s) % nx
    extra_ctx = jnp.where(xq >= d_s, zq * nx + xq - d_s, (zq - reach) * nx + x_src)
    slot_ctx = jnp.where(
        slot_ids <= reach,
        ctx - own_a * nx,
        jnp.where(a_s == reach, extra_ctx, (zq - a_s) * nx + x_src),
    )
    tails = kv_buf.reshape(n_slots, prow, -1)[:, rows_here:rows_here + 2, :N_DOC_IDS]
    tails = tails.astype(jnp.int32)
    below_all = tails[:, 0, :] * 32 + tails[:, 1, :]
    below_all = jnp.where((slot_ctx >= 0)[:, None], below_all, 0)
    floor_row = jnp.maximum(ctx - reach * nx, 0) * rows_here
    below_sum = jnp.sum(below_all, axis=0)
    onehot = doc_ids[:, None] == docs[None, :]
    doc_start = floor_row + jnp.sum(jnp.where(onehot, below_sum[None, :], 0), axis=1)

    def slot_of(kb):
        cp = kb // per_dev
        a = zq - cp // nx
        d = (xq - cp % nx) % nx
        slot = jnp.where(
            d == 0,
            a,
            jnp.where(
                (a == 0) | (a == reach),
                reach + 1 + (d - 1) * reach + (reach - 1),
                reach + 1 + (d - 1) * reach + (a - 1),
            ),
        )
        return (slot * prow + (kb % per_dev) * BLOCK) // 16

    outputs = attention(
        query_local, kv_buf, doc_start.astype(jnp.int32), block_keep, first_row, window,
        n_ctx * per_dev, slot_of,
    )
    return lax.all_to_all(outputs, "kvh", split_axis=0, concat_axis=1, tiled=True)


def solution(mesh):
    return jax.shard_map(
        local,
        mesh=mesh,
        in_specs=(
            P(("ctx", "kvh"), None),
            P(("ctx", "kvh"), None),
            P(("ctx", "kvh"), None),
            P("ctx"),
            P("ctx", None),
        ),
        out_specs=P(("ctx", "kvh"), None),
        check_vma=False,
    )
```

```python
import functools

import numpy as np

import jax
import jax.numpy as jnp
from jax import lax
from jax.experimental import pallas as pl
from jax.experimental.pallas import tpu as pltpu
from jax.sharding import PartitionSpec as P

HD = 128
BLOCK = 128
NX = 4
N_DOC_IDS = 8


def attn_kernel(
    tab_ref, cnt_ref, keep_ref, base_ref,
    qds_ref, q_ref, kv_ref,
    o_ref,
    m_sc, l_sc, acc_sc,
    *, heads, window,
):
    qbl = pl.program_id(0)
    qpos0 = base_ref[0] + qbl * BLOCK
    scale = HD ** (-0.5)
    width = heads * BLOCK
    qpos = qpos0 + lax.broadcasted_iota(jnp.int32, (BLOCK, BLOCK), 1)
    krel = lax.broadcasted_iota(jnp.int32, (BLOCK, BLOCK), 0)
    qds = qds_ref[pl.ds(qbl, 1), :]
    qmat = q_ref[...].reshape(width, HD)

    m_sc[...] = jnp.full(m_sc.shape, -1e30, jnp.float32)
    l_sc[...] = jnp.zeros(l_sc.shape, jnp.float32)
    acc_sc[...] = jnp.zeros(acc_sc.shape, jnp.float32)

    def absorb(kb, row_blk, masked):
        start = pl.multiple_of(row_blk * 16, 16)
        k = kv_ref[pl.ds(start, BLOCK), :HD]
        v = kv_ref[pl.ds(start, BLOCK), HD:]
        s = lax.dot_general(
            k, qmat, (((1,), (1,)), ((), ())), preferred_element_type=jnp.float32
        ) * scale
        if masked:
            kpos = kb * BLOCK + krel
            keep = keep_ref[qbl, kb]
            earlier = (
                (kpos < qpos)
                & (qpos - kpos < window)
                & (kpos >= qds)
                & (keep != 0)
            )
            allowed = (kpos == qpos) | earlier
            s = jnp.where(jnp.tile(allowed, (1, heads)), s, -1e30)
        m_prev = m_sc[...]
        m_new = jnp.maximum(m_prev, jnp.max(s, axis=0, keepdims=True))
        alpha = jnp.exp(m_prev - m_new)
        p = jnp.exp(s - m_new)
        l_sc[...] = alpha * l_sc[...] + jnp.sum(p, axis=0, keepdims=True)
        acc_sc[...] = acc_sc[...] * alpha + lax.dot_general(
            v, p.astype(jnp.bfloat16), (((0,), (0,)), ((), ())),
            preferred_element_type=jnp.float32,
        )
        m_sc[...] = m_new

    def body(n, carry):
        entry = tab_ref[qbl, n]
        kb = entry & 255
        row_blk = (entry >> 8) & 4095
        kind = entry >> 20

        @pl.when(kind == 0)
        def _():
            absorb(kb, row_blk, False)

        @pl.when(kind != 0)
        def _():
            absorb(kb, row_blk, True)

        return carry

    lax.fori_loop(0, cnt_ref[qbl], body, 0)

    out = acc_sc[...] / l_sc[...]
    for h in range(heads):
        o_ref[:, h * HD:(h + 1) * HD] = out[:, h * BLOCK:(h + 1) * BLOCK].T.astype(o_ref.dtype)


def block_tables(doc_start_q, keep_rows, first_blk, nkb, window, slot_of, n_rows_blk):
    nqb = keep_rows.shape[0]
    nwin = window // BLOCK
    ds_blocks = doc_start_q.reshape(nqb, BLOCK)
    ds_first = ds_blocks[:, :1]
    ds_last = ds_blocks[:, -1:]
    qb = first_blk + jnp.arange(nqb, dtype=jnp.int32)[:, None]
    kb = jnp.arange(nkb, dtype=jnp.int32)[None, :]
    diag = kb == qb
    inwin = (kb <= qb) & (kb >= qb - nwin)
    keep = keep_rows == 1
    needed = inwin & (diag | (keep & (kb * BLOCK + BLOCK - 1 >= ds_first)))
    full = needed & (~diag) & (kb > qb - nwin) & (kb * BLOCK >= ds_last) & keep
    sort_key = jnp.where(needed, jnp.where(diag, 0, 1), 2).astype(jnp.int32)
    row_blk = jnp.clip(slot_of(kb), 0, n_rows_blk - 1)
    payload = (kb + 256 * row_blk + (1 << 20) * jnp.where(full, 0, 1)).astype(jnp.int32)
    payload = jnp.broadcast_to(payload, sort_key.shape)
    _, tab = lax.sort((sort_key, payload), dimension=1, is_stable=True, num_keys=1)
    cnt = jnp.sum(needed, axis=1).astype(jnp.int32)
    return tab, cnt, ds_blocks


def attention(q_local, kv_all, doc_start_q, keep_rows, first_row, window, nkb, slot_of):
    rows_here = q_local.shape[0]
    heads = q_local.shape[1] // HD
    nqb = rows_here // BLOCK
    nk = kv_all.shape[0]
    first_blk = first_row // BLOCK
    tab, cnt, ds_blocks = block_tables(
        doc_start_q, keep_rows, first_blk, nkb, window, slot_of, (nk - BLOCK) // 16 + 1
    )
    base = jnp.reshape(first_row, (1,)).astype(jnp.int32)
    q_t = jnp.transpose(q_local.reshape(rows_here, heads, HD), (1, 0, 2))
    kernel = functools.partial(attn_kernel, heads=heads, window=window)
    grid_spec = pltpu.PrefetchScalarGridSpec(
        num_scalar_prefetch=4,
        grid=(nqb,),
        in_specs=[
            pl.BlockSpec((nqb, BLOCK), lambda i, *_: (0, 0)),
            pl.BlockSpec((heads, BLOCK, HD), lambda i, *_: (0, i, 0)),
            pl.BlockSpec((nk, 2 * HD), lambda i, *_: (0, 0)),
        ],
        out_specs=pl.BlockSpec((BLOCK, heads * HD), lambda i, *_: (i, 0)),
        scratch_shapes=[
            pltpu.VMEM((1, heads * BLOCK), jnp.float32),
            pltpu.VMEM((1, heads * BLOCK), jnp.float32),
            pltpu.VMEM((HD, heads * BLOCK), jnp.float32),
        ],
    )
    return pl.pallas_call(
        kernel,
        grid_spec=grid_spec,
        out_shape=jax.ShapeDtypeStruct((rows_here, heads * HD), q_local.dtype),
    )(tab, cnt, keep_rows.astype(jnp.int32), base, ds_blocks, q_t, kv_all)


def shift(x, pairs):
    return lax.ppermute(x, "ctx", pairs)


def local(queries, keys, values, doc_ids, block_keep):
    rows_in = keys.shape[0]
    groups = keys.shape[1] // HD
    qkv = jnp.concatenate(
        [
            queries.reshape(rows_in, groups, -1),
            keys.reshape(rows_in, groups, HD),
            values.reshape(rows_in, groups, HD),
        ],
        axis=2,
    ).reshape(rows_in, -1)
    qkv_local = lax.all_to_all(qkv, "kvh", split_axis=1, concat_axis=0, tiled=True)
    q_width = queries.shape[1] // groups
    query_local = qkv_local[:, :q_width]
    kv_local = qkv_local[:, q_width:]
    rows_here = query_local.shape[0]
    per_dev = rows_here // BLOCK
    n_ctx = lax.axis_size("ctx")
    nx = NX
    nz = n_ctx // nx
    reach = n_ctx // 2 // nx
    window = (n_ctx // 2) * rows_here
    ctx = lax.axis_index("ctx")
    first_row = ctx * rows_here
    zq, xq = ctx // nx, ctx % nx

    docs = jnp.arange(N_DOC_IDS, dtype=jnp.int32)
    below = jnp.sum((doc_ids[None, :] < docs[:, None]).astype(jnp.int32), axis=1)
    tail = jnp.zeros((16, kv_local.shape[1]), jnp.float32)
    tail = tail.at[0, :N_DOC_IDS].set((below // 32).astype(jnp.float32))
    tail = tail.at[1, :N_DOC_IDS].set((below % 32).astype(jnp.float32))
    piece = jnp.concatenate([kv_local, tail.astype(kv_local.dtype)], axis=0)
    prow = piece.shape[0]

    z_step = [(c, (c + nx) % n_ctx) for c in range(n_ctx)]

    def x_pairs(d):
        return [(z * nx + x, z * nx + (x + d) % nx) for z in range(nz) for x in range(nx)]

    col = [piece]
    for _ in range(reach):
        col.append(shift(col[-1], z_step))
    half = (reach + 1) // 2
    early = list(range(1, half + 1))
    late = list(range(half + 1, reach))
    parts, tags = list(col), [(a, 0) for a in range(reach + 1)]

    def add(arr, tag_list):
        parts.append(arr)
        tags.extend(tag_list)

    def blocks(idx):
        return jnp.concatenate([col[a] for a in idx], axis=0) if len(idx) > 1 else col[idx[0]]

    e_plus = shift(blocks(early), x_pairs(1))
    e_minus = shift(blocks(early), x_pairs(nx - 1))
    add(e_plus, [(a, 1) for a in early])
    add(e_minus, [(a, nx - 1) for a in early])
    add(shift(e_plus, x_pairs(1)), [(a, 2) for a in early])
    extra = {d: jnp.where(xq + d < nx, col[0], col[reach]) for d in range(1, nx)}
    l_plus = shift(jnp.concatenate([col[a] for a in late] + [extra[1]], axis=0), x_pairs(1))
    l_minus = shift(jnp.concatenate([col[a] for a in late] + [extra[nx - 1]], axis=0), x_pairs(nx - 1))
    add(l_plus, [(a, 1) for a in late] + [("e", 1)])
    add(l_minus, [(a, nx - 1) for a in late] + [("e", nx - 1)])
    if late:
        relay = l_minus[: prow * len(late)]
        add(shift(relay, x_pairs(nx - 1)), [(a, 2) for a in late])
    add(shift(extra[2], x_pairs(2)), [("e", 2)])
    kv_buf = jnp.concatenate(parts, axis=0)

    n_slots = len(tags)
    table = np.zeros((reach + 1, nx), np.int32)
    tag_a = np.zeros(n_slots, np.int32)
    tag_d = np.zeros(n_slots, np.int32)
    tag_e = np.zeros(n_slots, bool)
    for s, (a, d) in enumerate(tags):
        tag_d[s] = d
        if a == "e":
            tag_e[s] = True
            table[0, d] = s
            table[reach, d] = s
        else:
            tag_a[s] = a
            table[a, d] = s
    x_src = (xq - tag_d) % nx
    extra_ctx = jnp.where(xq >= tag_d, zq * nx + xq - tag_d, (zq - reach) * nx + x_src)
    slot_ctx = jnp.where(tag_e, extra_ctx, (zq - tag_a) * nx + x_src)
    tails = kv_buf.reshape(n_slots, prow, -1)[:, rows_here:rows_here + 2, :N_DOC_IDS]
    tails = tails.astype(jnp.int32)
    below_all = tails[:, 0, :] * 32 + tails[:, 1, :]
    below_all = jnp.where((slot_ctx >= 0)[:, None], below_all, 0)
    floor_row = jnp.maximum(ctx - reach * nx, 0) * rows_here
    below_sum = jnp.sum(below_all, axis=0)
    onehot = doc_ids[:, None] == docs[None, :]
    doc_start = floor_row + jnp.sum(jnp.where(onehot, below_sum[None, :], 0), axis=1)

    def slot_of(kb):
        cp = kb // per_dev
        a = zq - cp // nx
        d = (xq - cp % nx) % nx
        hit = (a[..., None, None] == np.arange(reach + 1)[:, None]) & (
            d[..., None, None] == np.arange(nx)[None, :]
        )
        slot = jnp.sum(jnp.where(hit, table, 0), axis=(-2, -1))
        return (slot * prow + (kb % per_dev) * BLOCK) // 16

    outputs = attention(
        query_local, kv_buf, doc_start.astype(jnp.int32), block_keep, first_row, window,
        n_ctx * per_dev, slot_of,
    )
    return lax.all_to_all(outputs, "kvh", split_axis=0, concat_axis=1, tiled=True)


def solution(mesh):
    return jax.shard_map(
        local,
        mesh=mesh,
        in_specs=(
            P(("ctx", "kvh"), None),
            P(("ctx", "kvh"), None),
            P(("ctx", "kvh"), None),
            P("ctx"),
            P("ctx", None),
        ),
        out_specs=P(("ctx", "kvh"), None),
        check_vma=False,
    )
```

```python
import functools

import numpy as np

import jax
import jax.numpy as jnp
from jax import lax
from jax.experimental import pallas as pl
from jax.experimental.pallas import tpu as pltpu
from jax.sharding import PartitionSpec as P

HD = 128
BLOCK = 128
NX = 4
N_DOC_IDS = 8


def attn_kernel(
    tab_ref, cnt_ref, keep_ref, base_ref,
    qds_ref, q_ref, kv_ref, *rest,
    heads, window, first, last, row_base,
):
    if first:
        state_in = ()
    else:
        state_in, rest = rest[:3], rest[3:]
    outs, (m_sc, l_sc, acc_sc) = rest[:-3], rest[-3:]
    qbl = pl.program_id(0)
    qpos0 = base_ref[0] + qbl * BLOCK
    scale = HD ** (-0.5)
    width = heads * BLOCK
    qpos = qpos0 + lax.broadcasted_iota(jnp.int32, (BLOCK, BLOCK), 1)
    krel = lax.broadcasted_iota(jnp.int32, (BLOCK, BLOCK), 0)
    qds = qds_ref[pl.ds(qbl, 1), :]
    qmat = q_ref[...].reshape(width, HD)

    if first:
        m_sc[...] = jnp.full(m_sc.shape, -1e30, jnp.float32)
        l_sc[...] = jnp.zeros(l_sc.shape, jnp.float32)
        acc_sc[...] = jnp.zeros(acc_sc.shape, jnp.float32)
    else:
        acc_in, m_in, l_in = state_in
        acc_sc[...] = acc_in[...]
        m_sc[...] = m_in[0:1, :]
        l_sc[...] = l_in[0:1, :]

    def absorb(kb, row_blk, masked):
        start = pl.multiple_of((row_blk - row_base) * 16, 16)
        k = kv_ref[pl.ds(start, BLOCK), :HD]
        v = kv_ref[pl.ds(start, BLOCK), HD:]
        s = lax.dot_general(
            k, qmat, (((1,), (1,)), ((), ())), preferred_element_type=jnp.float32
        ) * scale
        if masked:
            kpos = kb * BLOCK + krel
            keep = keep_ref[qbl, kb]
            earlier = (
                (kpos < qpos)
                & (qpos - kpos < window)
                & (kpos >= qds)
                & (keep != 0)
            )
            allowed = (kpos == qpos) | earlier
            s = jnp.where(jnp.tile(allowed, (1, heads)), s, -1e30)
        m_prev = m_sc[...]
        m_new = jnp.maximum(m_prev, jnp.max(s, axis=0, keepdims=True))
        alpha = jnp.exp(m_prev - m_new)
        p = jnp.exp(s - m_new)
        l_sc[...] = alpha * l_sc[...] + jnp.sum(p, axis=0, keepdims=True)
        acc_sc[...] = acc_sc[...] * alpha + lax.dot_general(
            v, p.astype(jnp.bfloat16), (((0,), (0,)), ((), ())),
            preferred_element_type=jnp.float32,
        )
        m_sc[...] = m_new

    def body(n, carry):
        entry = tab_ref[qbl, n]
        kb = entry & 255
        row_blk = (entry >> 8) & 4095
        kind = entry >> 20

        @pl.when(kind == 0)
        def _():
            absorb(kb, row_blk, False)

        @pl.when(kind != 0)
        def _():
            absorb(kb, row_blk, True)

        return carry

    lax.fori_loop(cnt_ref[qbl, 0], cnt_ref[qbl, 1], body, 0)

    if last:
        (o_ref,) = outs
        out = acc_sc[...] / l_sc[...]
        for h in range(heads):
            o_ref[:, h * HD:(h + 1) * HD] = out[:, h * BLOCK:(h + 1) * BLOCK].T.astype(o_ref.dtype)
    else:
        acc_o, m_o, l_o = outs
        acc_o[...] = acc_sc[...]
        m_o[...] = jnp.broadcast_to(m_sc[...], m_o.shape)
        l_o[...] = jnp.broadcast_to(l_sc[...], l_o.shape)


def block_tables(doc_start_q, keep_rows, first_blk, nkb, window, slot_of, own_rows):
    nqb = keep_rows.shape[0]
    nwin = window // BLOCK
    ds_blocks = doc_start_q.reshape(nqb, BLOCK)
    ds_first = ds_blocks[:, :1]
    ds_last = ds_blocks[:, -1:]
    qb = first_blk + jnp.arange(nqb, dtype=jnp.int32)[:, None]
    kb = jnp.arange(nkb, dtype=jnp.int32)[None, :]
    diag = kb == qb
    inwin = (kb <= qb) & (kb >= qb - nwin)
    keep = keep_rows == 1
    needed = inwin & (diag | (keep & (kb * BLOCK + BLOCK - 1 >= ds_first)))
    full = needed & (~diag) & (kb > qb - nwin) & (kb * BLOCK >= ds_last) & keep
    row_blk = jnp.clip(slot_of(kb), 0, 4095)
    own = row_blk < own_rows
    sort_key = jnp.where(needed, jnp.where(own, jnp.where(diag, 0, 1), 2), 3).astype(jnp.int32)
    payload = (kb + 256 * row_blk + (1 << 20) * jnp.where(full, 0, 1)).astype(jnp.int32)
    payload = jnp.broadcast_to(payload, sort_key.shape)
    _, tab = lax.sort((sort_key, payload), dimension=1, is_stable=True, num_keys=1)
    n_own = jnp.sum(needed & own, axis=1).astype(jnp.int32)
    n_all = jnp.sum(needed, axis=1).astype(jnp.int32)
    zero = jnp.zeros_like(n_own)
    return tab, jnp.stack([zero, n_own], 1), jnp.stack([n_own, n_all], 1), ds_blocks


def attend_call(tab, cnt, keep_rows, base, ds_blocks, q_t, kv, state, *, window, first, last, row_base):
    heads, rows_here, _ = q_t.shape
    nqb = rows_here // BLOCK
    width = heads * BLOCK
    nk = kv.shape[0]
    kernel = functools.partial(
        attn_kernel, heads=heads, window=window, first=first, last=last, row_base=row_base
    )
    in_specs = [
        pl.BlockSpec((nqb, BLOCK), lambda i, *_: (0, 0)),
        pl.BlockSpec((heads, BLOCK, HD), lambda i, *_: (0, i, 0)),
        pl.BlockSpec((nk, 2 * HD), lambda i, *_: (0, 0)),
    ]
    state_specs = [
        pl.BlockSpec((HD, width), lambda i, *_: (i, 0)),
        pl.BlockSpec((8, width), lambda i, *_: (i, 0)),
        pl.BlockSpec((8, width), lambda i, *_: (i, 0)),
    ]
    state_shapes = [
        jax.ShapeDtypeStruct((nqb * HD, width), jnp.float32),
        jax.ShapeDtypeStruct((nqb * 8, width), jnp.float32),
        jax.ShapeDtypeStruct((nqb * 8, width), jnp.float32),
    ]
    args = [tab, cnt, keep_rows, base, ds_blocks, q_t, kv]
    if not first:
        in_specs += state_specs
        args += list(state)
    if last:
        out_specs = pl.BlockSpec((BLOCK, width), lambda i, *_: (i, 0))
        out_shape = jax.ShapeDtypeStruct((rows_here, width), q_t.dtype)
    else:
        out_specs = state_specs
        out_shape = state_shapes
    grid_spec = pltpu.PrefetchScalarGridSpec(
        num_scalar_prefetch=4,
        grid=(nqb,),
        in_specs=in_specs,
        out_specs=out_specs,
        scratch_shapes=[
            pltpu.VMEM((1, width), jnp.float32),
            pltpu.VMEM((1, width), jnp.float32),
            pltpu.VMEM((HD, width), jnp.float32),
        ],
    )
    flops = 4 * rows_here * heads * HD * BLOCK * 8
    cost = pl.CostEstimate(flops=flops, transcendentals=flops // (4 * HD), bytes_accessed=nk * 4 * HD)
    return pl.pallas_call(
        kernel, grid_spec=grid_spec, out_shape=out_shape, cost_estimate=cost
    )(*args)


def attention(q_local, kv_own, kv_rest, doc_start_q, keep_rows, first_row, window, nkb, slot_of):
    rows_here = q_local.shape[0]
    heads = q_local.shape[1] // HD
    first_blk = first_row // BLOCK
    own_rows = kv_own.shape[0] // 16
    tab, cnt_a, cnt_b, ds_blocks = block_tables(
        doc_start_q, keep_rows, first_blk, nkb, window, slot_of, own_rows
    )
    base = jnp.reshape(first_row, (1,)).astype(jnp.int32)
    keep_i = keep_rows.astype(jnp.int32)
    q_t = jnp.transpose(q_local.reshape(rows_here, heads, HD), (1, 0, 2))
    state = attend_call(
        tab, cnt_a, keep_i, base, ds_blocks, q_t, kv_own, None,
        window=window, first=True, last=False, row_base=0,
    )
    return attend_call(
        tab, cnt_b, keep_i, base, ds_blocks, q_t, kv_rest, state,
        window=window, first=False, last=True, row_base=own_rows,
    )


def shift(x, pairs):
    return lax.ppermute(x, "ctx", pairs)


def local(queries, keys, values, doc_ids, block_keep):
    rows_in = keys.shape[0]
    groups = keys.shape[1] // HD
    qkv = jnp.concatenate(
        [
            queries.reshape(rows_in, groups, -1),
            keys.reshape(rows_in, groups, HD),
            values.reshape(rows_in, groups, HD),
        ],
        axis=2,
    ).reshape(rows_in, -1)
    qkv_local = lax.all_to_all(qkv, "kvh", split_axis=1, concat_axis=0, tiled=True)
    q_width = queries.shape[1] // groups
    query_local = qkv_local[:, :q_width]
    kv_local = qkv_local[:, q_width:]
    rows_here = query_local.shape[0]
    per_dev = rows_here // BLOCK
    n_ctx = lax.axis_size("ctx")
    nx = NX
    nz = n_ctx // nx
    reach = n_ctx // 2 // nx
    window = (n_ctx // 2) * rows_here
    ctx = lax.axis_index("ctx")
    first_row = ctx * rows_here
    zq, xq = ctx // nx, ctx % nx

    def x_pairs(d):
        return [(z * nx + x, z * nx + (x + d) % nx) for z in range(nz) for x in range(nx)]

    docs = jnp.arange(N_DOC_IDS, dtype=jnp.int32)
    below = jnp.sum((doc_ids[None, :] < docs[:, None]).astype(jnp.int32), axis=1)
    below_x = jnp.stack(
        [below] + [shift(below, x_pairs(d)) for d in range(1, nx)], axis=0
    ).reshape(-1)
    tail = jnp.zeros((16, kv_local.shape[1]), jnp.float32)
    tail = tail.at[0, :nx * N_DOC_IDS].set((below_x // 32).astype(jnp.float32))
    tail = tail.at[1, :nx * N_DOC_IDS].set((below_x % 32).astype(jnp.float32))
    piece = jnp.concatenate([kv_local, tail.astype(kv_local.dtype)], axis=0)
    prow = piece.shape[0]

    z_step = [(c, (c + nx) % n_ctx) for c in range(n_ctx)]

    col = [piece]
    for _ in range(reach):
        col.append(shift(col[-1], z_step))
    half = (reach + 1) // 2
    early = list(range(1, half + 1))
    late = list(range(half + 1, reach))
    parts, tags = list(col), [(a, 0) for a in range(reach + 1)]

    def add(arr, tag_list):
        parts.append(arr)
        tags.extend(tag_list)

    def blocks(idx):
        return jnp.concatenate([col[a] for a in idx], axis=0) if len(idx) > 1 else col[idx[0]]

    e_plus = shift(blocks(early), x_pairs(1))
    e_minus = shift(blocks(early), x_pairs(nx - 1))
    add(e_plus, [(a, 1) for a in early])
    add(e_minus, [(a, nx - 1) for a in early])
    add(shift(e_plus, x_pairs(1)), [(a, 2) for a in early])
    extra = {d: jnp.where(xq + d < nx, col[0], col[reach]) for d in range(1, nx)}
    l_plus = shift(jnp.concatenate([col[a] for a in late] + [extra[1]], axis=0), x_pairs(1))
    l_minus = shift(jnp.concatenate([col[a] for a in late] + [extra[nx - 1]], axis=0), x_pairs(nx - 1))
    add(l_plus, [(a, 1) for a in late] + [("e", 1)])
    add(l_minus, [(a, nx - 1) for a in late] + [("e", nx - 1)])
    if late:
        relay = l_minus[: prow * len(late)]
        add(shift(relay, x_pairs(nx - 1)), [(a, 2) for a in late])
    add(shift(extra[2], x_pairs(2)), [("e", 2)])
    kv_own = jnp.concatenate(parts[:reach + 1], axis=0)
    kv_rest = jnp.concatenate(parts[reach + 1:], axis=0)

    n_slots = len(tags)
    table = np.zeros((reach + 1, nx), np.int32)
    for s, (a, d) in enumerate(tags):
        if a == "e":
            table[0, d] = s
            table[reach, d] = s
        else:
            table[a, d] = s
    tails = kv_own.reshape(reach + 1, prow, -1)[:, rows_here:rows_here + 2, :nx * N_DOC_IDS]
    tails = tails.astype(jnp.int32)
    below_col = (tails[:, 0, :] * 32 + tails[:, 1, :]).reshape(reach + 1, nx, N_DOC_IDS)
    a_ids = np.arange(reach + 1)[:, None]
    d_ids = np.arange(nx)[None, :]
    src_ctx = (zq - a_ids) * nx + (xq - d_ids) % nx
    floor_ctx = jnp.maximum(ctx - reach * nx, 0)
    use = (src_ctx >= floor_ctx) & (src_ctx <= ctx)
    below_sum = jnp.sum(jnp.where(use[:, :, None], below_col, 0), axis=(0, 1))
    onehot = doc_ids[:, None] == docs[None, :]
    doc_start = floor_ctx * rows_here + jnp.sum(jnp.where(onehot, below_sum[None, :], 0), axis=1)

    def slot_of(kb):
        cp = kb // per_dev
        a = zq - cp // nx
        d = (xq - cp % nx) % nx
        hit = (a[..., None, None] == np.arange(reach + 1)[:, None]) & (
            d[..., None, None] == np.arange(nx)[None, :]
        )
        slot = jnp.sum(jnp.where(hit, table, 0), axis=(-2, -1))
        return (slot * prow + (kb % per_dev) * BLOCK) // 16

    outputs = attention(
        query_local, kv_own, kv_rest, doc_start.astype(jnp.int32), block_keep, first_row,
        window, n_ctx * per_dev, slot_of,
    )
    return lax.all_to_all(outputs, "kvh", split_axis=0, concat_axis=1, tiled=True)


def solution(mesh):
    return jax.shard_map(
        local,
        mesh=mesh,
        in_specs=(
            P(("ctx", "kvh"), None),
            P(("ctx", "kvh"), None),
            P(("ctx", "kvh"), None),
            P("ctx"),
            P("ctx", None),
        ),
        out_specs=P(("ctx", "kvh"), None),
        check_vma=False,
    )
```

```python
import functools

import numpy as np

import jax
import jax.numpy as jnp
from jax import lax
from jax.experimental import pallas as pl
from jax.experimental.pallas import tpu as pltpu
from jax.sharding import PartitionSpec as P

HD = 128
BLOCK = 128
NX = 4
N_DOC_IDS = 8


def attn_kernel(
    tab_ref, cnt_ref, keep_ref, base_ref,
    qds_ref, q_ref, kv_ref, *rest,
    heads, window, first, last, row_base,
):
    if first:
        state_in = ()
    else:
        state_in, rest = rest[:3], rest[3:]
    outs, (m_sc, l_sc, acc_sc) = rest[:-3], rest[-3:]
    qbl = pl.program_id(0)
    qpos0 = base_ref[0] + qbl * BLOCK
    scale = HD ** (-0.5)
    width = heads * BLOCK
    qpos = qpos0 + lax.broadcasted_iota(jnp.int32, (BLOCK, BLOCK), 1)
    krel = lax.broadcasted_iota(jnp.int32, (BLOCK, BLOCK), 0)
    qds = qds_ref[pl.ds(qbl, 1), :]
    qmat = q_ref[...].reshape(width, HD)

    if first:
        m_sc[...] = jnp.full(m_sc.shape, -1e30, jnp.float32)
        l_sc[...] = jnp.zeros(l_sc.shape, jnp.float32)
        acc_sc[...] = jnp.zeros(acc_sc.shape, jnp.float32)
    else:
        acc_in, m_in, l_in = state_in
        acc_sc[...] = acc_in[...]
        m_sc[...] = m_in[0:1, :]
        l_sc[...] = l_in[0:1, :]

    def mask_of(kb):
        kpos = kb * BLOCK + krel
        keep = keep_ref[qbl, kb]
        earlier = (kpos < qpos) & (qpos - kpos < window) & (kpos >= qds) & (keep != 0)
        return (kpos == qpos) | earlier

    def absorb(kb1, rb1, kb2, rb2, valid2, masked1, masked2):
        s1 = pl.multiple_of((rb1 - row_base) * 16, 16)
        s2 = pl.multiple_of((rb2 - row_base) * 16, 16)
        k = jnp.concatenate(
            [kv_ref[pl.ds(s1, BLOCK), :HD], kv_ref[pl.ds(s2, BLOCK), :HD]], axis=0
        )
        v = jnp.concatenate(
            [kv_ref[pl.ds(s1, BLOCK), HD:], kv_ref[pl.ds(s2, BLOCK), HD:]], axis=0
        )
        s = lax.dot_general(
            k, qmat, (((1,), (1,)), ((), ())), preferred_element_type=jnp.float32
        ) * scale
        if masked1 or masked2:
            full_true = jnp.ones((BLOCK, BLOCK), jnp.bool_)
            a1 = mask_of(kb1) if masked1 else full_true
            a2 = (mask_of(kb2) & valid2) if masked2 else full_true
            allowed = jnp.concatenate([a1, a2], axis=0)
            s = jnp.where(jnp.tile(allowed, (1, heads)), s, -1e30)
        m_prev = m_sc[...]
        m_new = jnp.maximum(m_prev, jnp.max(s, axis=0, keepdims=True))
        alpha = jnp.exp(m_prev - m_new)
        p = jnp.exp(s - m_new)
        l_sc[...] = alpha * l_sc[...] + jnp.sum(p, axis=0, keepdims=True)
        acc_sc[...] = acc_sc[...] * alpha + lax.dot_general(
            v, p.astype(jnp.bfloat16), (((0,), (0,)), ((), ())),
            preferred_element_type=jnp.float32,
        )
        m_sc[...] = m_new

    lo = cnt_ref[qbl, 0]
    hi = cnt_ref[qbl, 1]

    def body(i, carry):
        n = lo + 2 * i
        e1 = tab_ref[qbl, n]
        has2 = n + 1 < hi
        e2 = tab_ref[qbl, jnp.minimum(n + 1, hi - 1)]
        kb1, rb1, kind1 = e1 & 255, (e1 >> 8) & 4095, e1 >> 20
        kb2, rb2 = e2 & 255, (e2 >> 8) & 4095
        kind2 = jnp.where(has2, e2 >> 20, 1)
        for m1 in (False, True):
            for m2 in (False, True):
                @pl.when(((kind1 != 0) == m1) & ((kind2 != 0) == m2))
                def _(m1=m1, m2=m2):
                    absorb(kb1, rb1, kb2, rb2, has2, m1, m2)

        return carry

    lax.fori_loop(0, (hi - lo + 1) // 2, body, 0)

    if last:
        (o_ref,) = outs
        out = acc_sc[...] / l_sc[...]
        for h in range(heads):
            o_ref[:, h * HD:(h + 1) * HD] = out[:, h * BLOCK:(h + 1) * BLOCK].T.astype(o_ref.dtype)
    else:
        acc_o, m_o, l_o = outs
        acc_o[...] = acc_sc[...]
        m_o[...] = jnp.broadcast_to(m_sc[...], m_o.shape)
        l_o[...] = jnp.broadcast_to(l_sc[...], l_o.shape)


def block_tables(doc_start_q, keep_rows, first_blk, nkb, window, slot_of, own_rows):
    nqb = keep_rows.shape[0]
    nwin = window // BLOCK
    ds_blocks = doc_start_q.reshape(nqb, BLOCK)
    ds_first = ds_blocks[:, :1]
    ds_last = ds_blocks[:, -1:]
    qb = first_blk + jnp.arange(nqb, dtype=jnp.int32)[:, None]
    kb = jnp.arange(nkb, dtype=jnp.int32)[None, :]
    diag = kb == qb
    inwin = (kb <= qb) & (kb >= qb - nwin)
    keep = keep_rows == 1
    needed = inwin & (diag | (keep & (kb * BLOCK + BLOCK - 1 >= ds_first)))
    full = needed & (~diag) & (kb > qb - nwin) & (kb * BLOCK >= ds_last) & keep
    row_blk = jnp.clip(slot_of(kb), 0, 4095)
    own = row_blk < own_rows
    sort_key = jnp.where(needed, jnp.where(own, jnp.where(diag, 0, 1), 2), 3).astype(jnp.int32)
    payload = (kb + 256 * row_blk + (1 << 20) * jnp.where(full, 0, 1)).astype(jnp.int32)
    payload = jnp.broadcast_to(payload, sort_key.shape)
    _, tab = lax.sort((sort_key, payload), dimension=1, is_stable=True, num_keys=1)
    n_own = jnp.sum(needed & own, axis=1).astype(jnp.int32)
    n_all = jnp.sum(needed, axis=1).astype(jnp.int32)
    zero = jnp.zeros_like(n_own)
    return tab, jnp.stack([zero, n_own], 1), jnp.stack([n_own, n_all], 1), ds_blocks


def attend_call(tab, cnt, keep_rows, base, ds_blocks, q_t, kv, state, *, window, first, last, row_base):
    heads, rows_here, _ = q_t.shape
    nqb = rows_here // BLOCK
    width = heads * BLOCK
    nk = kv.shape[0]
    kernel = functools.partial(
        attn_kernel, heads=heads, window=window, first=first, last=last, row_base=row_base
    )
    in_specs = [
        pl.BlockSpec((nqb, BLOCK), lambda i, *_: (0, 0)),
        pl.BlockSpec((heads, BLOCK, HD), lambda i, *_: (0, i, 0)),
        pl.BlockSpec((nk, 2 * HD), lambda i, *_: (0, 0)),
    ]
    state_specs = [
        pl.BlockSpec((HD, width), lambda i, *_: (i, 0)),
        pl.BlockSpec((8, width), lambda i, *_: (i, 0)),
        pl.BlockSpec((8, width), lambda i, *_: (i, 0)),
    ]
    state_shapes = [
        jax.ShapeDtypeStruct((nqb * HD, width), jnp.float32),
        jax.ShapeDtypeStruct((nqb * 8, width), jnp.float32),
        jax.ShapeDtypeStruct((nqb * 8, width), jnp.float32),
    ]
    args = [tab, cnt, keep_rows, base, ds_blocks, q_t, kv]
    if not first:
        in_specs += state_specs
        args += list(state)
    if last:
        out_specs = pl.BlockSpec((BLOCK, width), lambda i, *_: (i, 0))
        out_shape = jax.ShapeDtypeStruct((rows_here, width), q_t.dtype)
    else:
        out_specs = state_specs
        out_shape = state_shapes
    grid_spec = pltpu.PrefetchScalarGridSpec(
        num_scalar_prefetch=4,
        grid=(nqb,),
        in_specs=in_specs,
        out_specs=out_specs,
        scratch_shapes=[
            pltpu.VMEM((1, width), jnp.float32),
            pltpu.VMEM((1, width), jnp.float32),
            pltpu.VMEM((HD, width), jnp.float32),
        ],
    )
    flops = 4 * rows_here * heads * HD * BLOCK * 8
    cost = pl.CostEstimate(flops=flops, transcendentals=flops // (4 * HD), bytes_accessed=nk * 4 * HD)
    return pl.pallas_call(
        kernel, grid_spec=grid_spec, out_shape=out_shape, cost_estimate=cost
    )(*args)


def attention(q_local, kv_own, kv_rest, doc_start_q, keep_rows, first_row, window, nkb, slot_of):
    rows_here = q_local.shape[0]
    heads = q_local.shape[1] // HD
    first_blk = first_row // BLOCK
    own_rows = kv_own.shape[0] // 16
    tab, cnt_a, cnt_b, ds_blocks = block_tables(
        doc_start_q, keep_rows, first_blk, nkb, window, slot_of, own_rows
    )
    base = jnp.reshape(first_row, (1,)).astype(jnp.int32)
    keep_i = keep_rows.astype(jnp.int32)
    q_t = jnp.transpose(q_local.reshape(rows_here, heads, HD), (1, 0, 2))
    state = attend_call(
        tab, cnt_a, keep_i, base, ds_blocks, q_t, kv_own, None,
        window=window, first=True, last=False, row_base=0,
    )
    return attend_call(
        tab, cnt_b, keep_i, base, ds_blocks, q_t, kv_rest, state,
        window=window, first=False, last=True, row_base=own_rows,
    )


def shift(x, pairs):
    return lax.ppermute(x, "ctx", pairs)


def local(queries, keys, values, doc_ids, block_keep):
    rows_in = keys.shape[0]
    groups = keys.shape[1] // HD
    qkv = jnp.concatenate(
        [
            queries.reshape(rows_in, groups, -1),
            keys.reshape(rows_in, groups, HD),
            values.reshape(rows_in, groups, HD),
        ],
        axis=2,
    ).reshape(rows_in, -1)
    qkv_local = lax.all_to_all(qkv, "kvh", split_axis=1, concat_axis=0, tiled=True)
    q_width = queries.shape[1] // groups
    query_local = qkv_local[:, :q_width]
    kv_local = qkv_local[:, q_width:]
    rows_here = query_local.shape[0]
    per_dev = rows_here // BLOCK
    n_ctx = lax.axis_size("ctx")
    nx = NX
    nz = n_ctx // nx
    reach = n_ctx // 2 // nx
    window = (n_ctx // 2) * rows_here
    ctx = lax.axis_index("ctx")
    first_row = ctx * rows_here
    zq, xq = ctx // nx, ctx % nx

    def x_pairs(d):
        return [(z * nx + x, z * nx + (x + d) % nx) for z in range(nz) for x in range(nx)]

    docs = jnp.arange(N_DOC_IDS, dtype=jnp.int32)
    below = jnp.sum((doc_ids[None, :] < docs[:, None]).astype(jnp.int32), axis=1)
    below_x = jnp.stack(
        [below] + [shift(below, x_pairs(d)) for d in range(1, nx)], axis=0
    ).reshape(-1)
    tail = jnp.zeros((16, kv_local.shape[1]), jnp.float32)
    tail = tail.at[0, :nx * N_DOC_IDS].set((below_x // 32).astype(jnp.float32))
    tail = tail.at[1, :nx * N_DOC_IDS].set((below_x % 32).astype(jnp.float32))
    piece = jnp.concatenate([kv_local, tail.astype(kv_local.dtype)], axis=0)
    prow = piece.shape[0]

    z_step = [(c, (c + nx) % n_ctx) for c in range(n_ctx)]

    col = [piece]
    for _ in range(reach):
        col.append(shift(col[-1], z_step))
    half = (reach + 1) // 2
    early = list(range(1, half + 1))
    late = list(range(half + 1, reach))
    parts, tags = list(col), [(a, 0) for a in range(reach + 1)]

    def add(arr, tag_list):
        parts.append(arr)
        tags.extend(tag_list)

    def blocks(idx):
        return jnp.concatenate([col[a] for a in idx], axis=0) if len(idx) > 1 else col[idx[0]]

    e_plus = shift(blocks(early), x_pairs(1))
    e_minus = shift(blocks(early), x_pairs(nx - 1))
    add(e_plus, [(a, 1) for a in early])
    add(e_minus, [(a, nx - 1) for a in early])
    add(shift(e_plus, x_pairs(1)), [(a, 2) for a in early])
    extra = {d: jnp.where(xq + d < nx, col[0], col[reach]) for d in range(1, nx)}
    l_plus = shift(jnp.concatenate([col[a] for a in late] + [extra[1]], axis=0), x_pairs(1))
    l_minus = shift(jnp.concatenate([col[a] for a in late] + [extra[nx - 1]], axis=0), x_pairs(nx - 1))
    add(l_plus, [(a, 1) for a in late] + [("e", 1)])
    add(l_minus, [(a, nx - 1) for a in late] + [("e", nx - 1)])
    if late:
        relay = l_minus[: prow * len(late)]
        add(shift(relay, x_pairs(nx - 1)), [(a, 2) for a in late])
    add(shift(extra[2], x_pairs(2)), [("e", 2)])
    kv_own = jnp.concatenate(parts[:reach + 1], axis=0)
    kv_rest = jnp.concatenate(parts[reach + 1:], axis=0)

    n_slots = len(tags)
    table = np.zeros((reach + 1, nx), np.int32)
    for s, (a, d) in enumerate(tags):
        if a == "e":
            table[0, d] = s
            table[reach, d] = s
        else:
            table[a, d] = s
    tails = kv_own.reshape(reach + 1, prow, -1)[:, rows_here:rows_here + 2, :nx * N_DOC_IDS]
    tails = tails.astype(jnp.int32)
    below_col = (tails[:, 0, :] * 32 + tails[:, 1, :]).reshape(reach + 1, nx, N_DOC_IDS)
    a_ids = np.arange(reach + 1)[:, None]
    d_ids = np.arange(nx)[None, :]
    src_ctx = (zq - a_ids) * nx + (xq - d_ids) % nx
    floor_ctx = jnp.maximum(ctx - reach * nx, 0)
    use = (src_ctx >= floor_ctx) & (src_ctx <= ctx)
    below_sum = jnp.sum(jnp.where(use[:, :, None], below_col, 0), axis=(0, 1))
    onehot = doc_ids[:, None] == docs[None, :]
    doc_start = floor_ctx * rows_here + jnp.sum(jnp.where(onehot, below_sum[None, :], 0), axis=1)

    def slot_of(kb):
        cp = kb // per_dev
        a = zq - cp // nx
        d = (xq - cp % nx) % nx
        hit = (a[..., None, None] == np.arange(reach + 1)[:, None]) & (
            d[..., None, None] == np.arange(nx)[None, :]
        )
        slot = jnp.sum(jnp.where(hit, table, 0), axis=(-2, -1))
        return (slot * prow + (kb % per_dev) * BLOCK) // 16

    outputs = attention(
        query_local, kv_own, kv_rest, doc_start.astype(jnp.int32), block_keep, first_row,
        window, n_ctx * per_dev, slot_of,
    )
    return lax.all_to_all(outputs, "kvh", split_axis=0, concat_axis=1, tiled=True)


def solution(mesh):
    return jax.shard_map(
        local,
        mesh=mesh,
        in_specs=(
            P(("ctx", "kvh"), None),
            P(("ctx", "kvh"), None),
            P(("ctx", "kvh"), None),
            P("ctx"),
            P("ctx", None),
        ),
        out_specs=P(("ctx", "kvh"), None),
        check_vma=False,
    )
```

```python
import functools

import numpy as np

import jax
import jax.numpy as jnp
from jax import lax
from jax.experimental import pallas as pl
from jax.experimental.pallas import tpu as pltpu
from jax.sharding import PartitionSpec as P

HD = 128
BLOCK = 128
NX = 4
N_DOC_IDS = 8
KEY_GROUP = 4


def attn_kernel(
    tab_ref, cnt_ref, keep_ref, base_ref,
    qds_ref, q_ref, kv_ref, *rest,
    heads, window, first, last, row_base,
):
    if first:
        state_in = ()
    else:
        state_in, rest = rest[:3], rest[3:]
    outs, (m_sc, l_sc, acc_sc) = rest[:-3], rest[-3:]
    qbl = pl.program_id(0)
    qpos0 = base_ref[0] + qbl * BLOCK
    scale = HD ** (-0.5)
    width = heads * BLOCK
    qpos = qpos0 + lax.broadcasted_iota(jnp.int32, (BLOCK, BLOCK), 1)
    krel = lax.broadcasted_iota(jnp.int32, (BLOCK, BLOCK), 0)
    qds = qds_ref[pl.ds(qbl, 1), :]
    qmat = q_ref[...].reshape(width, HD)

    if first:
        m_sc[...] = jnp.full(m_sc.shape, -1e30, jnp.float32)
        l_sc[...] = jnp.zeros(l_sc.shape, jnp.float32)
        acc_sc[...] = jnp.zeros(acc_sc.shape, jnp.float32)
    else:
        acc_in, m_in, l_in = state_in
        acc_sc[...] = acc_in[...]
        m_sc[...] = m_in[0:1, :]
        l_sc[...] = l_in[0:1, :]

    def mask_of(kb):
        kpos = kb * BLOCK + krel
        keep = keep_ref[qbl, kb]
        earlier = (kpos < qpos) & (qpos - kpos < window) & (kpos >= qds) & (keep != 0)
        return (kpos == qpos) | earlier

    def absorb(ents, masked):
        starts = [pl.multiple_of((rb - row_base) * 16, 16) for _, rb, _, _ in ents]
        k = jnp.concatenate([kv_ref[pl.ds(st, BLOCK), :HD] for st in starts], axis=0)
        v = jnp.concatenate([kv_ref[pl.ds(st, BLOCK), HD:] for st in starts], axis=0)
        s = lax.dot_general(
            k, qmat, (((1,), (1,)), ((), ())), preferred_element_type=jnp.float32
        ) * scale
        if masked:
            allowed = jnp.concatenate(
                [
                    (mask_of(kb) | (kind == 0)) & valid
                    for kb, _, kind, valid in ents
                ],
                axis=0,
            )
            s = jnp.where(jnp.tile(allowed, (1, heads)), s, -1e30)
        m_prev = m_sc[...]
        m_new = jnp.maximum(m_prev, jnp.max(s, axis=0, keepdims=True))
        alpha = jnp.exp(m_prev - m_new)
        p = jnp.exp(s - m_new)
        l_sc[...] = alpha * l_sc[...] + jnp.sum(p, axis=0, keepdims=True)
        acc_sc[...] = acc_sc[...] * alpha + lax.dot_general(
            v, p.astype(jnp.bfloat16), (((0,), (0,)), ((), ())),
            preferred_element_type=jnp.float32,
        )
        m_sc[...] = m_new

    lo = cnt_ref[qbl, 0]
    hi = cnt_ref[qbl, 1]

    def body(i, carry):
        n = lo + KEY_GROUP * i
        ents = []
        any_masked = False
        for j in range(KEY_GROUP):
            e = tab_ref[qbl, jnp.minimum(n + j, hi - 1)]
            valid = n + j < hi
            kind = jnp.where(valid, e >> 20, 1)
            ents.append((e & 255, (e >> 8) & 4095, kind, valid))
            any_masked = any_masked | (kind != 0)

        @pl.when(jnp.logical_not(any_masked))
        def _():
            absorb(ents, False)

        @pl.when(any_masked)
        def _():
            absorb(ents, True)

        return carry

    lax.fori_loop(0, (hi - lo + KEY_GROUP - 1) // KEY_GROUP, body, 0)

    if last:
        (o_ref,) = outs
        out = acc_sc[...] / l_sc[...]
        for h in range(heads):
            o_ref[:, h * HD:(h + 1) * HD] = out[:, h * BLOCK:(h + 1) * BLOCK].T.astype(o_ref.dtype)
    else:
        acc_o, m_o, l_o = outs
        acc_o[...] = acc_sc[...]
        m_o[...] = jnp.broadcast_to(m_sc[...], m_o.shape)
        l_o[...] = jnp.broadcast_to(l_sc[...], l_o.shape)


def block_tables(doc_start_q, keep_rows, first_blk, nkb, window, slot_of, own_rows):
    nqb = keep_rows.shape[0]
    nwin = window // BLOCK
    ds_blocks = doc_start_q.reshape(nqb, BLOCK)
    ds_first = ds_blocks[:, :1]
    ds_last = ds_blocks[:, -1:]
    qb = first_blk + jnp.arange(nqb, dtype=jnp.int32)[:, None]
    kb = jnp.arange(nkb, dtype=jnp.int32)[None, :]
    diag = kb == qb
    inwin = (kb <= qb) & (kb >= qb - nwin)
    keep = keep_rows == 1
    needed = inwin & (diag | (keep & (kb * BLOCK + BLOCK - 1 >= ds_first)))
    full = needed & (~diag) & (kb > qb - nwin) & (kb * BLOCK >= ds_last) & keep
    row_blk = jnp.clip(slot_of(kb), 0, 4095)
    own = row_blk < own_rows
    rank = jnp.where(diag, 0, jnp.where(full, 1, 2))
    sort_key = jnp.where(needed, jnp.where(own, rank, 3 + rank), 6).astype(jnp.int32)
    payload = (kb + 256 * row_blk + (1 << 20) * jnp.where(full, 0, 1)).astype(jnp.int32)
    payload = jnp.broadcast_to(payload, sort_key.shape)
    _, tab = lax.sort((sort_key, payload), dimension=1, is_stable=True, num_keys=1)
    n_own = jnp.sum(needed & own, axis=1).astype(jnp.int32)
    n_all = jnp.sum(needed, axis=1).astype(jnp.int32)
    zero = jnp.zeros_like(n_own)
    return tab, jnp.stack([zero, n_own], 1), jnp.stack([n_own, n_all], 1), ds_blocks


def attend_call(tab, cnt, keep_rows, base, ds_blocks, q_t, kv, state, *, window, first, last, row_base):
    heads, rows_here, _ = q_t.shape
    nqb = rows_here // BLOCK
    width = heads * BLOCK
    nk = kv.shape[0]
    kernel = functools.partial(
        attn_kernel, heads=heads, window=window, first=first, last=last, row_base=row_base
    )
    in_specs = [
        pl.BlockSpec((nqb, BLOCK), lambda i, *_: (0, 0)),
        pl.BlockSpec((heads, BLOCK, HD), lambda i, *_: (0, i, 0)),
        pl.BlockSpec((nk, 2 * HD), lambda i, *_: (0, 0)),
    ]
    state_specs = [
        pl.BlockSpec((HD, width), lambda i, *_: (i, 0)),
        pl.BlockSpec((8, width), lambda i, *_: (i, 0)),
        pl.BlockSpec((8, width), lambda i, *_: (i, 0)),
    ]
    state_shapes = [
        jax.ShapeDtypeStruct((nqb * HD, width), jnp.float32),
        jax.ShapeDtypeStruct((nqb * 8, width), jnp.float32),
        jax.ShapeDtypeStruct((nqb * 8, width), jnp.float32),
    ]
    args = [tab, cnt, keep_rows, base, ds_blocks, q_t, kv]
    if not first:
        in_specs += state_specs
        args += list(state)
    if last:
        out_specs = pl.BlockSpec((BLOCK, width), lambda i, *_: (i, 0))
        out_shape = jax.ShapeDtypeStruct((rows_here, width), q_t.dtype)
    else:
        out_specs = state_specs
        out_shape = state_shapes
    grid_spec = pltpu.PrefetchScalarGridSpec(
        num_scalar_prefetch=4,
        grid=(nqb,),
        in_specs=in_specs,
        out_specs=out_specs,
        scratch_shapes=[
            pltpu.VMEM((1, width), jnp.float32),
            pltpu.VMEM((1, width), jnp.float32),
            pltpu.VMEM((HD, width), jnp.float32),
        ],
    )
    flops = 4 * rows_here * heads * HD * BLOCK * 8
    cost = pl.CostEstimate(flops=flops, transcendentals=flops // (4 * HD), bytes_accessed=nk * 4 * HD)
    return pl.pallas_call(
        kernel, grid_spec=grid_spec, out_shape=out_shape, cost_estimate=cost
    )(*args)


def attention(q_local, kv_own, kv_rest, doc_start_q, keep_rows, first_row, window, nkb, slot_of):
    rows_here = q_local.shape[0]
    heads = q_local.shape[1] // HD
    first_blk = first_row // BLOCK
    own_rows = kv_own.shape[0] // 16
    tab, cnt_a, cnt_b, ds_blocks = block_tables(
        doc_start_q, keep_rows, first_blk, nkb, window, slot_of, own_rows
    )
    base = jnp.reshape(first_row, (1,)).astype(jnp.int32)
    keep_i = keep_rows.astype(jnp.int32)
    q_t = jnp.transpose(q_local.reshape(rows_here, heads, HD), (1, 0, 2))
    state = attend_call(
        tab, cnt_a, keep_i, base, ds_blocks, q_t, kv_own, None,
        window=window, first=True, last=False, row_base=0,
    )
    return attend_call(
        tab, cnt_b, keep_i, base, ds_blocks, q_t, kv_rest, state,
        window=window, first=False, last=True, row_base=own_rows,
    )


def shift(x, pairs):
    return lax.ppermute(x, "ctx", pairs)


def local(queries, keys, values, doc_ids, block_keep):
    rows_in = keys.shape[0]
    groups = keys.shape[1] // HD
    qkv = jnp.concatenate(
        [
            queries.reshape(rows_in, groups, -1),
            keys.reshape(rows_in, groups, HD),
            values.reshape(rows_in, groups, HD),
        ],
        axis=2,
    ).reshape(rows_in, -1)
    qkv_local = lax.all_to_all(qkv, "kvh", split_axis=1, concat_axis=0, tiled=True)
    q_width = queries.shape[1] // groups
    query_local = qkv_local[:, :q_width]
    kv_local = qkv_local[:, q_width:]
    rows_here = query_local.shape[0]
    per_dev = rows_here // BLOCK
    n_ctx = lax.axis_size("ctx")
    nx = NX
    nz = n_ctx // nx
    reach = n_ctx // 2 // nx
    window = (n_ctx // 2) * rows_here
    ctx = lax.axis_index("ctx")
    first_row = ctx * rows_here
    zq, xq = ctx // nx, ctx % nx

    def x_pairs(d):
        return [(z * nx + x, z * nx + (x + d) % nx) for z in range(nz) for x in range(nx)]

    docs = jnp.arange(N_DOC_IDS, dtype=jnp.int32)
    below = jnp.sum((doc_ids[None, :] < docs[:, None]).astype(jnp.int32), axis=1)
    below_x = jnp.stack(
        [below] + [shift(below, x_pairs(d)) for d in range(1, nx)], axis=0
    ).reshape(-1)
    tail = jnp.zeros((16, kv_local.shape[1]), jnp.float32)
    tail = tail.at[0, :nx * N_DOC_IDS].set((below_x // 32).astype(jnp.float32))
    tail = tail.at[1, :nx * N_DOC_IDS].set((below_x % 32).astype(jnp.float32))
    piece = jnp.concatenate([kv_local, tail.astype(kv_local.dtype)], axis=0)
    prow = piece.shape[0]

    z_step = [(c, (c + nx) % n_ctx) for c in range(n_ctx)]

    col = [piece]
    for _ in range(reach):
        col.append(shift(col[-1], z_step))
    half = (reach + 1) // 2
    early = list(range(1, half + 1))
    late = list(range(half + 1, reach))
    parts, tags = list(col), [(a, 0) for a in range(reach + 1)]

    def add(arr, tag_list):
        parts.append(arr)
        tags.extend(tag_list)

    def blocks(idx):
        return jnp.concatenate([col[a] for a in idx], axis=0) if len(idx) > 1 else col[idx[0]]

    e_plus = shift(blocks(early), x_pairs(1))
    e_minus = shift(blocks(early), x_pairs(nx - 1))
    add(e_plus, [(a, 1) for a in early])
    add(e_minus, [(a, nx - 1) for a in early])
    add(shift(e_plus, x_pairs(1)), [(a, 2) for a in early])
    extra = {d: jnp.where(xq + d < nx, col[0], col[reach]) for d in range(1, nx)}
    l_plus = shift(jnp.concatenate([col[a] for a in late] + [extra[1]], axis=0), x_pairs(1))
    l_minus = shift(jnp.concatenate([col[a] for a in late] + [extra[nx - 1]], axis=0), x_pairs(nx - 1))
    add(l_plus, [(a, 1) for a in late] + [("e", 1)])
    add(l_minus, [(a, nx - 1) for a in late] + [("e", nx - 1)])
    if late:
        relay = l_minus[: prow * len(late)]
        add(shift(relay, x_pairs(nx - 1)), [(a, 2) for a in late])
    add(shift(extra[2], x_pairs(2)), [("e", 2)])
    kv_own = jnp.concatenate(parts[:reach + 1], axis=0)
    kv_rest = jnp.concatenate(parts[reach + 1:], axis=0)

    n_slots = len(tags)
    table = np.zeros((reach + 1, nx), np.int32)
    for s, (a, d) in enumerate(tags):
        if a == "e":
            table[0, d] = s
            table[reach, d] = s
        else:
            table[a, d] = s
    tails = kv_own.reshape(reach + 1, prow, -1)[:, rows_here:rows_here + 2, :nx * N_DOC_IDS]
    tails = tails.astype(jnp.int32)
    below_col = (tails[:, 0, :] * 32 + tails[:, 1, :]).reshape(reach + 1, nx, N_DOC_IDS)
    a_ids = np.arange(reach + 1)[:, None]
    d_ids = np.arange(nx)[None, :]
    src_ctx = (zq - a_ids) * nx + (xq - d_ids) % nx
    floor_ctx = jnp.maximum(ctx - reach * nx, 0)
    use = (src_ctx >= floor_ctx) & (src_ctx <= ctx)
    below_sum = jnp.sum(jnp.where(use[:, :, None], below_col, 0), axis=(0, 1))
    onehot = doc_ids[:, None] == docs[None, :]
    doc_start = floor_ctx * rows_here + jnp.sum(jnp.where(onehot, below_sum[None, :], 0), axis=1)

    def slot_of(kb):
        cp = kb // per_dev
        a = zq - cp // nx
        d = (xq - cp % nx) % nx
        hit = (a[..., None, None] == np.arange(reach + 1)[:, None]) & (
            d[..., None, None] == np.arange(nx)[None, :]
        )
        slot = jnp.sum(jnp.where(hit, table, 0), axis=(-2, -1))
        return (slot * prow + (kb % per_dev) * BLOCK) // 16

    outputs = attention(
        query_local, kv_own, kv_rest, doc_start.astype(jnp.int32), block_keep, first_row,
        window, n_ctx * per_dev, slot_of,
    )
    return lax.all_to_all(outputs, "kvh", split_axis=0, concat_axis=1, tiled=True)


def solution(mesh):
    return jax.shard_map(
        local,
        mesh=mesh,
        in_specs=(
            P(("ctx", "kvh"), None),
            P(("ctx", "kvh"), None),
            P(("ctx", "kvh"), None),
            P("ctx"),
            P("ctx", None),
        ),
        out_specs=P(("ctx", "kvh"), None),
        check_vma=False,
    )
```

```python
import functools

import numpy as np

import jax
import jax.numpy as jnp
from jax import lax
from jax.experimental import pallas as pl
from jax.experimental.pallas import tpu as pltpu
from jax.sharding import PartitionSpec as P

HD = 128
BLOCK = 128
NX = 4
N_DOC_IDS = 8
KEY_GROUP = 8


def attn_kernel(
    tab_ref, cnt_ref, keep_ref, base_ref,
    qds_ref, q_ref, kv_ref, *rest,
    heads, window, first, last, row_base,
):
    if first:
        state_in = ()
    else:
        state_in, rest = rest[:3], rest[3:]
    outs, (m_sc, l_sc, acc_sc) = rest[:-3], rest[-3:]
    qbl = pl.program_id(0)
    qpos0 = base_ref[0] + qbl * BLOCK
    scale = HD ** (-0.5)
    width = heads * BLOCK
    qpos = qpos0 + lax.broadcasted_iota(jnp.int32, (BLOCK, BLOCK), 1)
    krel = lax.broadcasted_iota(jnp.int32, (BLOCK, BLOCK), 0)
    qds = qds_ref[pl.ds(qbl, 1), :]
    qmat = q_ref[...].reshape(width, HD)

    if first:
        m_sc[...] = jnp.full(m_sc.shape, -1e30, jnp.float32)
        l_sc[...] = jnp.zeros(l_sc.shape, jnp.float32)
        acc_sc[...] = jnp.zeros(acc_sc.shape, jnp.float32)
    else:
        acc_in, m_in, l_in = state_in
        acc_sc[...] = acc_in[...]
        m_sc[...] = m_in[0:1, :]
        l_sc[...] = l_in[0:1, :]

    def mask_of(kb):
        kpos = kb * BLOCK + krel
        keep = keep_ref[qbl, kb]
        earlier = (kpos < qpos) & (qpos - kpos < window) & (kpos >= qds) & (keep != 0)
        return (kpos == qpos) | earlier

    def absorb(ents, masked):
        starts = [pl.multiple_of((rb - row_base) * 16, 16) for _, rb, _, _ in ents]
        k = jnp.concatenate([kv_ref[pl.ds(st, BLOCK), :HD] for st in starts], axis=0)
        v = jnp.concatenate([kv_ref[pl.ds(st, BLOCK), HD:] for st in starts], axis=0)
        s = lax.dot_general(
            k, qmat, (((1,), (1,)), ((), ())), preferred_element_type=jnp.float32
        ) * scale
        if masked:
            allowed = jnp.concatenate(
                [
                    (mask_of(kb) | (kind == 0)) & valid
                    for kb, _, kind, valid in ents
                ],
                axis=0,
            )
            s = jnp.where(jnp.tile(allowed, (1, heads)), s, -1e30)
        m_prev = m_sc[...]
        m_new = jnp.maximum(m_prev, jnp.max(s, axis=0, keepdims=True))
        alpha = jnp.exp(m_prev - m_new)
        p = jnp.exp(s - m_new)
        l_sc[...] = alpha * l_sc[...] + jnp.sum(p, axis=0, keepdims=True)
        acc_sc[...] = acc_sc[...] * alpha + lax.dot_general(
            v, p.astype(jnp.bfloat16), (((0,), (0,)), ((), ())),
            preferred_element_type=jnp.float32,
        )
        m_sc[...] = m_new

    lo = cnt_ref[qbl, 0]
    hi = cnt_ref[qbl, 1]

    def body(i, carry):
        n = lo + KEY_GROUP * i
        ents = []
        any_masked = False
        for j in range(KEY_GROUP):
            e = tab_ref[qbl, jnp.minimum(n + j, hi - 1)]
            valid = n + j < hi
            kind = jnp.where(valid, e >> 20, 1)
            ents.append((e & 255, (e >> 8) & 4095, kind, valid))
            any_masked = any_masked | (kind != 0)

        @pl.when(jnp.logical_not(any_masked))
        def _():
            absorb(ents, False)

        @pl.when(any_masked)
        def _():
            absorb(ents, True)

        return carry

    lax.fori_loop(0, (hi - lo + KEY_GROUP - 1) // KEY_GROUP, body, 0)

    if last:
        (o_ref,) = outs
        out = acc_sc[...] / l_sc[...]
        for h in range(heads):
            o_ref[:, h * HD:(h + 1) * HD] = out[:, h * BLOCK:(h + 1) * BLOCK].T.astype(o_ref.dtype)
    else:
        acc_o, m_o, l_o = outs
        acc_o[...] = acc_sc[...]
        m_o[...] = jnp.broadcast_to(m_sc[...], m_o.shape)
        l_o[...] = jnp.broadcast_to(l_sc[...], l_o.shape)


def block_tables(doc_start_q, keep_rows, first_blk, nkb, window, slot_of, own_rows):
    nqb = keep_rows.shape[0]
    nwin = window // BLOCK
    ds_blocks = doc_start_q.reshape(nqb, BLOCK)
    ds_first = ds_blocks[:, :1]
    ds_last = ds_blocks[:, -1:]
    qb = first_blk + jnp.arange(nqb, dtype=jnp.int32)[:, None]
    kb = jnp.arange(nkb, dtype=jnp.int32)[None, :]
    diag = kb == qb
    inwin = (kb <= qb) & (kb >= qb - nwin)
    keep = keep_rows == 1
    needed = inwin & (diag | (keep & (kb * BLOCK + BLOCK - 1 >= ds_first)))
    full = needed & (~diag) & (kb > qb - nwin) & (kb * BLOCK >= ds_last) & keep
    row_blk = jnp.clip(slot_of(kb), 0, 4095)
    own = row_blk < own_rows
    rank = jnp.where(diag, 0, jnp.where(full, 1, 2))
    sort_key = jnp.where(needed, jnp.where(own, rank, 3 + rank), 6).astype(jnp.int32)
    payload = (kb + 256 * row_blk + (1 << 20) * jnp.where(full, 0, 1)).astype(jnp.int32)
    payload = jnp.broadcast_to(payload, sort_key.shape)
    _, tab = lax.sort((sort_key, payload), dimension=1, is_stable=True, num_keys=1)
    n_own = jnp.sum(needed & own, axis=1).astype(jnp.int32)
    n_all = jnp.sum(needed, axis=1).astype(jnp.int32)
    zero = jnp.zeros_like(n_own)
    return tab, jnp.stack([zero, n_own], 1), jnp.stack([n_own, n_all], 1), ds_blocks


def attend_call(tab, cnt, keep_rows, base, ds_blocks, q_t, kv, state, *, window, first, last, row_base):
    heads, rows_here, _ = q_t.shape
    nqb = rows_here // BLOCK
    width = heads * BLOCK
    nk = kv.shape[0]
    kernel = functools.partial(
        attn_kernel, heads=heads, window=window, first=first, last=last, row_base=row_base
    )
    in_specs = [
        pl.BlockSpec((nqb, BLOCK), lambda i, *_: (0, 0)),
        pl.BlockSpec((heads, BLOCK, HD), lambda i, *_: (0, i, 0)),
        pl.BlockSpec((nk, 2 * HD), lambda i, *_: (0, 0)),
    ]
    state_specs = [
        pl.BlockSpec((HD, width), lambda i, *_: (i, 0)),
        pl.BlockSpec((8, width), lambda i, *_: (i, 0)),
        pl.BlockSpec((8, width), lambda i, *_: (i, 0)),
    ]
    state_shapes = [
        jax.ShapeDtypeStruct((nqb * HD, width), jnp.float32),
        jax.ShapeDtypeStruct((nqb * 8, width), jnp.float32),
        jax.ShapeDtypeStruct((nqb * 8, width), jnp.float32),
    ]
    args = [tab, cnt, keep_rows, base, ds_blocks, q_t, kv]
    if not first:
        in_specs += state_specs
        args += list(state)
    if last:
        out_specs = pl.BlockSpec((BLOCK, width), lambda i, *_: (i, 0))
        out_shape = jax.ShapeDtypeStruct((rows_here, width), q_t.dtype)
    else:
        out_specs = state_specs
        out_shape = state_shapes
    grid_spec = pltpu.PrefetchScalarGridSpec(
        num_scalar_prefetch=4,
        grid=(nqb,),
        in_specs=in_specs,
        out_specs=out_specs,
        scratch_shapes=[
            pltpu.VMEM((1, width), jnp.float32),
            pltpu.VMEM((1, width), jnp.float32),
            pltpu.VMEM((HD, width), jnp.float32),
        ],
    )
    flops = 4 * rows_here * heads * HD * BLOCK * 8
    cost = pl.CostEstimate(flops=flops, transcendentals=flops // (4 * HD), bytes_accessed=nk * 4 * HD)
    return pl.pallas_call(
        kernel, grid_spec=grid_spec, out_shape=out_shape, cost_estimate=cost
    )(*args)


def attention(q_local, kv_own, kv_rest, doc_start_q, keep_rows, first_row, window, nkb, slot_of):
    rows_here = q_local.shape[0]
    heads = q_local.shape[1] // HD
    first_blk = first_row // BLOCK
    own_rows = kv_own.shape[0] // 16
    tab, cnt_a, cnt_b, ds_blocks = block_tables(
        doc_start_q, keep_rows, first_blk, nkb, window, slot_of, own_rows
    )
    base = jnp.reshape(first_row, (1,)).astype(jnp.int32)
    keep_i = keep_rows.astype(jnp.int32)
    q_t = jnp.transpose(q_local.reshape(rows_here, heads, HD), (1, 0, 2))
    state = attend_call(
        tab, cnt_a, keep_i, base, ds_blocks, q_t, kv_own, None,
        window=window, first=True, last=False, row_base=0,
    )
    return attend_call(
        tab, cnt_b, keep_i, base, ds_blocks, q_t, kv_rest, state,
        window=window, first=False, last=True, row_base=own_rows,
    )


def shift(x, pairs):
    return lax.ppermute(x, "ctx", pairs)


def local(queries, keys, values, doc_ids, block_keep):
    rows_in = keys.shape[0]
    groups = keys.shape[1] // HD
    qkv = jnp.concatenate(
        [
            queries.reshape(rows_in, groups, -1),
            keys.reshape(rows_in, groups, HD),
            values.reshape(rows_in, groups, HD),
        ],
        axis=2,
    ).reshape(rows_in, -1)
    qkv_local = lax.all_to_all(qkv, "kvh", split_axis=1, concat_axis=0, tiled=True)
    q_width = queries.shape[1] // groups
    query_local = qkv_local[:, :q_width]
    kv_local = qkv_local[:, q_width:]
    rows_here = query_local.shape[0]
    per_dev = rows_here // BLOCK
    n_ctx = lax.axis_size("ctx")
    nx = NX
    nz = n_ctx // nx
    reach = n_ctx // 2 // nx
    window = (n_ctx // 2) * rows_here
    ctx = lax.axis_index("ctx")
    first_row = ctx * rows_here
    zq, xq = ctx // nx, ctx % nx

    def x_pairs(d):
        return [(z * nx + x, z * nx + (x + d) % nx) for z in range(nz) for x in range(nx)]

    docs = jnp.arange(N_DOC_IDS, dtype=jnp.int32)
    below = jnp.sum((doc_ids[None, :] < docs[:, None]).astype(jnp.int32), axis=1)
    below_x = jnp.stack(
        [below] + [shift(below, x_pairs(d)) for d in range(1, nx)], axis=0
    ).reshape(-1)
    tail = jnp.zeros((16, kv_local.shape[1]), jnp.float32)
    tail = tail.at[0, :nx * N_DOC_IDS].set((below_x // 32).astype(jnp.float32))
    tail = tail.at[1, :nx * N_DOC_IDS].set((below_x % 32).astype(jnp.float32))
    piece = jnp.concatenate([kv_local, tail.astype(kv_local.dtype)], axis=0)
    prow = piece.shape[0]

    z_step = [(c, (c + nx) % n_ctx) for c in range(n_ctx)]

    col = [piece]
    for _ in range(reach):
        col.append(shift(col[-1], z_step))
    half = (reach + 1) // 2
    early = list(range(1, half + 1))
    late = list(range(half + 1, reach))
    parts, tags = list(col), [(a, 0) for a in range(reach + 1)]

    def add(arr, tag_list):
        parts.append(arr)
        tags.extend(tag_list)

    def blocks(idx):
        return jnp.concatenate([col[a] for a in idx], axis=0) if len(idx) > 1 else col[idx[0]]

    e_plus = shift(blocks(early), x_pairs(1))
    e_minus = shift(blocks(early), x_pairs(nx - 1))
    add(e_plus, [(a, 1) for a in early])
    add(e_minus, [(a, nx - 1) for a in early])
    add(shift(e_plus, x_pairs(1)), [(a, 2) for a in early])
    extra = {d: jnp.where(xq + d < nx, col[0], col[reach]) for d in range(1, nx)}
    l_plus = shift(jnp.concatenate([col[a] for a in late] + [extra[1]], axis=0), x_pairs(1))
    l_minus = shift(jnp.concatenate([col[a] for a in late] + [extra[nx - 1]], axis=0), x_pairs(nx - 1))
    add(l_plus, [(a, 1) for a in late] + [("e", 1)])
    add(l_minus, [(a, nx - 1) for a in late] + [("e", nx - 1)])
    if late:
        relay = l_minus[: prow * len(late)]
        add(shift(relay, x_pairs(nx - 1)), [(a, 2) for a in late])
    add(shift(extra[2], x_pairs(2)), [("e", 2)])
    kv_own = jnp.concatenate(parts[:reach + 1], axis=0)
    kv_rest = jnp.concatenate(parts[reach + 1:], axis=0)

    n_slots = len(tags)
    table = np.zeros((reach + 1, nx), np.int32)
    for s, (a, d) in enumerate(tags):
        if a == "e":
            table[0, d] = s
            table[reach, d] = s
        else:
            table[a, d] = s
    tails = kv_own.reshape(reach + 1, prow, -1)[:, rows_here:rows_here + 2, :nx * N_DOC_IDS]
    tails = tails.astype(jnp.int32)
    below_col = (tails[:, 0, :] * 32 + tails[:, 1, :]).reshape(reach + 1, nx, N_DOC_IDS)
    a_ids = np.arange(reach + 1)[:, None]
    d_ids = np.arange(nx)[None, :]
    src_ctx = (zq - a_ids) * nx + (xq - d_ids) % nx
    floor_ctx = jnp.maximum(ctx - reach * nx, 0)
    use = (src_ctx >= floor_ctx) & (src_ctx <= ctx)
    below_sum = jnp.sum(jnp.where(use[:, :, None], below_col, 0), axis=(0, 1))
    onehot = doc_ids[:, None] == docs[None, :]
    doc_start = floor_ctx * rows_here + jnp.sum(jnp.where(onehot, below_sum[None, :], 0), axis=1)

    def slot_of(kb):
        cp = kb // per_dev
        a = zq - cp // nx
        d = (xq - cp % nx) % nx
        hit = (a[..., None, None] == np.arange(reach + 1)[:, None]) & (
            d[..., None, None] == np.arange(nx)[None, :]
        )
        slot = jnp.sum(jnp.where(hit, table, 0), axis=(-2, -1))
        return (slot * prow + (kb % per_dev) * BLOCK) // 16

    outputs = attention(
        query_local, kv_own, kv_rest, doc_start.astype(jnp.int32), block_keep, first_row,
        window, n_ctx * per_dev, slot_of,
    )
    return lax.all_to_all(outputs, "kvh", split_axis=0, concat_axis=1, tiled=True)


def solution(mesh):
    return jax.shard_map(
        local,
        mesh=mesh,
        in_specs=(
            P(("ctx", "kvh"), None),
            P(("ctx", "kvh"), None),
            P(("ctx", "kvh"), None),
            P("ctx"),
            P("ctx", None),
        ),
        out_specs=P(("ctx", "kvh"), None),
        check_vma=False,
    )
```

```python
import functools

import numpy as np

import jax
import jax.numpy as jnp
from jax import lax
from jax.experimental import pallas as pl
from jax.experimental.pallas import tpu as pltpu
from jax.sharding import PartitionSpec as P

HD = 128
BLOCK = 128
NX = 4
N_DOC_IDS = 8
KEY_GROUP = 4


def attn_kernel(
    tab_ref, cnt_ref, keep_ref, base_ref,
    qds_ref, q_ref, kv_ref, *rest,
    heads, window, first, last, row_base,
):
    if first:
        state_in = ()
    else:
        state_in, rest = rest[:3], rest[3:]
    outs, (m_sc, l_sc, acc_sc) = rest[:-3], rest[-3:]
    qbl = pl.program_id(0)
    qpos0 = base_ref[0] + qbl * BLOCK
    scale = HD ** (-0.5)
    width = heads * BLOCK
    qpos = qpos0 + lax.broadcasted_iota(jnp.int32, (BLOCK, BLOCK), 1)
    krel = lax.broadcasted_iota(jnp.int32, (BLOCK, BLOCK), 0)
    qds = qds_ref[pl.ds(qbl, 1), :]
    qmat = q_ref[...].reshape(width, HD)

    if first:
        m_sc[...] = jnp.full(m_sc.shape, -1e30, jnp.float32)
        l_sc[...] = jnp.zeros(l_sc.shape, jnp.float32)
        acc_sc[...] = jnp.zeros(acc_sc.shape, jnp.float32)
    else:
        acc_in, m_in, l_in = state_in
        acc_sc[...] = acc_in[...]
        m_sc[...] = m_in[0:1, :]
        l_sc[...] = l_in[0:1, :]

    def mask_of(kb):
        kpos = kb * BLOCK + krel
        keep = keep_ref[qbl, kb]
        earlier = (kpos < qpos) & (qpos - kpos < window) & (kpos >= qds) & (keep != 0)
        return (kpos == qpos) | earlier

    def absorb(ents, masked):
        starts = [pl.multiple_of((rb - row_base) * 16, 16) for _, rb, _, _ in ents]
        k = jnp.concatenate([kv_ref[pl.ds(st, BLOCK), :HD] for st in starts], axis=0)
        v = jnp.concatenate([kv_ref[pl.ds(st, BLOCK), HD:] for st in starts], axis=0)
        s = lax.dot_general(
            k, qmat, (((1,), (1,)), ((), ())), preferred_element_type=jnp.float32
        ) * scale
        if masked:
            allowed = jnp.concatenate(
                [
                    (mask_of(kb) | (kind == 0)) & valid
                    for kb, _, kind, valid in ents
                ],
                axis=0,
            )
            s = jnp.where(jnp.tile(allowed, (1, heads)), s, -1e30)
        m_prev = m_sc[...]
        m_new = jnp.maximum(m_prev, jnp.max(s, axis=0, keepdims=True))
        alpha = jnp.exp(m_prev - m_new)
        p = jnp.exp(s - m_new)
        l_sc[...] = alpha * l_sc[...] + jnp.sum(p, axis=0, keepdims=True)
        acc_sc[...] = acc_sc[...] * alpha + lax.dot_general(
            v, p.astype(jnp.bfloat16), (((0,), (0,)), ((), ())),
            preferred_element_type=jnp.float32,
        )
        m_sc[...] = m_new

    lo = cnt_ref[qbl, 0]
    hi = cnt_ref[qbl, 1]

    def body(i, carry):
        n = lo + KEY_GROUP * i
        ents = []
        any_masked = False
        for j in range(KEY_GROUP):
            e = tab_ref[qbl, jnp.minimum(n + j, hi - 1)]
            valid = n + j < hi
            kind = jnp.where(valid, e >> 20, 1)
            ents.append((e & 255, (e >> 8) & 4095, kind, valid))
            any_masked = any_masked | (kind != 0)

        @pl.when(jnp.logical_not(any_masked))
        def _():
            absorb(ents, False)

        @pl.when(any_masked)
        def _():
            absorb(ents, True)

        return carry

    lax.fori_loop(0, (hi - lo + KEY_GROUP - 1) // KEY_GROUP, body, 0)

    if last:
        (o_ref,) = outs
        out = acc_sc[...] / l_sc[...]
        for h in range(heads):
            o_ref[:, h * HD:(h + 1) * HD] = out[:, h * BLOCK:(h + 1) * BLOCK].T.astype(o_ref.dtype)
    else:
        acc_o, m_o, l_o = outs
        acc_o[...] = acc_sc[...]
        m_o[...] = jnp.broadcast_to(m_sc[...], m_o.shape)
        l_o[...] = jnp.broadcast_to(l_sc[...], l_o.shape)


def block_tables(doc_start_q, keep_rows, first_blk, nkb, window, slot_of, own_rows):
    nqb = keep_rows.shape[0]
    nwin = window // BLOCK
    ds_blocks = doc_start_q.reshape(nqb, BLOCK)
    ds_first = ds_blocks[:, :1]
    ds_last = ds_blocks[:, -1:]
    qb = first_blk + jnp.arange(nqb, dtype=jnp.int32)[:, None]
    kb = jnp.arange(nkb, dtype=jnp.int32)[None, :]
    diag = kb == qb
    inwin = (kb <= qb) & (kb >= qb - nwin)
    keep = keep_rows == 1
    needed = inwin & (diag | (keep & (kb * BLOCK + BLOCK - 1 >= ds_first)))
    full = needed & (~diag) & (kb > qb - nwin) & (kb * BLOCK >= ds_last) & keep
    row_blk = jnp.clip(slot_of(kb), 0, 4095)
    own = row_blk < own_rows
    rank = jnp.where(diag, 0, jnp.where(full, 1, 2))
    sort_key = jnp.where(needed, jnp.where(own, rank, 3 + rank), 6).astype(jnp.int32)
    payload = (kb + 256 * row_blk + (1 << 20) * jnp.where(full, 0, 1)).astype(jnp.int32)
    payload = jnp.broadcast_to(payload, sort_key.shape)
    _, tab = lax.sort((sort_key, payload), dimension=1, is_stable=True, num_keys=1)
    n_own = jnp.sum(needed & own, axis=1).astype(jnp.int32)
    n_all = jnp.sum(needed, axis=1).astype(jnp.int32)
    zero = jnp.zeros_like(n_own)
    return tab, jnp.stack([zero, n_own], 1), jnp.stack([n_own, n_all], 1), ds_blocks


def attend_call(tab, cnt, keep_rows, base, ds_blocks, q_t, kv, state, *, window, first, last, row_base):
    heads, rows_here, _ = q_t.shape
    nqb = rows_here // BLOCK
    width = heads * BLOCK
    nk = kv.shape[0]
    kernel = functools.partial(
        attn_kernel, heads=heads, window=window, first=first, last=last, row_base=row_base
    )
    in_specs = [
        pl.BlockSpec((nqb, BLOCK), lambda i, *_: (0, 0)),
        pl.BlockSpec((heads, BLOCK, HD), lambda i, *_: (0, i, 0)),
        pl.BlockSpec((nk, 2 * HD), lambda i, *_: (0, 0)),
    ]
    state_specs = [
        pl.BlockSpec((HD, width), lambda i, *_: (i, 0)),
        pl.BlockSpec((8, width), lambda i, *_: (i, 0)),
        pl.BlockSpec((8, width), lambda i, *_: (i, 0)),
    ]
    state_shapes = [
        jax.ShapeDtypeStruct((nqb * HD, width), jnp.float32),
        jax.ShapeDtypeStruct((nqb * 8, width), jnp.float32),
        jax.ShapeDtypeStruct((nqb * 8, width), jnp.float32),
    ]
    args = [tab, cnt, keep_rows, base, ds_blocks, q_t, kv]
    if not first:
        in_specs += state_specs
        args += list(state)
    if last:
        out_specs = pl.BlockSpec((BLOCK, width), lambda i, *_: (i, 0))
        out_shape = jax.ShapeDtypeStruct((rows_here, width), q_t.dtype)
    else:
        out_specs = state_specs
        out_shape = state_shapes
    grid_spec = pltpu.PrefetchScalarGridSpec(
        num_scalar_prefetch=4,
        grid=(nqb,),
        in_specs=in_specs,
        out_specs=out_specs,
        scratch_shapes=[
            pltpu.VMEM((1, width), jnp.float32),
            pltpu.VMEM((1, width), jnp.float32),
            pltpu.VMEM((HD, width), jnp.float32),
        ],
    )
    flops = 4 * rows_here * heads * HD * BLOCK * 8
    cost = pl.CostEstimate(flops=flops, transcendentals=flops // (4 * HD), bytes_accessed=nk * 4 * HD)
    return pl.pallas_call(
        kernel, grid_spec=grid_spec, out_shape=out_shape, cost_estimate=cost
    )(*args)


def attention(q_local, kv_own, kv_rest, doc_start_q, keep_rows, first_row, window, nkb, slot_of):
    rows_here = q_local.shape[0]
    heads = q_local.shape[1] // HD
    first_blk = first_row // BLOCK
    own_rows = kv_own.shape[0] // 16
    tab, cnt_a, cnt_b, ds_blocks = block_tables(
        doc_start_q, keep_rows, first_blk, nkb, window, slot_of, own_rows
    )
    base = jnp.reshape(first_row, (1,)).astype(jnp.int32)
    keep_i = keep_rows.astype(jnp.int32)
    q_t = jnp.transpose(q_local.reshape(rows_here, heads, HD), (1, 0, 2))
    state = attend_call(
        tab, cnt_a, keep_i, base, ds_blocks, q_t, kv_own, None,
        window=window, first=True, last=False, row_base=0,
    )
    return attend_call(
        tab, cnt_b, keep_i, base, ds_blocks, q_t, kv_rest, state,
        window=window, first=False, last=True, row_base=own_rows,
    )


def shift(x, pairs):
    return lax.ppermute(x, "ctx", pairs)


def local(queries, keys, values, doc_ids, block_keep):
    rows_in = keys.shape[0]
    groups = keys.shape[1] // HD
    kv = jnp.concatenate(
        [keys.reshape(rows_in, groups, HD), values.reshape(rows_in, groups, HD)], axis=2
    ).reshape(rows_in, -1)
    kv_local = lax.all_to_all(kv, "kvh", split_axis=1, concat_axis=0, tiled=True)
    query_local = lax.all_to_all(queries, "kvh", split_axis=1, concat_axis=0, tiled=True)
    rows_here = query_local.shape[0]
    per_dev = rows_here // BLOCK
    n_ctx = lax.axis_size("ctx")
    nx = NX
    nz = n_ctx // nx
    reach = n_ctx // 2 // nx
    window = (n_ctx // 2) * rows_here
    ctx = lax.axis_index("ctx")
    first_row = ctx * rows_here
    zq, xq = ctx // nx, ctx % nx

    def x_pairs(d):
        return [(z * nx + x, z * nx + (x + d) % nx) for z in range(nz) for x in range(nx)]

    docs = jnp.arange(N_DOC_IDS, dtype=jnp.int32)
    below = jnp.sum((doc_ids[None, :] < docs[:, None]).astype(jnp.int32), axis=1)
    below_x = jnp.stack(
        [below] + [shift(below, x_pairs(d)) for d in range(1, nx)], axis=0
    ).reshape(-1)
    tail = jnp.zeros((16, kv_local.shape[1]), jnp.float32)
    tail = tail.at[0, :nx * N_DOC_IDS].set((below_x // 32).astype(jnp.float32))
    tail = tail.at[1, :nx * N_DOC_IDS].set((below_x % 32).astype(jnp.float32))
    piece = jnp.concatenate([kv_local, tail.astype(kv_local.dtype)], axis=0)
    prow = piece.shape[0]

    z_step = [(c, (c + nx) % n_ctx) for c in range(n_ctx)]

    col = [piece]
    for _ in range(reach):
        col.append(shift(col[-1], z_step))
    half = (reach + 1) // 2
    early = list(range(1, half + 1))
    late = list(range(half + 1, reach))
    parts, tags = list(col), [(a, 0) for a in range(reach + 1)]

    def add(arr, tag_list):
        parts.append(arr)
        tags.extend(tag_list)

    def blocks(idx):
        return jnp.concatenate([col[a] for a in idx], axis=0) if len(idx) > 1 else col[idx[0]]

    e_plus = shift(blocks(early), x_pairs(1))
    e_minus = shift(blocks(early), x_pairs(nx - 1))
    add(e_plus, [(a, 1) for a in early])
    add(e_minus, [(a, nx - 1) for a in early])
    add(shift(e_plus, x_pairs(1)), [(a, 2) for a in early])
    extra = {d: jnp.where(xq + d < nx, col[0], col[reach]) for d in range(1, nx)}
    l_plus = shift(jnp.concatenate([col[a] for a in late] + [extra[1]], axis=0), x_pairs(1))
    l_minus = shift(jnp.concatenate([col[a] for a in late] + [extra[nx - 1]], axis=0), x_pairs(nx - 1))
    add(l_plus, [(a, 1) for a in late] + [("e", 1)])
    add(l_minus, [(a, nx - 1) for a in late] + [("e", nx - 1)])
    if late:
        relay = l_minus[: prow * len(late)]
        add(shift(relay, x_pairs(nx - 1)), [(a, 2) for a in late])
    add(shift(extra[2], x_pairs(2)), [("e", 2)])
    kv_own = jnp.concatenate(parts[:reach + 1], axis=0)
    kv_rest = jnp.concatenate(parts[reach + 1:], axis=0)

    n_slots = len(tags)
    table = np.zeros((reach + 1, nx), np.int32)
    for s, (a, d) in enumerate(tags):
        if a == "e":
            table[0, d] = s
            table[reach, d] = s
        else:
            table[a, d] = s
    tails = kv_own.reshape(reach + 1, prow, -1)[:, rows_here:rows_here + 2, :nx * N_DOC_IDS]
    tails = tails.astype(jnp.int32)
    below_col = (tails[:, 0, :] * 32 + tails[:, 1, :]).reshape(reach + 1, nx, N_DOC_IDS)
    a_ids = np.arange(reach + 1)[:, None]
    d_ids = np.arange(nx)[None, :]
    src_ctx = (zq - a_ids) * nx + (xq - d_ids) % nx
    floor_ctx = jnp.maximum(ctx - reach * nx, 0)
    use = (src_ctx >= floor_ctx) & (src_ctx <= ctx)
    below_sum = jnp.sum(jnp.where(use[:, :, None], below_col, 0), axis=(0, 1))
    onehot = doc_ids[:, None] == docs[None, :]
    doc_start = floor_ctx * rows_here + jnp.sum(jnp.where(onehot, below_sum[None, :], 0), axis=1)

    def slot_of(kb):
        cp = kb // per_dev
        a = zq - cp // nx
        d = (xq - cp % nx) % nx
        hit = (a[..., None, None] == np.arange(reach + 1)[:, None]) & (
            d[..., None, None] == np.arange(nx)[None, :]
        )
        slot = jnp.sum(jnp.where(hit, table, 0), axis=(-2, -1))
        return (slot * prow + (kb % per_dev) * BLOCK) // 16

    outputs = attention(
        query_local, kv_own, kv_rest, doc_start.astype(jnp.int32), block_keep, first_row,
        window, n_ctx * per_dev, slot_of,
    )
    return lax.all_to_all(outputs, "kvh", split_axis=0, concat_axis=1, tiled=True)


def solution(mesh):
    return jax.shard_map(
        local,
        mesh=mesh,
        in_specs=(
            P(("ctx", "kvh"), None),
            P(("ctx", "kvh"), None),
            P(("ctx", "kvh"), None),
            P("ctx"),
            P("ctx", None),
        ),
        out_specs=P(("ctx", "kvh"), None),
        check_vma=False,
    )
```

```python
import functools

import numpy as np

import jax
import jax.numpy as jnp
from jax import lax
from jax.experimental import pallas as pl
from jax.experimental.pallas import tpu as pltpu
from jax.sharding import PartitionSpec as P

HD = 128
BLOCK = 128
NX = 4
N_DOC_IDS = 8
KEY_GROUP = 4


def attn_kernel(
    tab_ref, cnt_ref, keep_ref, base_ref,
    qds_ref, q_ref, kv_ref, *rest,
    heads, window, first, last, row_base,
):
    if first:
        state_in = ()
    else:
        state_in, rest = rest[:3], rest[3:]
    outs, (m_sc, l_sc, acc_sc) = rest[:-3], rest[-3:]
    qbl = pl.program_id(0)
    qpos0 = base_ref[0] + qbl * BLOCK
    scale = HD ** (-0.5)
    width = heads * BLOCK
    qpos = qpos0 + lax.broadcasted_iota(jnp.int32, (BLOCK, BLOCK), 1)
    krel = lax.broadcasted_iota(jnp.int32, (BLOCK, BLOCK), 0)
    qds = qds_ref[pl.ds(qbl, 1), :]
    qmat = q_ref[...].reshape(width, HD)

    if first:
        m_sc[...] = jnp.full(m_sc.shape, -1e30, jnp.float32)
        l_sc[...] = jnp.zeros(l_sc.shape, jnp.float32)
        acc_sc[...] = jnp.zeros(acc_sc.shape, jnp.float32)
    else:
        acc_in, m_in, l_in = state_in
        acc_sc[...] = acc_in[...]
        m_sc[...] = m_in[0:1, :]
        l_sc[...] = l_in[0:1, :]

    def mask_of(kb):
        kpos = kb * BLOCK + krel
        keep = keep_ref[qbl, kb]
        earlier = (kpos < qpos) & (qpos - kpos < window) & (kpos >= qds) & (keep != 0)
        return (kpos == qpos) | earlier

    def absorb(ents, masked):
        starts = [pl.multiple_of((rb - row_base) * 16, 16) for _, rb, _, _ in ents]
        k = jnp.concatenate([kv_ref[pl.ds(st, BLOCK), :HD] for st in starts], axis=0)
        v = jnp.concatenate([kv_ref[pl.ds(st, BLOCK), HD:] for st in starts], axis=0)
        s = lax.dot_general(
            k, qmat, (((1,), (1,)), ((), ())), preferred_element_type=jnp.float32
        ) * scale
        if masked:
            allowed = jnp.concatenate(
                [
                    (mask_of(kb) | (kind == 0)) & valid
                    for kb, _, kind, valid in ents
                ],
                axis=0,
            )
            s = jnp.where(jnp.tile(allowed, (1, heads)), s, -1e30)
        m_prev = m_sc[...]
        m_new = jnp.maximum(m_prev, jnp.max(s, axis=0, keepdims=True))
        alpha = jnp.exp(m_prev - m_new)
        p = jnp.exp(s - m_new)
        l_sc[...] = alpha * l_sc[...] + jnp.sum(p, axis=0, keepdims=True)
        acc_sc[...] = acc_sc[...] * alpha + lax.dot_general(
            v, p.astype(jnp.bfloat16), (((0,), (0,)), ((), ())),
            preferred_element_type=jnp.float32,
        )
        m_sc[...] = m_new

    lo = cnt_ref[qbl, 0]
    hi = cnt_ref[qbl, 1]

    def body(i, carry):
        n = lo + KEY_GROUP * i
        ents = []
        any_masked = False
        for j in range(KEY_GROUP):
            e = tab_ref[qbl, jnp.minimum(n + j, hi - 1)]
            valid = n + j < hi
            kind = jnp.where(valid, e >> 20, 1)
            ents.append((e & 255, (e >> 8) & 4095, kind, valid))
            any_masked = any_masked | (kind != 0)

        @pl.when(jnp.logical_not(any_masked))
        def _():
            absorb(ents, False)

        @pl.when(any_masked)
        def _():
            absorb(ents, True)

        return carry

    lax.fori_loop(0, (hi - lo + KEY_GROUP - 1) // KEY_GROUP, body, 0)

    if last:
        (o_ref,) = outs
        out = acc_sc[...] / l_sc[...]
        for h in range(heads):
            o_ref[:, h * HD:(h + 1) * HD] = out[:, h * BLOCK:(h + 1) * BLOCK].T.astype(o_ref.dtype)
    else:
        acc_o, m_o, l_o = outs
        acc_o[...] = acc_sc[...]
        m_o[...] = jnp.broadcast_to(m_sc[...], m_o.shape)
        l_o[...] = jnp.broadcast_to(l_sc[...], l_o.shape)


def block_tables(doc_start_q, keep_rows, first_blk, nkb, window, slot_of, own_rows):
    nqb = keep_rows.shape[0]
    nwin = window // BLOCK
    ds_blocks = doc_start_q.reshape(nqb, BLOCK)
    ds_first = ds_blocks[:, :1]
    ds_last = ds_blocks[:, -1:]
    qb = first_blk + jnp.arange(nqb, dtype=jnp.int32)[:, None]
    kb = jnp.arange(nkb, dtype=jnp.int32)[None, :]
    diag = kb == qb
    inwin = (kb <= qb) & (kb >= qb - nwin)
    keep = keep_rows == 1
    needed = inwin & (diag | (keep & (kb * BLOCK + BLOCK - 1 >= ds_first)))
    full = needed & (~diag) & (kb > qb - nwin) & (kb * BLOCK >= ds_last) & keep
    row_blk = jnp.clip(slot_of(kb), 0, 4095)
    own = row_blk < own_rows
    rank = jnp.where(diag, 0, jnp.where(full, 1, 2))
    sort_key = jnp.where(needed, jnp.where(own, rank, 3 + rank), 6).astype(jnp.int32)
    payload = (kb + 256 * row_blk + (1 << 20) * jnp.where(full, 0, 1)).astype(jnp.int32)
    payload = jnp.broadcast_to(payload, sort_key.shape)
    _, tab = lax.sort((sort_key, payload), dimension=1, is_stable=True, num_keys=1)
    n_own = jnp.sum(needed & own, axis=1).astype(jnp.int32)
    n_all = jnp.sum(needed, axis=1).astype(jnp.int32)
    zero = jnp.zeros_like(n_own)
    return tab, jnp.stack([zero, n_own], 1), jnp.stack([n_own, n_all], 1), ds_blocks


def attend_call(tab, cnt, keep_rows, base, ds_blocks, q_t, kv, state, *, window, first, last, row_base):
    heads, rows_here, _ = q_t.shape
    nqb = rows_here // BLOCK
    width = heads * BLOCK
    nk = kv.shape[0]
    kernel = functools.partial(
        attn_kernel, heads=heads, window=window, first=first, last=last, row_base=row_base
    )
    in_specs = [
        pl.BlockSpec((nqb, BLOCK), lambda i, *_: (0, 0)),
        pl.BlockSpec((heads, BLOCK, HD), lambda i, *_: (0, i, 0)),
        pl.BlockSpec((nk, 2 * HD), lambda i, *_: (0, 0)),
    ]
    state_specs = [
        pl.BlockSpec((HD, width), lambda i, *_: (i, 0)),
        pl.BlockSpec((8, width), lambda i, *_: (i, 0)),
        pl.BlockSpec((8, width), lambda i, *_: (i, 0)),
    ]
    state_shapes = [
        jax.ShapeDtypeStruct((nqb * HD, width), jnp.float32),
        jax.ShapeDtypeStruct((nqb * 8, width), jnp.float32),
        jax.ShapeDtypeStruct((nqb * 8, width), jnp.float32),
    ]
    args = [tab, cnt, keep_rows, base, ds_blocks, q_t, kv]
    if not first:
        in_specs += state_specs
        args += list(state)
    if last:
        out_specs = pl.BlockSpec((BLOCK, width), lambda i, *_: (i, 0))
        out_shape = jax.ShapeDtypeStruct((rows_here, width), q_t.dtype)
    else:
        out_specs = state_specs
        out_shape = state_shapes
    grid_spec = pltpu.PrefetchScalarGridSpec(
        num_scalar_prefetch=4,
        grid=(nqb,),
        in_specs=in_specs,
        out_specs=out_specs,
        scratch_shapes=[
            pltpu.VMEM((1, width), jnp.float32),
            pltpu.VMEM((1, width), jnp.float32),
            pltpu.VMEM((HD, width), jnp.float32),
        ],
    )
    flops = 4 * rows_here * heads * HD * BLOCK * 8
    cost = pl.CostEstimate(flops=flops, transcendentals=flops // (4 * HD), bytes_accessed=nk * 4 * HD)
    return pl.pallas_call(
        kernel, grid_spec=grid_spec, out_shape=out_shape, cost_estimate=cost
    )(*args)


def attention(q_local, kv_own, kv_rest, doc_start_q, keep_rows, first_row, window, nkb, slot_of):
    rows_here = q_local.shape[0]
    heads = q_local.shape[1] // HD
    first_blk = first_row // BLOCK
    own_rows = kv_own.shape[0] // 16
    tab, cnt_a, cnt_b, ds_blocks = block_tables(
        doc_start_q, keep_rows, first_blk, nkb, window, slot_of, own_rows
    )
    base = jnp.reshape(first_row, (1,)).astype(jnp.int32)
    keep_i = keep_rows.astype(jnp.int32)
    q_t = jnp.transpose(q_local.reshape(rows_here, heads, HD), (1, 0, 2))
    state = attend_call(
        tab, cnt_a, keep_i, base, ds_blocks, q_t, kv_own, None,
        window=window, first=True, last=False, row_base=0,
    )
    return attend_call(
        tab, cnt_b, keep_i, base, ds_blocks, q_t, kv_rest, state,
        window=window, first=False, last=True, row_base=own_rows,
    )


def shift(x, pairs):
    return lax.ppermute(x, "ctx", pairs)


def local(queries, keys, values, doc_ids, block_keep):
    rows_in = keys.shape[0]
    groups = keys.shape[1] // HD
    kv = jnp.concatenate(
        [keys.reshape(rows_in, groups, HD), values.reshape(rows_in, groups, HD)], axis=2
    ).reshape(rows_in, -1)
    kv_local = lax.all_to_all(kv, "kvh", split_axis=1, concat_axis=0, tiled=True)
    query_local = lax.all_to_all(queries, "kvh", split_axis=1, concat_axis=0, tiled=True)
    rows_here = query_local.shape[0]
    per_dev = rows_here // BLOCK
    n_ctx = lax.axis_size("ctx")
    nx = NX
    nz = n_ctx // nx
    reach = n_ctx // 2 // nx
    window = (n_ctx // 2) * rows_here
    ctx = lax.axis_index("ctx")
    first_row = ctx * rows_here
    zq, xq = ctx // nx, ctx % nx

    def x_pairs(d):
        return [(z * nx + x, z * nx + (x + d) % nx) for z in range(nz) for x in range(nx)]

    docs = jnp.arange(N_DOC_IDS, dtype=jnp.int32)
    below = jnp.sum((doc_ids[None, :] < docs[:, None]).astype(jnp.int32), axis=1)
    below_x = jnp.stack(
        [below] + [shift(below, x_pairs(d)) for d in range(1, nx)], axis=0
    ).reshape(-1)
    tail = jnp.zeros((16, kv_local.shape[1]), jnp.float32)
    tail = tail.at[0, :nx * N_DOC_IDS].set((below_x // 32).astype(jnp.float32))
    tail = tail.at[1, :nx * N_DOC_IDS].set((below_x % 32).astype(jnp.float32))
    piece = jnp.concatenate([kv_local, tail.astype(kv_local.dtype)], axis=0)
    prow = piece.shape[0]

    z_step = [(c, (c + nx) % n_ctx) for c in range(n_ctx)]

    col = [piece]
    for _ in range(reach):
        col.append(shift(col[-1], z_step))
    half = (reach + 1) // 2
    early = list(range(1, half + 1))
    late = list(range(half + 1, reach))
    parts, tags = list(col), [(a, 0) for a in range(reach + 1)]

    def add(arr, tag_list):
        parts.append(arr)
        tags.extend(tag_list)

    def blocks(idx):
        return jnp.concatenate([col[a] for a in idx], axis=0) if len(idx) > 1 else col[idx[0]]

    e_plus = shift(blocks(early), x_pairs(1))
    e_minus = shift(blocks(early), x_pairs(nx - 1))
    add(e_plus, [(a, 1) for a in early])
    add(e_minus, [(a, nx - 1) for a in early])
    add(shift(e_plus, x_pairs(1)), [(a, 2) for a in early])
    extra = {d: jnp.where(xq + d < nx, col[0], col[reach]) for d in range(1, nx)}
    l_plus = shift(jnp.concatenate([col[a] for a in late] + [extra[1]], axis=0), x_pairs(1))
    l_minus = shift(jnp.concatenate([col[a] for a in late] + [extra[nx - 1]], axis=0), x_pairs(nx - 1))
    add(l_plus, [(a, 1) for a in late] + [("e", 1)])
    add(l_minus, [(a, nx - 1) for a in late] + [("e", nx - 1)])
    if late:
        relay = l_minus[: prow * len(late)]
        add(shift(relay, x_pairs(nx - 1)), [(a, 2) for a in late])
    add(shift(extra[2], x_pairs(2)), [("e", 2)])
    kv_own = jnp.concatenate(parts[:reach + 3], axis=0)
    kv_rest = jnp.concatenate(parts[reach + 3:], axis=0)

    n_slots = len(tags)
    table = np.zeros((reach + 1, nx), np.int32)
    for s, (a, d) in enumerate(tags):
        if a == "e":
            table[0, d] = s
            table[reach, d] = s
        else:
            table[a, d] = s
    tails = kv_own[: (reach + 1) * prow].reshape(reach + 1, prow, -1)
    tails = tails[:, rows_here:rows_here + 2, :nx * N_DOC_IDS]
    tails = tails.astype(jnp.int32)
    below_col = (tails[:, 0, :] * 32 + tails[:, 1, :]).reshape(reach + 1, nx, N_DOC_IDS)
    a_ids = np.arange(reach + 1)[:, None]
    d_ids = np.arange(nx)[None, :]
    src_ctx = (zq - a_ids) * nx + (xq - d_ids) % nx
    floor_ctx = jnp.maximum(ctx - reach * nx, 0)
    use = (src_ctx >= floor_ctx) & (src_ctx <= ctx)
    below_sum = jnp.sum(jnp.where(use[:, :, None], below_col, 0), axis=(0, 1))
    onehot = doc_ids[:, None] == docs[None, :]
    doc_start = floor_ctx * rows_here + jnp.sum(jnp.where(onehot, below_sum[None, :], 0), axis=1)

    def slot_of(kb):
        cp = kb // per_dev
        a = zq - cp // nx
        d = (xq - cp % nx) % nx
        hit = (a[..., None, None] == np.arange(reach + 1)[:, None]) & (
            d[..., None, None] == np.arange(nx)[None, :]
        )
        slot = jnp.sum(jnp.where(hit, table, 0), axis=(-2, -1))
        return (slot * prow + (kb % per_dev) * BLOCK) // 16

    outputs = attention(
        query_local, kv_own, kv_rest, doc_start.astype(jnp.int32), block_keep, first_row,
        window, n_ctx * per_dev, slot_of,
    )
    return lax.all_to_all(outputs, "kvh", split_axis=0, concat_axis=1, tiled=True)


def solution(mesh):
    return jax.shard_map(
        local,
        mesh=mesh,
        in_specs=(
            P(("ctx", "kvh"), None),
            P(("ctx", "kvh"), None),
            P(("ctx", "kvh"), None),
            P("ctx"),
            P("ctx", None),
        ),
        out_specs=P(("ctx", "kvh"), None),
        check_vma=False,
    )
```

```python
import functools

import numpy as np

import jax
import jax.numpy as jnp
from jax import lax
from jax.experimental import pallas as pl
from jax.experimental.pallas import tpu as pltpu
from jax.sharding import PartitionSpec as P

HD = 128
BLOCK = 128
NX = 4
N_DOC_IDS = 8
KEY_GROUP = 4


def attn_kernel(
    tab_ref, cnt_ref, keep_ref, base_ref,
    qds_ref, q_ref, kv_ref, *rest,
    heads, window, first, last, row_base,
):
    if first:
        state_in = ()
    else:
        state_in, rest = rest[:3], rest[3:]
    outs, (m_sc, l_sc, acc_sc) = rest[:-3], rest[-3:]
    qbl = pl.program_id(0)
    qpos0 = base_ref[0] + qbl * BLOCK
    scale = HD ** (-0.5)
    width = heads * BLOCK
    qpos = qpos0 + lax.broadcasted_iota(jnp.int32, (BLOCK, BLOCK), 1)
    krel = lax.broadcasted_iota(jnp.int32, (BLOCK, BLOCK), 0)
    qds = qds_ref[pl.ds(qbl, 1), :]
    qmat = q_ref[...].reshape(width, HD)

    if first:
        m_sc[...] = jnp.full(m_sc.shape, -1e30, jnp.float32)
        l_sc[...] = jnp.zeros(l_sc.shape, jnp.float32)
        acc_sc[...] = jnp.zeros(acc_sc.shape, jnp.float32)
    else:
        acc_in, m_in, l_in = state_in
        acc_sc[...] = acc_in[...]
        m_sc[...] = m_in[0:1, :]
        l_sc[...] = l_in[0:1, :]

    def mask_of(kb):
        kpos = kb * BLOCK + krel
        keep = keep_ref[qbl, kb]
        earlier = (kpos < qpos) & (qpos - kpos < window) & (kpos >= qds) & (keep != 0)
        return (kpos == qpos) | earlier

    def absorb(ents, masked):
        starts = [pl.multiple_of((rb - row_base) * 16, 16) for _, rb, _, _ in ents]
        k = jnp.concatenate([kv_ref[pl.ds(st, BLOCK), :HD] for st in starts], axis=0)
        v = jnp.concatenate([kv_ref[pl.ds(st, BLOCK), HD:] for st in starts], axis=0)
        s = lax.dot_general(
            k, qmat, (((1,), (1,)), ((), ())), preferred_element_type=jnp.float32
        ) * scale
        if masked:
            allowed = jnp.concatenate(
                [
                    (mask_of(kb) | (kind == 0)) & valid
                    for kb, _, kind, valid in ents
                ],
                axis=0,
            )
            s = jnp.where(jnp.tile(allowed, (1, heads)), s, -1e30)
        m_prev = m_sc[...]
        m_new = jnp.maximum(m_prev, jnp.max(s, axis=0, keepdims=True))
        alpha = jnp.exp(m_prev - m_new)
        p = jnp.exp(s - m_new)
        l_sc[...] = alpha * l_sc[...] + jnp.sum(p, axis=0, keepdims=True)
        acc_sc[...] = acc_sc[...] * alpha + lax.dot_general(
            v, p.astype(jnp.bfloat16), (((0,), (0,)), ((), ())),
            preferred_element_type=jnp.float32,
        )
        m_sc[...] = m_new

    lo = cnt_ref[qbl, 0]
    hi = cnt_ref[qbl, 1]

    def body(i, carry):
        n = lo + KEY_GROUP * i
        ents = []
        any_masked = False
        for j in range(KEY_GROUP):
            e = tab_ref[qbl, jnp.minimum(n + j, hi - 1)]
            valid = n + j < hi
            kind = jnp.where(valid, e >> 20, 1)
            ents.append((e & 255, (e >> 8) & 4095, kind, valid))
            any_masked = any_masked | (kind != 0)

        @pl.when(jnp.logical_not(any_masked))
        def _():
            absorb(ents, False)

        @pl.when(any_masked)
        def _():
            absorb(ents, True)

        return carry

    lax.fori_loop(0, (hi - lo + KEY_GROUP - 1) // KEY_GROUP, body, 0)

    if last:
        (o_ref,) = outs
        out = acc_sc[...] / l_sc[...]
        for h in range(heads):
            o_ref[:, h * HD:(h + 1) * HD] = out[:, h * BLOCK:(h + 1) * BLOCK].T.astype(o_ref.dtype)
    else:
        acc_o, m_o, l_o = outs
        acc_o[...] = acc_sc[...]
        m_o[...] = jnp.broadcast_to(m_sc[...], m_o.shape)
        l_o[...] = jnp.broadcast_to(l_sc[...], l_o.shape)


def block_tables(doc_start_q, keep_rows, first_blk, nkb, window, slot_of, own_rows):
    nqb = keep_rows.shape[0]
    nwin = window // BLOCK
    ds_blocks = doc_start_q.reshape(nqb, BLOCK)
    ds_first = ds_blocks[:, :1]
    ds_last = ds_blocks[:, -1:]
    qb = first_blk + jnp.arange(nqb, dtype=jnp.int32)[:, None]
    kb = jnp.arange(nkb, dtype=jnp.int32)[None, :]
    diag = kb == qb
    inwin = (kb <= qb) & (kb >= qb - nwin)
    keep = keep_rows == 1
    needed = inwin & (diag | (keep & (kb * BLOCK + BLOCK - 1 >= ds_first)))
    full = needed & (~diag) & (kb > qb - nwin) & (kb * BLOCK >= ds_last) & keep
    row_blk = jnp.clip(slot_of(kb), 0, 4095)
    own = row_blk < own_rows
    rank = jnp.where(diag, 0, jnp.where(full, 1, 2))
    sort_key = jnp.where(needed, jnp.where(own, rank, 3 + rank), 6).astype(jnp.int32)
    payload = (kb + 256 * row_blk + (1 << 20) * jnp.where(full, 0, 1)).astype(jnp.int32)
    payload = jnp.broadcast_to(payload, sort_key.shape)
    _, tab = lax.sort((sort_key, payload), dimension=1, is_stable=True, num_keys=1)
    n_own = jnp.sum(needed & own, axis=1).astype(jnp.int32)
    n_all = jnp.sum(needed, axis=1).astype(jnp.int32)
    zero = jnp.zeros_like(n_own)
    return tab, jnp.stack([zero, n_own], 1), jnp.stack([n_own, n_all], 1), ds_blocks


def attend_call(tab, cnt, keep_rows, base, ds_blocks, q_t, kv, state, *, window, first, last, row_base):
    heads, rows_here, _ = q_t.shape
    nqb = rows_here // BLOCK
    width = heads * BLOCK
    nk = kv.shape[0]
    kernel = functools.partial(
        attn_kernel, heads=heads, window=window, first=first, last=last, row_base=row_base
    )
    in_specs = [
        pl.BlockSpec((nqb, BLOCK), lambda i, *_: (0, 0)),
        pl.BlockSpec((heads, BLOCK, HD), lambda i, *_: (0, i, 0)),
        pl.BlockSpec((nk, 2 * HD), lambda i, *_: (0, 0)),
    ]
    state_specs = [
        pl.BlockSpec((HD, width), lambda i, *_: (i, 0)),
        pl.BlockSpec((8, width), lambda i, *_: (i, 0)),
        pl.BlockSpec((8, width), lambda i, *_: (i, 0)),
    ]
    state_shapes = [
        jax.ShapeDtypeStruct((nqb * HD, width), jnp.float32),
        jax.ShapeDtypeStruct((nqb * 8, width), jnp.float32),
        jax.ShapeDtypeStruct((nqb * 8, width), jnp.float32),
    ]
    args = [tab, cnt, keep_rows, base, ds_blocks, q_t, kv]
    if not first:
        in_specs += state_specs
        args += list(state)
    if last:
        out_specs = pl.BlockSpec((BLOCK, width), lambda i, *_: (i, 0))
        out_shape = jax.ShapeDtypeStruct((rows_here, width), q_t.dtype)
    else:
        out_specs = state_specs
        out_shape = state_shapes
    grid_spec = pltpu.PrefetchScalarGridSpec(
        num_scalar_prefetch=4,
        grid=(nqb,),
        in_specs=in_specs,
        out_specs=out_specs,
        scratch_shapes=[
            pltpu.VMEM((1, width), jnp.float32),
            pltpu.VMEM((1, width), jnp.float32),
            pltpu.VMEM((HD, width), jnp.float32),
        ],
    )
    flops = 4 * rows_here * heads * HD * BLOCK * 8
    cost = pl.CostEstimate(flops=flops, transcendentals=flops // (4 * HD), bytes_accessed=nk * 4 * HD)
    return pl.pallas_call(
        kernel, grid_spec=grid_spec, out_shape=out_shape, cost_estimate=cost
    )(*args)


def attention(q_local, kv_own, kv_rest, doc_start_q, keep_rows, first_row, window, nkb, slot_of):
    rows_here = q_local.shape[0]
    heads = q_local.shape[1] // HD
    first_blk = first_row // BLOCK
    own_rows = kv_own.shape[0] // 16
    tab, cnt_a, cnt_b, ds_blocks = block_tables(
        doc_start_q, keep_rows, first_blk, nkb, window, slot_of, own_rows
    )
    base = jnp.reshape(first_row, (1,)).astype(jnp.int32)
    keep_i = keep_rows.astype(jnp.int32)
    q_t = jnp.transpose(q_local.reshape(rows_here, heads, HD), (1, 0, 2))
    state = attend_call(
        tab, cnt_a, keep_i, base, ds_blocks, q_t, kv_own, None,
        window=window, first=True, last=False, row_base=0,
    )
    return attend_call(
        tab, cnt_b, keep_i, base, ds_blocks, q_t, kv_rest, state,
        window=window, first=False, last=True, row_base=own_rows,
    )


def shift(x, pairs):
    return lax.ppermute(x, "ctx", pairs)


def local(queries, keys, values, doc_ids, block_keep):
    rows_in = keys.shape[0]
    groups = keys.shape[1] // HD
    kv = jnp.concatenate(
        [keys.reshape(rows_in, groups, HD), values.reshape(rows_in, groups, HD)], axis=2
    ).reshape(rows_in, -1)
    kv_local = lax.all_to_all(kv, "kvh", split_axis=1, concat_axis=0, tiled=True)
    query_local = lax.all_to_all(queries, "kvh", split_axis=1, concat_axis=0, tiled=True)
    rows_here = query_local.shape[0]
    per_dev = rows_here // BLOCK
    n_ctx = lax.axis_size("ctx")
    nx = NX
    nz = n_ctx // nx
    reach = n_ctx // 2 // nx
    window = (n_ctx // 2) * rows_here
    ctx = lax.axis_index("ctx")
    first_row = ctx * rows_here
    zq, xq = ctx // nx, ctx % nx

    def x_pairs(d):
        return [(z * nx + x, z * nx + (x + d) % nx) for z in range(nz) for x in range(nx)]

    docs = jnp.arange(N_DOC_IDS, dtype=jnp.int32)
    below = jnp.sum((doc_ids[None, :] < docs[:, None]).astype(jnp.int32), axis=1)
    below_x = jnp.stack(
        [below] + [shift(below, x_pairs(d)) for d in range(1, nx)], axis=0
    ).reshape(-1)
    tail = jnp.zeros((16, kv_local.shape[1]), jnp.float32)
    tail = tail.at[0, :nx * N_DOC_IDS].set((below_x // 32).astype(jnp.float32))
    tail = tail.at[1, :nx * N_DOC_IDS].set((below_x % 32).astype(jnp.float32))
    piece = jnp.concatenate([kv_local, tail.astype(kv_local.dtype)], axis=0)
    prow = piece.shape[0]

    z_step = [(c, (c + nx) % n_ctx) for c in range(n_ctx)]

    col = [piece]
    for _ in range(reach):
        col.append(shift(col[-1], z_step))
    half = (reach + 1) // 2
    early = list(range(1, half + 1))
    late = list(range(half + 1, reach))
    parts, tags = list(col), [(a, 0) for a in range(reach + 1)]

    def add(arr, tag_list):
        parts.append(arr)
        tags.extend(tag_list)

    def blocks(idx):
        return jnp.concatenate([col[a] for a in idx], axis=0) if len(idx) > 1 else col[idx[0]]

    e_plus = shift(blocks(early), x_pairs(1))
    e_minus = shift(blocks(early), x_pairs(nx - 1))
    add(e_plus, [(a, 1) for a in early])
    add(e_minus, [(a, nx - 1) for a in early])
    add(shift(e_plus, x_pairs(1)), [(a, 2) for a in early])
    extra = {d: jnp.where(xq + d < nx, col[0], col[reach]) for d in range(1, nx)}
    l_plus = shift(jnp.concatenate([col[a] for a in late] + [extra[1]], axis=0), x_pairs(1))
    l_minus = shift(jnp.concatenate([col[a] for a in late] + [extra[nx - 1]], axis=0), x_pairs(nx - 1))
    add(l_plus, [(a, 1) for a in late] + [("e", 1)])
    add(l_minus, [(a, nx - 1) for a in late] + [("e", nx - 1)])
    if late:
        relay = l_minus[: prow * len(late)]
        add(shift(relay, x_pairs(nx - 1)), [(a, 2) for a in late])
    add(shift(extra[2], x_pairs(2)), [("e", 2)])
    kv_own = jnp.concatenate(parts[:reach + 4], axis=0)
    kv_rest = jnp.concatenate(parts[reach + 4:], axis=0)

    n_slots = len(tags)
    table = np.zeros((reach + 1, nx), np.int32)
    for s, (a, d) in enumerate(tags):
        if a == "e":
            table[0, d] = s
            table[reach, d] = s
        else:
            table[a, d] = s
    tails = kv_own[: (reach + 1) * prow].reshape(reach + 1, prow, -1)
    tails = tails[:, rows_here:rows_here + 2, :nx * N_DOC_IDS]
    tails = tails.astype(jnp.int32)
    below_col = (tails[:, 0, :] * 32 + tails[:, 1, :]).reshape(reach + 1, nx, N_DOC_IDS)
    a_ids = np.arange(reach + 1)[:, None]
    d_ids = np.arange(nx)[None, :]
    src_ctx = (zq - a_ids) * nx + (xq - d_ids) % nx
    floor_ctx = jnp.maximum(ctx - reach * nx, 0)
    use = (src_ctx >= floor_ctx) & (src_ctx <= ctx)
    below_sum = jnp.sum(jnp.where(use[:, :, None], below_col, 0), axis=(0, 1))
    onehot = doc_ids[:, None] == docs[None, :]
    doc_start = floor_ctx * rows_here + jnp.sum(jnp.where(onehot, below_sum[None, :], 0), axis=1)

    def slot_of(kb):
        cp = kb // per_dev
        a = zq - cp // nx
        d = (xq - cp % nx) % nx
        hit = (a[..., None, None] == np.arange(reach + 1)[:, None]) & (
            d[..., None, None] == np.arange(nx)[None, :]
        )
        slot = jnp.sum(jnp.where(hit, table, 0), axis=(-2, -1))
        return (slot * prow + (kb % per_dev) * BLOCK) // 16

    outputs = attention(
        query_local, kv_own, kv_rest, doc_start.astype(jnp.int32), block_keep, first_row,
        window, n_ctx * per_dev, slot_of,
    )
    return lax.all_to_all(outputs, "kvh", split_axis=0, concat_axis=1, tiled=True)


def solution(mesh):
    return jax.shard_map(
        local,
        mesh=mesh,
        in_specs=(
            P(("ctx", "kvh"), None),
            P(("ctx", "kvh"), None),
            P(("ctx", "kvh"), None),
            P("ctx"),
            P("ctx", None),
        ),
        out_specs=P(("ctx", "kvh"), None),
        check_vma=False,
    )
```

```python
import functools

import numpy as np

import jax
import jax.numpy as jnp
from jax import lax
from jax.experimental import pallas as pl
from jax.experimental.pallas import tpu as pltpu
from jax.sharding import PartitionSpec as P

HD = 128
BLOCK = 128
NX = 4
N_DOC_IDS = 8
KEY_GROUP = 4


def attn_kernel(
    tab_ref, cnt_ref, keep_ref, base_ref,
    qds_ref, q_ref, kv_ref, *rest,
    heads, window, first, last, row_base,
):
    if first:
        state_in = ()
    else:
        state_in, rest = rest[:3], rest[3:]
    outs, (m_sc, l_sc, acc_sc) = rest[:-3], rest[-3:]
    qbl = pl.program_id(0)
    qpos0 = base_ref[0] + qbl * BLOCK
    scale = HD ** (-0.5)
    width = heads * BLOCK
    qpos = qpos0 + lax.broadcasted_iota(jnp.int32, (BLOCK, BLOCK), 1)
    krel = lax.broadcasted_iota(jnp.int32, (BLOCK, BLOCK), 0)
    qds = qds_ref[pl.ds(qbl, 1), :]
    qmat = q_ref[...].reshape(width, HD)

    if first:
        m_sc[...] = jnp.full(m_sc.shape, -1e30, jnp.float32)
        l_sc[...] = jnp.zeros(l_sc.shape, jnp.float32)
        acc_sc[...] = jnp.zeros(acc_sc.shape, jnp.float32)
    else:
        acc_in, m_in, l_in = state_in
        acc_sc[...] = acc_in[...]
        m_sc[...] = m_in[0:1, :]
        l_sc[...] = l_in[0:1, :]

    def mask_of(kb):
        kpos = kb * BLOCK + krel
        keep = keep_ref[qbl, kb]
        earlier = (kpos < qpos) & (qpos - kpos < window) & (kpos >= qds) & (keep != 0)
        return (kpos == qpos) | earlier

    def absorb(ents, masked):
        starts = [pl.multiple_of((rb - row_base) * 16, 16) for _, rb, _, _ in ents]
        k = jnp.concatenate([kv_ref[pl.ds(st, BLOCK), :HD] for st in starts], axis=0)
        v = jnp.concatenate([kv_ref[pl.ds(st, BLOCK), HD:] for st in starts], axis=0)
        s = lax.dot_general(
            k, qmat, (((1,), (1,)), ((), ())), preferred_element_type=jnp.float32
        ) * scale
        if masked:
            allowed = jnp.concatenate(
                [
                    (mask_of(kb) | (kind == 0)) & valid
                    for kb, _, kind, valid in ents
                ],
                axis=0,
            )
            s = jnp.where(jnp.tile(allowed, (1, heads)), s, -1e30)
        m_prev = m_sc[...]
        m_new = jnp.maximum(m_prev, jnp.max(s, axis=0, keepdims=True))
        alpha = jnp.exp(m_prev - m_new)
        p = jnp.exp(s - m_new)
        l_sc[...] = alpha * l_sc[...] + jnp.sum(p, axis=0, keepdims=True)
        acc_sc[...] = acc_sc[...] * alpha + lax.dot_general(
            v, p.astype(jnp.bfloat16), (((0,), (0,)), ((), ())),
            preferred_element_type=jnp.float32,
        )
        m_sc[...] = m_new

    lo = cnt_ref[qbl, 0]
    hi = cnt_ref[qbl, 1]

    def body(i, carry):
        n = lo + KEY_GROUP * i
        ents = []
        any_masked = False
        for j in range(KEY_GROUP):
            e = tab_ref[qbl, jnp.minimum(n + j, hi - 1)]
            valid = n + j < hi
            kind = jnp.where(valid, e >> 20, 1)
            ents.append((e & 255, (e >> 8) & 4095, kind, valid))
            any_masked = any_masked | (kind != 0)

        @pl.when(jnp.logical_not(any_masked))
        def _():
            absorb(ents, False)

        @pl.when(any_masked)
        def _():
            absorb(ents, True)

        return carry

    lax.fori_loop(0, (hi - lo + KEY_GROUP - 1) // KEY_GROUP, body, 0)

    if last:
        (o_ref,) = outs
        out = acc_sc[...] / l_sc[...]
        for h in range(heads):
            o_ref[:, h * HD:(h + 1) * HD] = out[:, h * BLOCK:(h + 1) * BLOCK].T.astype(o_ref.dtype)
    else:
        acc_o, m_o, l_o = outs
        acc_o[...] = acc_sc[...]
        m_o[...] = jnp.broadcast_to(m_sc[...], m_o.shape)
        l_o[...] = jnp.broadcast_to(l_sc[...], l_o.shape)


def block_tables(doc_start_q, keep_rows, first_blk, nkb, window, slot_of, own_rows):
    nqb = keep_rows.shape[0]
    nwin = window // BLOCK
    ds_blocks = doc_start_q.reshape(nqb, BLOCK)
    ds_first = ds_blocks[:, :1]
    ds_last = ds_blocks[:, -1:]
    qb = first_blk + jnp.arange(nqb, dtype=jnp.int32)[:, None]
    kb = jnp.arange(nkb, dtype=jnp.int32)[None, :]
    diag = kb == qb
    inwin = (kb <= qb) & (kb >= qb - nwin)
    keep = keep_rows == 1
    needed = inwin & (diag | (keep & (kb * BLOCK + BLOCK - 1 >= ds_first)))
    full = needed & (~diag) & (kb > qb - nwin) & (kb * BLOCK >= ds_last) & keep
    row_blk = jnp.clip(slot_of(kb), 0, 4095)
    own = row_blk < own_rows
    rank = jnp.where(diag, 0, jnp.where(full, 1, 2))
    sort_key = jnp.where(needed, jnp.where(own, rank, 3 + rank), 6).astype(jnp.int32)
    payload = (kb + 256 * row_blk + (1 << 20) * jnp.where(full, 0, 1)).astype(jnp.int32)
    payload = jnp.broadcast_to(payload, sort_key.shape)
    _, tab = lax.sort((sort_key, payload), dimension=1, is_stable=True, num_keys=1)
    n_own = jnp.sum(needed & own, axis=1).astype(jnp.int32)
    n_all = jnp.sum(needed, axis=1).astype(jnp.int32)
    zero = jnp.zeros_like(n_own)
    return tab, jnp.stack([zero, n_own], 1), jnp.stack([n_own, n_all], 1), ds_blocks


def attend_call(tab, cnt, keep_rows, base, ds_blocks, q_t, kv, state, *, window, first, last, row_base):
    heads, rows_here, _ = q_t.shape
    nqb = rows_here // BLOCK
    width = heads * BLOCK
    nk = kv.shape[0]
    kernel = functools.partial(
        attn_kernel, heads=heads, window=window, first=first, last=last, row_base=row_base
    )
    in_specs = [
        pl.BlockSpec((nqb, BLOCK), lambda i, *_: (0, 0)),
        pl.BlockSpec((heads, BLOCK, HD), lambda i, *_: (0, i, 0)),
        pl.BlockSpec((nk, 2 * HD), lambda i, *_: (0, 0)),
    ]
    state_specs = [
        pl.BlockSpec((HD, width), lambda i, *_: (i, 0)),
        pl.BlockSpec((8, width), lambda i, *_: (i, 0)),
        pl.BlockSpec((8, width), lambda i, *_: (i, 0)),
    ]
    state_shapes = [
        jax.ShapeDtypeStruct((nqb * HD, width), jnp.float32),
        jax.ShapeDtypeStruct((nqb * 8, width), jnp.float32),
        jax.ShapeDtypeStruct((nqb * 8, width), jnp.float32),
    ]
    args = [tab, cnt, keep_rows, base, ds_blocks, q_t, kv]
    if not first:
        in_specs += state_specs
        args += list(state)
    if last:
        out_specs = pl.BlockSpec((BLOCK, width), lambda i, *_: (i, 0))
        out_shape = jax.ShapeDtypeStruct((rows_here, width), q_t.dtype)
    else:
        out_specs = state_specs
        out_shape = state_shapes
    grid_spec = pltpu.PrefetchScalarGridSpec(
        num_scalar_prefetch=4,
        grid=(nqb,),
        in_specs=in_specs,
        out_specs=out_specs,
        scratch_shapes=[
            pltpu.VMEM((1, width), jnp.float32),
            pltpu.VMEM((1, width), jnp.float32),
            pltpu.VMEM((HD, width), jnp.float32),
        ],
    )
    flops = 4 * rows_here * heads * HD * BLOCK * 8
    cost = pl.CostEstimate(flops=flops, transcendentals=flops // (4 * HD), bytes_accessed=nk * 4 * HD)
    return pl.pallas_call(
        kernel, grid_spec=grid_spec, out_shape=out_shape, cost_estimate=cost
    )(*args)


def attention(q_local, kv_own, kv_rest, doc_start_q, keep_rows, first_row, window, nkb, slot_of):
    rows_here = q_local.shape[0]
    heads = q_local.shape[1] // HD
    first_blk = first_row // BLOCK
    own_rows = kv_own.shape[0] // 16
    tab, cnt_a, cnt_b, ds_blocks = block_tables(
        doc_start_q, keep_rows, first_blk, nkb, window, slot_of, own_rows
    )
    base = jnp.reshape(first_row, (1,)).astype(jnp.int32)
    keep_i = keep_rows.astype(jnp.int32)
    q_t = jnp.transpose(q_local.reshape(rows_here, heads, HD), (1, 0, 2))
    state = attend_call(
        tab, cnt_a, keep_i, base, ds_blocks, q_t, kv_own, None,
        window=window, first=True, last=False, row_base=0,
    )
    return attend_call(
        tab, cnt_b, keep_i, base, ds_blocks, q_t, kv_rest, state,
        window=window, first=False, last=True, row_base=own_rows,
    )


def shift(x, pairs):
    return lax.ppermute(x, "ctx", pairs)


def local(queries, keys, values, doc_ids, block_keep):
    rows_in = keys.shape[0]
    groups = keys.shape[1] // HD
    kv = jnp.concatenate(
        [keys.reshape(rows_in, groups, HD), values.reshape(rows_in, groups, HD)], axis=2
    ).reshape(rows_in, -1)
    kv_local = lax.all_to_all(kv, "kvh", split_axis=1, concat_axis=0, tiled=True)
    query_local = lax.all_to_all(queries, "kvh", split_axis=1, concat_axis=0, tiled=True)
    rows_here = query_local.shape[0]
    per_dev = rows_here // BLOCK
    n_ctx = lax.axis_size("ctx")
    nx = NX
    nz = n_ctx // nx
    reach = n_ctx // 2 // nx
    window = (n_ctx // 2) * rows_here
    ctx = lax.axis_index("ctx")
    first_row = ctx * rows_here
    zq, xq = ctx // nx, ctx % nx

    def x_pairs(d):
        return [(z * nx + x, z * nx + (x + d) % nx) for z in range(nz) for x in range(nx)]

    docs = jnp.arange(N_DOC_IDS, dtype=jnp.int32)
    below = jnp.sum((doc_ids[None, :] < docs[:, None]).astype(jnp.int32), axis=1)
    below_x = jnp.stack(
        [below] + [shift(below, x_pairs(d)) for d in range(1, nx)], axis=0
    ).reshape(-1)
    tail = jnp.zeros((16, kv_local.shape[1]), jnp.float32)
    tail = tail.at[0, :nx * N_DOC_IDS].set((below_x // 32).astype(jnp.float32))
    tail = tail.at[1, :nx * N_DOC_IDS].set((below_x % 32).astype(jnp.float32))
    piece = jnp.concatenate([kv_local, tail.astype(kv_local.dtype)], axis=0)
    prow = piece.shape[0]

    z_step = [(c, (c + nx) % n_ctx) for c in range(n_ctx)]

    col = [piece]
    for _ in range(reach):
        col.append(shift(col[-1], z_step))
    half = (reach + 1) // 2
    early = list(range(1, half + 1))
    late = list(range(half + 1, reach))
    parts, tags = list(col), [(a, 0) for a in range(reach + 1)]

    def add(arr, tag_list):
        parts.append(arr)
        tags.extend(tag_list)

    def blocks(idx):
        return jnp.concatenate([col[a] for a in idx], axis=0) if len(idx) > 1 else col[idx[0]]

    e_plus = shift(blocks(early), x_pairs(1))
    e_minus = shift(blocks(early), x_pairs(nx - 1))
    add(e_plus, [(a, 1) for a in early])
    add(e_minus, [(a, nx - 1) for a in early])
    add(shift(e_plus, x_pairs(1)), [(a, 2) for a in early])
    extra = {d: jnp.where(xq + d < nx, col[0], col[reach]) for d in range(1, nx)}
    l_plus = shift(jnp.concatenate([col[a] for a in late] + [extra[1]], axis=0), x_pairs(1))
    l_minus = shift(jnp.concatenate([col[a] for a in late] + [extra[nx - 1]], axis=0), x_pairs(nx - 1))
    add(l_plus, [(a, 1) for a in late] + [("e", 1)])
    add(l_minus, [(a, nx - 1) for a in late] + [("e", nx - 1)])
    if late:
        add(shift(blocks(late), x_pairs(2)), [(a, 2) for a in late])
    add(shift(extra[2], x_pairs(2)), [("e", 2)])
    kv_own = jnp.concatenate(parts[:reach + 3], axis=0)
    kv_rest = jnp.concatenate(parts[reach + 3:], axis=0)

    n_slots = len(tags)
    table = np.zeros((reach + 1, nx), np.int32)
    for s, (a, d) in enumerate(tags):
        if a == "e":
            table[0, d] = s
            table[reach, d] = s
        else:
            table[a, d] = s
    tails = kv_own[: (reach + 1) * prow].reshape(reach + 1, prow, -1)
    tails = tails[:, rows_here:rows_here + 2, :nx * N_DOC_IDS]
    tails = tails.astype(jnp.int32)
    below_col = (tails[:, 0, :] * 32 + tails[:, 1, :]).reshape(reach + 1, nx, N_DOC_IDS)
    a_ids = np.arange(reach + 1)[:, None]
    d_ids = np.arange(nx)[None, :]
    src_ctx = (zq - a_ids) * nx + (xq - d_ids) % nx
    floor_ctx = jnp.maximum(ctx - reach * nx, 0)
    use = (src_ctx >= floor_ctx) & (src_ctx <= ctx)
    below_sum = jnp.sum(jnp.where(use[:, :, None], below_col, 0), axis=(0, 1))
    onehot = doc_ids[:, None] == docs[None, :]
    doc_start = floor_ctx * rows_here + jnp.sum(jnp.where(onehot, below_sum[None, :], 0), axis=1)

    def slot_of(kb):
        cp = kb // per_dev
        a = zq - cp // nx
        d = (xq - cp % nx) % nx
        hit = (a[..., None, None] == np.arange(reach + 1)[:, None]) & (
            d[..., None, None] == np.arange(nx)[None, :]
        )
        slot = jnp.sum(jnp.where(hit, table, 0), axis=(-2, -1))
        return (slot * prow + (kb % per_dev) * BLOCK) // 16

    outputs = attention(
        query_local, kv_own, kv_rest, doc_start.astype(jnp.int32), block_keep, first_row,
        window, n_ctx * per_dev, slot_of,
    )
    return lax.all_to_all(outputs, "kvh", split_axis=0, concat_axis=1, tiled=True)


def solution(mesh):
    return jax.shard_map(
        local,
        mesh=mesh,
        in_specs=(
            P(("ctx", "kvh"), None),
            P(("ctx", "kvh"), None),
            P(("ctx", "kvh"), None),
            P("ctx"),
            P("ctx", None),
        ),
        out_specs=P(("ctx", "kvh"), None),
        check_vma=False,
    )
```

```python
import functools

import numpy as np

import jax
import jax.numpy as jnp
from jax import lax
from jax.experimental import pallas as pl
from jax.experimental.pallas import tpu as pltpu
from jax.sharding import PartitionSpec as P

HD = 128
BLOCK = 128
NX = 4
N_DOC_IDS = 8
KEY_GROUP = 4


def attn_kernel(
    tab_ref, cnt_ref, keep_ref, base_ref,
    qds_ref, q_ref, kv_ref, *rest,
    heads, window, first, last, row_base,
):
    if first:
        state_in = ()
    else:
        state_in, rest = rest[:3], rest[3:]
    outs, (m_sc, l_sc, acc_sc) = rest[:-3], rest[-3:]
    qbl = pl.program_id(0)
    qpos0 = base_ref[0] + qbl * BLOCK
    scale = HD ** (-0.5)
    width = heads * BLOCK
    qpos = qpos0 + lax.broadcasted_iota(jnp.int32, (BLOCK, BLOCK), 1)
    krel = lax.broadcasted_iota(jnp.int32, (BLOCK, BLOCK), 0)
    qds = qds_ref[pl.ds(qbl, 1), :]
    qmat = q_ref[...].reshape(width, HD)

    if first:
        m_sc[...] = jnp.full(m_sc.shape, -1e30, jnp.float32)
        l_sc[...] = jnp.zeros(l_sc.shape, jnp.float32)
        acc_sc[...] = jnp.zeros(acc_sc.shape, jnp.float32)
    else:
        acc_in, m_in, l_in = state_in
        acc_sc[...] = acc_in[...]
        m_sc[...] = m_in[0:1, :]
        l_sc[...] = l_in[0:1, :]

    def mask_of(kb):
        kpos = kb * BLOCK + krel
        keep = keep_ref[qbl, kb]
        earlier = (kpos < qpos) & (qpos - kpos < window) & (kpos >= qds) & (keep != 0)
        return (kpos == qpos) | earlier

    def absorb(ents, masked):
        starts = [pl.multiple_of((rb - row_base) * 16, 16) for _, rb, _, _ in ents]
        k = jnp.concatenate([kv_ref[pl.ds(st, BLOCK), :HD] for st in starts], axis=0)
        v = jnp.concatenate([kv_ref[pl.ds(st, BLOCK), HD:] for st in starts], axis=0)
        s = lax.dot_general(
            k, qmat, (((1,), (1,)), ((), ())), preferred_element_type=jnp.float32
        ) * scale
        if masked:
            allowed = jnp.concatenate(
                [
                    (mask_of(kb) | (kind == 0)) & valid
                    for kb, _, kind, valid in ents
                ],
                axis=0,
            )
            s = jnp.where(jnp.tile(allowed, (1, heads)), s, -1e30)
        m_prev = m_sc[...]
        m_new = jnp.maximum(m_prev, jnp.max(s, axis=0, keepdims=True))
        alpha = jnp.exp(m_prev - m_new)
        p = jnp.exp(s - m_new)
        l_sc[...] = alpha * l_sc[...] + jnp.sum(p, axis=0, keepdims=True)
        acc_sc[...] = acc_sc[...] * alpha + lax.dot_general(
            v, p.astype(jnp.bfloat16), (((0,), (0,)), ((), ())),
            preferred_element_type=jnp.float32,
        )
        m_sc[...] = m_new

    lo = cnt_ref[qbl, 0]
    hi = cnt_ref[qbl, 1]

    def body(i, carry):
        n = lo + KEY_GROUP * i
        ents = []
        any_masked = False
        for j in range(KEY_GROUP):
            e = tab_ref[qbl, jnp.minimum(n + j, hi - 1)]
            valid = n + j < hi
            kind = jnp.where(valid, e >> 20, 1)
            ents.append((e & 255, (e >> 8) & 4095, kind, valid))
            any_masked = any_masked | (kind != 0)

        @pl.when(jnp.logical_not(any_masked))
        def _():
            absorb(ents, False)

        @pl.when(any_masked)
        def _():
            absorb(ents, True)

        return carry

    lax.fori_loop(0, (hi - lo + KEY_GROUP - 1) // KEY_GROUP, body, 0)

    if last:
        (o_ref,) = outs
        out = acc_sc[...] / l_sc[...]
        for h in range(heads):
            o_ref[:, h * HD:(h + 1) * HD] = out[:, h * BLOCK:(h + 1) * BLOCK].T.astype(o_ref.dtype)
    else:
        acc_o, m_o, l_o = outs
        acc_o[...] = acc_sc[...]
        m_o[...] = jnp.broadcast_to(m_sc[...], m_o.shape)
        l_o[...] = jnp.broadcast_to(l_sc[...], l_o.shape)


def block_tables(doc_start_q, keep_rows, first_blk, nkb, window, slot_of, own_rows):
    nqb = keep_rows.shape[0]
    nwin = window // BLOCK
    ds_blocks = doc_start_q.reshape(nqb, BLOCK)
    ds_first = ds_blocks[:, :1]
    ds_last = ds_blocks[:, -1:]
    qb = first_blk + jnp.arange(nqb, dtype=jnp.int32)[:, None]
    kb = jnp.arange(nkb, dtype=jnp.int32)[None, :]
    diag = kb == qb
    inwin = (kb <= qb) & (kb >= qb - nwin)
    keep = keep_rows == 1
    needed = inwin & (diag | (keep & (kb * BLOCK + BLOCK - 1 >= ds_first)))
    full = needed & (~diag) & (kb > qb - nwin) & (kb * BLOCK >= ds_last) & keep
    row_blk = jnp.clip(slot_of(kb), 0, 4095)
    own = row_blk < own_rows
    rank = jnp.where(diag, 0, jnp.where(full, 1, 2))
    sort_key = jnp.where(needed, jnp.where(own, rank, 3 + rank), 6).astype(jnp.int32)
    payload = (kb + 256 * row_blk + (1 << 20) * jnp.where(full, 0, 1)).astype(jnp.int32)
    payload = jnp.broadcast_to(payload, sort_key.shape)
    _, tab = lax.sort((sort_key, payload), dimension=1, is_stable=True, num_keys=1)
    n_own = jnp.sum(needed & own, axis=1).astype(jnp.int32)
    n_all = jnp.sum(needed, axis=1).astype(jnp.int32)
    zero = jnp.zeros_like(n_own)
    return tab, jnp.stack([zero, n_own], 1), jnp.stack([n_own, n_all], 1), ds_blocks


def attend_call(tab, cnt, keep_rows, base, ds_blocks, q_t, kv, state, *, window, first, last, row_base):
    heads, rows_here, _ = q_t.shape
    nqb = rows_here // BLOCK
    width = heads * BLOCK
    nk = kv.shape[0]
    kernel = functools.partial(
        attn_kernel, heads=heads, window=window, first=first, last=last, row_base=row_base
    )
    in_specs = [
        pl.BlockSpec((nqb, BLOCK), lambda i, *_: (0, 0)),
        pl.BlockSpec((heads, BLOCK, HD), lambda i, *_: (0, i, 0)),
        pl.BlockSpec((nk, 2 * HD), lambda i, *_: (0, 0)),
    ]
    state_specs = [
        pl.BlockSpec((HD, width), lambda i, *_: (i, 0)),
        pl.BlockSpec((8, width), lambda i, *_: (i, 0)),
        pl.BlockSpec((8, width), lambda i, *_: (i, 0)),
    ]
    state_shapes = [
        jax.ShapeDtypeStruct((nqb * HD, width), jnp.float32),
        jax.ShapeDtypeStruct((nqb * 8, width), jnp.float32),
        jax.ShapeDtypeStruct((nqb * 8, width), jnp.float32),
    ]
    args = [tab, cnt, keep_rows, base, ds_blocks, q_t, kv]
    if not first:
        in_specs += state_specs
        args += list(state)
    if last:
        out_specs = pl.BlockSpec((BLOCK, width), lambda i, *_: (i, 0))
        out_shape = jax.ShapeDtypeStruct((rows_here, width), q_t.dtype)
    else:
        out_specs = state_specs
        out_shape = state_shapes
    grid_spec = pltpu.PrefetchScalarGridSpec(
        num_scalar_prefetch=4,
        grid=(nqb,),
        in_specs=in_specs,
        out_specs=out_specs,
        scratch_shapes=[
            pltpu.VMEM((1, width), jnp.float32),
            pltpu.VMEM((1, width), jnp.float32),
            pltpu.VMEM((HD, width), jnp.float32),
        ],
    )
    flops = 4 * rows_here * heads * HD * BLOCK * 8
    cost = pl.CostEstimate(flops=flops, transcendentals=flops // (4 * HD), bytes_accessed=nk * 4 * HD)
    return pl.pallas_call(
        kernel, grid_spec=grid_spec, out_shape=out_shape, cost_estimate=cost
    )(*args)


def attention(q_local, kv_own, kv_rest, doc_start_q, keep_rows, first_row, window, nkb, slot_of):
    rows_here = q_local.shape[0]
    heads = q_local.shape[1] // HD
    first_blk = first_row // BLOCK
    own_rows = kv_own.shape[0] // 16
    tab, cnt_a, cnt_b, ds_blocks = block_tables(
        doc_start_q, keep_rows, first_blk, nkb, window, slot_of, own_rows
    )
    base = jnp.reshape(first_row, (1,)).astype(jnp.int32)
    keep_i = keep_rows.astype(jnp.int32)
    q_t = jnp.transpose(q_local.reshape(rows_here, heads, HD), (1, 0, 2))
    state = attend_call(
        tab, cnt_a, keep_i, base, ds_blocks, q_t, kv_own, None,
        window=window, first=True, last=False, row_base=0,
    )
    return attend_call(
        tab, cnt_b, keep_i, base, ds_blocks, q_t, kv_rest, state,
        window=window, first=False, last=True, row_base=own_rows,
    )


def shift(x, pairs):
    return lax.ppermute(x, "ctx", pairs)


def local(queries, keys, values, doc_ids, block_keep):
    rows_in = keys.shape[0]
    groups = keys.shape[1] // HD
    kv = jnp.concatenate(
        [keys.reshape(rows_in, groups, HD), values.reshape(rows_in, groups, HD)], axis=2
    ).reshape(rows_in, -1)
    kv_local = lax.all_to_all(kv, "kvh", split_axis=1, concat_axis=0, tiled=True)
    rows_here = kv_local.shape[0]
    per_dev = rows_here // BLOCK
    n_ctx = lax.axis_size("ctx")
    nx = NX
    nz = n_ctx // nx
    reach = n_ctx // 2 // nx
    window = (n_ctx // 2) * rows_here
    ctx = lax.axis_index("ctx")
    first_row = ctx * rows_here
    zq, xq = ctx // nx, ctx % nx

    def x_pairs(d):
        return [(z * nx + x, z * nx + (x + d) % nx) for z in range(nz) for x in range(nx)]

    docs = jnp.arange(N_DOC_IDS, dtype=jnp.int32)
    below = jnp.sum((doc_ids[None, :] < docs[:, None]).astype(jnp.int32), axis=1)
    below_x = jnp.stack(
        [below] + [shift(below, x_pairs(d)) for d in range(1, nx)], axis=0
    ).reshape(-1)
    tail = jnp.zeros((16, kv_local.shape[1]), jnp.float32)
    tail = tail.at[0, :nx * N_DOC_IDS].set((below_x // 32).astype(jnp.float32))
    tail = tail.at[1, :nx * N_DOC_IDS].set((below_x % 32).astype(jnp.float32))
    piece = jnp.concatenate([kv_local, tail.astype(kv_local.dtype)], axis=0)
    prow = piece.shape[0]

    z_step = [(c, (c + nx) % n_ctx) for c in range(n_ctx)]

    col = [piece]
    for _ in range(reach):
        col.append(shift(col[-1], z_step))
    queries, _ = lax.optimization_barrier((queries, col[1]))
    query_local = lax.all_to_all(queries, "kvh", split_axis=1, concat_axis=0, tiled=True)
    half = (reach + 1) // 2
    early = list(range(1, half + 1))
    late = list(range(half + 1, reach))
    parts, tags = list(col), [(a, 0) for a in range(reach + 1)]

    def add(arr, tag_list):
        parts.append(arr)
        tags.extend(tag_list)

    def blocks(idx):
        return jnp.concatenate([col[a] for a in idx], axis=0) if len(idx) > 1 else col[idx[0]]

    e_plus = shift(blocks(early), x_pairs(1))
    e_minus = shift(blocks(early), x_pairs(nx - 1))
    add(e_plus, [(a, 1) for a in early])
    add(e_minus, [(a, nx - 1) for a in early])
    add(shift(e_plus, x_pairs(1)), [(a, 2) for a in early])
    extra = {d: jnp.where(xq + d < nx, col[0], col[reach]) for d in range(1, nx)}
    l_plus = shift(jnp.concatenate([col[a] for a in late] + [extra[1]], axis=0), x_pairs(1))
    l_minus = shift(jnp.concatenate([col[a] for a in late] + [extra[nx - 1]], axis=0), x_pairs(nx - 1))
    add(l_plus, [(a, 1) for a in late] + [("e", 1)])
    add(l_minus, [(a, nx - 1) for a in late] + [("e", nx - 1)])
    if late:
        relay = l_minus[: prow * len(late)]
        add(shift(relay, x_pairs(nx - 1)), [(a, 2) for a in late])
    add(shift(extra[2], x_pairs(2)), [("e", 2)])
    kv_own = jnp.concatenate(parts[:reach + 3], axis=0)
    kv_rest = jnp.concatenate(parts[reach + 3:], axis=0)

    n_slots = len(tags)
    table = np.zeros((reach + 1, nx), np.int32)
    for s, (a, d) in enumerate(tags):
        if a == "e":
            table[0, d] = s
            table[reach, d] = s
        else:
            table[a, d] = s
    tails = kv_own[: (reach + 1) * prow].reshape(reach + 1, prow, -1)
    tails = tails[:, rows_here:rows_here + 2, :nx * N_DOC_IDS]
    tails = tails.astype(jnp.int32)
    below_col = (tails[:, 0, :] * 32 + tails[:, 1, :]).reshape(reach + 1, nx, N_DOC_IDS)
    a_ids = np.arange(reach + 1)[:, None]
    d_ids = np.arange(nx)[None, :]
    src_ctx = (zq - a_ids) * nx + (xq - d_ids) % nx
    floor_ctx = jnp.maximum(ctx - reach * nx, 0)
    use = (src_ctx >= floor_ctx) & (src_ctx <= ctx)
    below_sum = jnp.sum(jnp.where(use[:, :, None], below_col, 0), axis=(0, 1))
    onehot = doc_ids[:, None] == docs[None, :]
    doc_start = floor_ctx * rows_here + jnp.sum(jnp.where(onehot, below_sum[None, :], 0), axis=1)

    def slot_of(kb):
        cp = kb // per_dev
        a = zq - cp // nx
        d = (xq - cp % nx) % nx
        hit = (a[..., None, None] == np.arange(reach + 1)[:, None]) & (
            d[..., None, None] == np.arange(nx)[None, :]
        )
        slot = jnp.sum(jnp.where(hit, table, 0), axis=(-2, -1))
        return (slot * prow + (kb % per_dev) * BLOCK) // 16

    outputs = attention(
        query_local, kv_own, kv_rest, doc_start.astype(jnp.int32), block_keep, first_row,
        window, n_ctx * per_dev, slot_of,
    )
    return lax.all_to_all(outputs, "kvh", split_axis=0, concat_axis=1, tiled=True)


def solution(mesh):
    return jax.shard_map(
        local,
        mesh=mesh,
        in_specs=(
            P(("ctx", "kvh"), None),
            P(("ctx", "kvh"), None),
            P(("ctx", "kvh"), None),
            P("ctx"),
            P("ctx", None),
        ),
        out_specs=P(("ctx", "kvh"), None),
        check_vma=False,
    )
```

```python
import functools

import numpy as np

import jax
import jax.numpy as jnp
from jax import lax
from jax.experimental import pallas as pl
from jax.experimental.pallas import tpu as pltpu
from jax.sharding import PartitionSpec as P

HD = 128
BLOCK = 128
NX = 4
N_DOC_IDS = 8
KEY_GROUP = 4


def attn_kernel(
    tab_ref, cnt_ref, keep_ref, base_ref,
    qds_ref, q_ref, kv_ref, *rest,
    heads, window, first, last, row_base,
):
    if first:
        state_in = ()
    else:
        state_in, rest = rest[:3], rest[3:]
    outs, (m_sc, l_sc, acc_sc) = rest[:-3], rest[-3:]
    qbl = pl.program_id(0)
    qpos0 = base_ref[0] + qbl * BLOCK
    scale = HD ** (-0.5)
    width = heads * BLOCK
    qpos = qpos0 + lax.broadcasted_iota(jnp.int32, (BLOCK, BLOCK), 1)
    krel = lax.broadcasted_iota(jnp.int32, (BLOCK, BLOCK), 0)
    qds = qds_ref[pl.ds(qbl, 1), :]
    qmat = q_ref[...].reshape(width, HD)

    if first:
        m_sc[...] = jnp.full(m_sc.shape, -1e30, jnp.float32)
        l_sc[...] = jnp.zeros(l_sc.shape, jnp.float32)
        acc_sc[...] = jnp.zeros(acc_sc.shape, jnp.float32)
    else:
        acc_in, m_in, l_in = state_in
        acc_sc[...] = acc_in[...]
        m_sc[...] = m_in[0:1, :]
        l_sc[...] = l_in[0:1, :]

    def mask_of(kb):
        kpos = kb * BLOCK + krel
        keep = keep_ref[qbl, kb]
        earlier = (kpos < qpos) & (qpos - kpos < window) & (kpos >= qds) & (keep != 0)
        return (kpos == qpos) | earlier

    def absorb(ents, masked):
        starts = [pl.multiple_of((rb - row_base) * 16, 16) for _, rb, _, _ in ents]
        k = jnp.concatenate([kv_ref[pl.ds(st, BLOCK), :HD] for st in starts], axis=0)
        v = jnp.concatenate([kv_ref[pl.ds(st, BLOCK), HD:] for st in starts], axis=0)
        s = lax.dot_general(
            k, qmat, (((1,), (1,)), ((), ())), preferred_element_type=jnp.float32
        ) * scale
        if masked:
            allowed = jnp.concatenate(
                [
                    (mask_of(kb) | (kind == 0)) & valid
                    for kb, _, kind, valid in ents
                ],
                axis=0,
            )
            s = jnp.where(jnp.tile(allowed, (1, heads)), s, -1e30)
        m_prev = m_sc[...]
        m_new = jnp.maximum(m_prev, jnp.max(s, axis=0, keepdims=True))
        alpha = jnp.exp(m_prev - m_new)
        p = jnp.exp(s - m_new)
        l_sc[...] = alpha * l_sc[...] + jnp.sum(p, axis=0, keepdims=True)
        acc_sc[...] = acc_sc[...] * alpha + lax.dot_general(
            v, p.astype(jnp.bfloat16), (((0,), (0,)), ((), ())),
            preferred_element_type=jnp.float32,
        )
        m_sc[...] = m_new

    lo = cnt_ref[qbl, 0]
    hi = cnt_ref[qbl, 1]

    def body(i, carry):
        n = lo + KEY_GROUP * i
        ents = []
        any_masked = False
        for j in range(KEY_GROUP):
            e = tab_ref[qbl, jnp.minimum(n + j, hi - 1)]
            valid = n + j < hi
            kind = jnp.where(valid, e >> 20, 1)
            ents.append((e & 255, (e >> 8) & 4095, kind, valid))
            any_masked = any_masked | (kind != 0)

        @pl.when(jnp.logical_not(any_masked))
        def _():
            absorb(ents, False)

        @pl.when(any_masked)
        def _():
            absorb(ents, True)

        return carry

    lax.fori_loop(0, (hi - lo + KEY_GROUP - 1) // KEY_GROUP, body, 0)

    if last:
        (o_ref,) = outs
        out = acc_sc[...] / l_sc[...]
        for h in range(heads):
            o_ref[:, h * HD:(h + 1) * HD] = out[:, h * BLOCK:(h + 1) * BLOCK].T.astype(o_ref.dtype)
    else:
        acc_o, m_o, l_o = outs
        acc_o[...] = acc_sc[...]
        m_o[...] = jnp.broadcast_to(m_sc[...], m_o.shape)
        l_o[...] = jnp.broadcast_to(l_sc[...], l_o.shape)


def block_tables(doc_start_q, keep_rows, first_blk, nkb, window, slot_of, own_rows):
    nqb = keep_rows.shape[0]
    nwin = window // BLOCK
    ds_blocks = doc_start_q.reshape(nqb, BLOCK)
    ds_first = ds_blocks[:, :1]
    ds_last = ds_blocks[:, -1:]
    qb = first_blk + jnp.arange(nqb, dtype=jnp.int32)[:, None]
    kb = jnp.arange(nkb, dtype=jnp.int32)[None, :]
    diag = kb == qb
    inwin = (kb <= qb) & (kb >= qb - nwin)
    keep = keep_rows == 1
    needed = inwin & (diag | (keep & (kb * BLOCK + BLOCK - 1 >= ds_first)))
    full = needed & (~diag) & (kb > qb - nwin) & (kb * BLOCK >= ds_last) & keep
    row_blk = jnp.clip(slot_of(kb), 0, 4095)
    own = row_blk < own_rows
    rank = jnp.where(diag, 0, jnp.where(full, 1, 2))
    sort_key = jnp.where(needed, jnp.where(own, rank, 3 + rank), 6).astype(jnp.int32)
    payload = (kb + 256 * row_blk + (1 << 20) * jnp.where(full, 0, 1)).astype(jnp.int32)
    payload = jnp.broadcast_to(payload, sort_key.shape)
    _, tab = lax.sort((sort_key, payload), dimension=1, is_stable=True, num_keys=1)
    n_own = jnp.sum(needed & own, axis=1).astype(jnp.int32)
    n_all = jnp.sum(needed, axis=1).astype(jnp.int32)
    zero = jnp.zeros_like(n_own)
    return tab, jnp.stack([zero, n_own], 1), jnp.stack([n_own, n_all], 1), ds_blocks


def attend_call(tab, cnt, keep_rows, base, ds_blocks, q_t, kv, state, *, window, first, last, row_base):
    heads, rows_here, _ = q_t.shape
    nqb = rows_here // BLOCK
    width = heads * BLOCK
    nk = kv.shape[0]
    kernel = functools.partial(
        attn_kernel, heads=heads, window=window, first=first, last=last, row_base=row_base
    )
    in_specs = [
        pl.BlockSpec((nqb, BLOCK), lambda i, *_: (0, 0)),
        pl.BlockSpec((heads, BLOCK, HD), lambda i, *_: (0, i, 0)),
        pl.BlockSpec((nk, 2 * HD), lambda i, *_: (0, 0)),
    ]
    state_specs = [
        pl.BlockSpec((HD, width), lambda i, *_: (i, 0)),
        pl.BlockSpec((8, width), lambda i, *_: (i, 0)),
        pl.BlockSpec((8, width), lambda i, *_: (i, 0)),
    ]
    state_shapes = [
        jax.ShapeDtypeStruct((nqb * HD, width), jnp.float32),
        jax.ShapeDtypeStruct((nqb * 8, width), jnp.float32),
        jax.ShapeDtypeStruct((nqb * 8, width), jnp.float32),
    ]
    args = [tab, cnt, keep_rows, base, ds_blocks, q_t, kv]
    if not first:
        in_specs += state_specs
        args += list(state)
    if last:
        out_specs = pl.BlockSpec((BLOCK, width), lambda i, *_: (i, 0))
        out_shape = jax.ShapeDtypeStruct((rows_here, width), q_t.dtype)
    else:
        out_specs = state_specs
        out_shape = state_shapes
    grid_spec = pltpu.PrefetchScalarGridSpec(
        num_scalar_prefetch=4,
        grid=(nqb,),
        in_specs=in_specs,
        out_specs=out_specs,
        scratch_shapes=[
            pltpu.VMEM((1, width), jnp.float32),
            pltpu.VMEM((1, width), jnp.float32),
            pltpu.VMEM((HD, width), jnp.float32),
        ],
    )
    flops = 4 * rows_here * heads * HD * BLOCK * 8
    cost = pl.CostEstimate(flops=flops, transcendentals=flops // (4 * HD), bytes_accessed=nk * 4 * HD)
    return pl.pallas_call(
        kernel, grid_spec=grid_spec, out_shape=out_shape, cost_estimate=cost
    )(*args)


def attention(q_local, kv_own, kv_rest, doc_start_q, keep_rows, first_row, window, nkb, slot_of):
    rows_here = q_local.shape[0]
    heads = q_local.shape[1] // HD
    first_blk = first_row // BLOCK
    own_rows = kv_own.shape[0] // 16
    tab, cnt_a, cnt_b, ds_blocks = block_tables(
        doc_start_q, keep_rows, first_blk, nkb, window, slot_of, own_rows
    )
    base = jnp.reshape(first_row, (1,)).astype(jnp.int32)
    keep_i = keep_rows.astype(jnp.int32)
    q_t = jnp.transpose(q_local.reshape(rows_here, heads, HD), (1, 0, 2))
    state = attend_call(
        tab, cnt_a, keep_i, base, ds_blocks, q_t, kv_own, None,
        window=window, first=True, last=False, row_base=0,
    )
    return attend_call(
        tab, cnt_b, keep_i, base, ds_blocks, q_t, kv_rest, state,
        window=window, first=False, last=True, row_base=own_rows,
    )


def shift(x, pairs):
    return lax.ppermute(x, "ctx", pairs)


def local(queries, keys, values, doc_ids, block_keep):
    rows_in = keys.shape[0]
    groups = keys.shape[1] // HD
    kv = jnp.concatenate(
        [keys.reshape(rows_in, groups, HD), values.reshape(rows_in, groups, HD)], axis=2
    ).reshape(rows_in, -1)
    kv_local = lax.all_to_all(kv, "kvh", split_axis=1, concat_axis=0, tiled=True)
    rows_here = kv_local.shape[0]
    per_dev = rows_here // BLOCK
    n_ctx = lax.axis_size("ctx")
    nx = NX
    nz = n_ctx // nx
    reach = n_ctx // 2 // nx
    window = (n_ctx // 2) * rows_here
    ctx = lax.axis_index("ctx")
    first_row = ctx * rows_here
    zq, xq = ctx // nx, ctx % nx

    def x_pairs(d):
        return [(z * nx + x, z * nx + (x + d) % nx) for z in range(nz) for x in range(nx)]

    docs = jnp.arange(N_DOC_IDS, dtype=jnp.int32)
    below = jnp.sum((doc_ids[None, :] < docs[:, None]).astype(jnp.int32), axis=1)
    below_x = jnp.stack(
        [below] + [shift(below, x_pairs(d)) for d in range(1, nx)], axis=0
    ).reshape(-1)
    tail = jnp.zeros((16, kv_local.shape[1]), jnp.float32)
    tail = tail.at[0, :nx * N_DOC_IDS].set((below_x // 32).astype(jnp.float32))
    tail = tail.at[1, :nx * N_DOC_IDS].set((below_x % 32).astype(jnp.float32))
    piece = jnp.concatenate([kv_local, tail.astype(kv_local.dtype)], axis=0)
    prow = piece.shape[0]

    z_step = [(c, (c + nx) % n_ctx) for c in range(n_ctx)]

    col = [piece]
    for _ in range(reach):
        col.append(shift(col[-1], z_step))
    queries, _ = lax.optimization_barrier((queries, col[2]))
    query_local = lax.all_to_all(queries, "kvh", split_axis=1, concat_axis=0, tiled=True)
    half = (reach + 1) // 2
    early = list(range(1, half + 1))
    late = list(range(half + 1, reach))
    parts, tags = list(col), [(a, 0) for a in range(reach + 1)]

    def add(arr, tag_list):
        parts.append(arr)
        tags.extend(tag_list)

    def blocks(idx):
        return jnp.concatenate([col[a] for a in idx], axis=0) if len(idx) > 1 else col[idx[0]]

    e_plus = shift(blocks(early), x_pairs(1))
    e_minus = shift(blocks(early), x_pairs(nx - 1))
    add(e_plus, [(a, 1) for a in early])
    add(e_minus, [(a, nx - 1) for a in early])
    add(shift(e_plus, x_pairs(1)), [(a, 2) for a in early])
    extra = {d: jnp.where(xq + d < nx, col[0], col[reach]) for d in range(1, nx)}
    l_plus = shift(jnp.concatenate([col[a] for a in late] + [extra[1]], axis=0), x_pairs(1))
    l_minus = shift(jnp.concatenate([col[a] for a in late] + [extra[nx - 1]], axis=0), x_pairs(nx - 1))
    add(l_plus, [(a, 1) for a in late] + [("e", 1)])
    add(l_minus, [(a, nx - 1) for a in late] + [("e", nx - 1)])
    if late:
        relay = l_minus[: prow * len(late)]
        add(shift(relay, x_pairs(nx - 1)), [(a, 2) for a in late])
    add(shift(extra[2], x_pairs(2)), [("e", 2)])
    kv_own = jnp.concatenate(parts[:reach + 3], axis=0)
    kv_rest = jnp.concatenate(parts[reach + 3:], axis=0)

    n_slots = len(tags)
    table = np.zeros((reach + 1, nx), np.int32)
    for s, (a, d) in enumerate(tags):
        if a == "e":
            table[0, d] = s
            table[reach, d] = s
        else:
            table[a, d] = s
    tails = kv_own[: (reach + 1) * prow].reshape(reach + 1, prow, -1)
    tails = tails[:, rows_here:rows_here + 2, :nx * N_DOC_IDS]
    tails = tails.astype(jnp.int32)
    below_col = (tails[:, 0, :] * 32 + tails[:, 1, :]).reshape(reach + 1, nx, N_DOC_IDS)
    a_ids = np.arange(reach + 1)[:, None]
    d_ids = np.arange(nx)[None, :]
    src_ctx = (zq - a_ids) * nx + (xq - d_ids) % nx
    floor_ctx = jnp.maximum(ctx - reach * nx, 0)
    use = (src_ctx >= floor_ctx) & (src_ctx <= ctx)
    below_sum = jnp.sum(jnp.where(use[:, :, None], below_col, 0), axis=(0, 1))
    onehot = doc_ids[:, None] == docs[None, :]
    doc_start = floor_ctx * rows_here + jnp.sum(jnp.where(onehot, below_sum[None, :], 0), axis=1)

    def slot_of(kb):
        cp = kb // per_dev
        a = zq - cp // nx
        d = (xq - cp % nx) % nx
        hit = (a[..., None, None] == np.arange(reach + 1)[:, None]) & (
            d[..., None, None] == np.arange(nx)[None, :]
        )
        slot = jnp.sum(jnp.where(hit, table, 0), axis=(-2, -1))
        return (slot * prow + (kb % per_dev) * BLOCK) // 16

    outputs = attention(
        query_local, kv_own, kv_rest, doc_start.astype(jnp.int32), block_keep, first_row,
        window, n_ctx * per_dev, slot_of,
    )
    return lax.all_to_all(outputs, "kvh", split_axis=0, concat_axis=1, tiled=True)


def solution(mesh):
    return jax.shard_map(
        local,
        mesh=mesh,
        in_specs=(
            P(("ctx", "kvh"), None),
            P(("ctx", "kvh"), None),
            P(("ctx", "kvh"), None),
            P("ctx"),
            P("ctx", None),
        ),
        out_specs=P(("ctx", "kvh"), None),
        check_vma=False,
    )
```

```python
import functools

import numpy as np

import jax
import jax.numpy as jnp
from jax import lax
from jax.experimental import pallas as pl
from jax.experimental.pallas import tpu as pltpu
from jax.sharding import PartitionSpec as P

HD = 128
BLOCK = 128
NX = 4
N_DOC_IDS = 8
KEY_GROUP = 4


def attn_kernel(
    tab_ref, cnt_ref, keep_ref, base_ref,
    qds_ref, q_ref, kv_ref, *rest,
    heads, window, first, last, row_base,
):
    if first:
        state_in = ()
    else:
        state_in, rest = rest[:3], rest[3:]
    outs, (m_sc, l_sc, acc_sc) = rest[:-3], rest[-3:]
    qbl = pl.program_id(0)
    qpos0 = base_ref[0] + qbl * BLOCK
    scale = HD ** (-0.5)
    width = heads * BLOCK
    qpos = qpos0 + lax.broadcasted_iota(jnp.int32, (BLOCK, BLOCK), 1)
    krel = lax.broadcasted_iota(jnp.int32, (BLOCK, BLOCK), 0)
    qds = qds_ref[pl.ds(qbl, 1), :]
    qmat = jnp.concatenate([q_ref[:, h * HD:(h + 1) * HD] for h in range(heads)], axis=0)

    if first:
        m_sc[...] = jnp.full(m_sc.shape, -1e30, jnp.float32)
        l_sc[...] = jnp.zeros(l_sc.shape, jnp.float32)
        acc_sc[...] = jnp.zeros(acc_sc.shape, jnp.float32)
    else:
        acc_in, m_in, l_in = state_in
        acc_sc[...] = acc_in[...]
        m_sc[...] = m_in[0:1, :]
        l_sc[...] = l_in[0:1, :]

    def mask_of(kb):
        kpos = kb * BLOCK + krel
        keep = keep_ref[qbl, kb]
        earlier = (kpos < qpos) & (qpos - kpos < window) & (kpos >= qds) & (keep != 0)
        return (kpos == qpos) | earlier

    def absorb(ents, masked):
        starts = [pl.multiple_of((rb - row_base) * 16, 16) for _, rb, _, _ in ents]
        k = jnp.concatenate([kv_ref[pl.ds(st, BLOCK), :HD] for st in starts], axis=0)
        v = jnp.concatenate([kv_ref[pl.ds(st, BLOCK), HD:] for st in starts], axis=0)
        s = lax.dot_general(
            k, qmat, (((1,), (1,)), ((), ())), preferred_element_type=jnp.float32
        ) * scale
        if masked:
            allowed = jnp.concatenate(
                [
                    (mask_of(kb) | (kind == 0)) & valid
                    for kb, _, kind, valid in ents
                ],
                axis=0,
            )
            s = jnp.where(jnp.tile(allowed, (1, heads)), s, -1e30)
        m_prev = m_sc[...]
        m_new = jnp.maximum(m_prev, jnp.max(s, axis=0, keepdims=True))
        alpha = jnp.exp(m_prev - m_new)
        p = jnp.exp(s - m_new)
        l_sc[...] = alpha * l_sc[...] + jnp.sum(p, axis=0, keepdims=True)
        acc_sc[...] = acc_sc[...] * alpha + lax.dot_general(
            v, p.astype(jnp.bfloat16), (((0,), (0,)), ((), ())),
            preferred_element_type=jnp.float32,
        )
        m_sc[...] = m_new

    lo = cnt_ref[qbl, 0]
    hi = cnt_ref[qbl, 1]

    def body(i, carry):
        n = lo + KEY_GROUP * i
        ents = []
        any_masked = False
        for j in range(KEY_GROUP):
            e = tab_ref[qbl, jnp.minimum(n + j, hi - 1)]
            valid = n + j < hi
            kind = jnp.where(valid, e >> 20, 1)
            ents.append((e & 255, (e >> 8) & 4095, kind, valid))
            any_masked = any_masked | (kind != 0)

        @pl.when(jnp.logical_not(any_masked))
        def _():
            absorb(ents, False)

        @pl.when(any_masked)
        def _():
            absorb(ents, True)

        return carry

    lax.fori_loop(0, (hi - lo + KEY_GROUP - 1) // KEY_GROUP, body, 0)

    if last:
        (o_ref,) = outs
        out = acc_sc[...] / l_sc[...]
        for h in range(heads):
            o_ref[:, h * HD:(h + 1) * HD] = out[:, h * BLOCK:(h + 1) * BLOCK].T.astype(o_ref.dtype)
    else:
        acc_o, m_o, l_o = outs
        acc_o[...] = acc_sc[...]
        m_o[...] = jnp.broadcast_to(m_sc[...], m_o.shape)
        l_o[...] = jnp.broadcast_to(l_sc[...], l_o.shape)


def block_tables(doc_start_q, keep_rows, first_blk, nkb, window, slot_of, own_rows):
    nqb = keep_rows.shape[0]
    nwin = window // BLOCK
    ds_blocks = doc_start_q.reshape(nqb, BLOCK)
    ds_first = ds_blocks[:, :1]
    ds_last = ds_blocks[:, -1:]
    qb = first_blk + jnp.arange(nqb, dtype=jnp.int32)[:, None]
    kb = jnp.arange(nkb, dtype=jnp.int32)[None, :]
    diag = kb == qb
    inwin = (kb <= qb) & (kb >= qb - nwin)
    keep = keep_rows == 1
    needed = inwin & (diag | (keep & (kb * BLOCK + BLOCK - 1 >= ds_first)))
    full = needed & (~diag) & (kb > qb - nwin) & (kb * BLOCK >= ds_last) & keep
    row_blk = jnp.clip(slot_of(kb), 0, 4095)
    own = row_blk < own_rows
    rank = jnp.where(diag, 0, jnp.where(full, 1, 2))
    sort_key = jnp.where(needed, jnp.where(own, rank, 3 + rank), 6).astype(jnp.int32)
    payload = (kb + 256 * row_blk + (1 << 20) * jnp.where(full, 0, 1)).astype(jnp.int32)
    payload = jnp.broadcast_to(payload, sort_key.shape)
    _, tab = lax.sort((sort_key, payload), dimension=1, is_stable=True, num_keys=1)
    n_own = jnp.sum(needed & own, axis=1).astype(jnp.int32)
    n_all = jnp.sum(needed, axis=1).astype(jnp.int32)
    zero = jnp.zeros_like(n_own)
    return tab, jnp.stack([zero, n_own], 1), jnp.stack([n_own, n_all], 1), ds_blocks


def attend_call(tab, cnt, keep_rows, base, ds_blocks, q_t, kv, state, *, window, first, last, row_base):
    rows_here = q_t.shape[0]
    heads = q_t.shape[1] // HD
    nqb = rows_here // BLOCK
    width = heads * BLOCK
    nk = kv.shape[0]
    kernel = functools.partial(
        attn_kernel, heads=heads, window=window, first=first, last=last, row_base=row_base
    )
    in_specs = [
        pl.BlockSpec((nqb, BLOCK), lambda i, *_: (0, 0)),
        pl.BlockSpec((BLOCK, heads * HD), lambda i, *_: (i, 0)),
        pl.BlockSpec((nk, 2 * HD), lambda i, *_: (0, 0)),
    ]
    state_specs = [
        pl.BlockSpec((HD, width), lambda i, *_: (i, 0)),
        pl.BlockSpec((8, width), lambda i, *_: (i, 0)),
        pl.BlockSpec((8, width), lambda i, *_: (i, 0)),
    ]
    state_shapes = [
        jax.ShapeDtypeStruct((nqb * HD, width), jnp.float32),
        jax.ShapeDtypeStruct((nqb * 8, width), jnp.float32),
        jax.ShapeDtypeStruct((nqb * 8, width), jnp.float32),
    ]
    args = [tab, cnt, keep_rows, base, ds_blocks, q_t, kv]
    if not first:
        in_specs += state_specs
        args += list(state)
    if last:
        out_specs = pl.BlockSpec((BLOCK, width), lambda i, *_: (i, 0))
        out_shape = jax.ShapeDtypeStruct((rows_here, width), q_t.dtype)
    else:
        out_specs = state_specs
        out_shape = state_shapes
    grid_spec = pltpu.PrefetchScalarGridSpec(
        num_scalar_prefetch=4,
        grid=(nqb,),
        in_specs=in_specs,
        out_specs=out_specs,
        scratch_shapes=[
            pltpu.VMEM((1, width), jnp.float32),
            pltpu.VMEM((1, width), jnp.float32),
            pltpu.VMEM((HD, width), jnp.float32),
        ],
    )
    flops = 4 * rows_here * heads * HD * BLOCK * 8
    cost = pl.CostEstimate(flops=flops, transcendentals=flops // (4 * HD), bytes_accessed=nk * 4 * HD)
    return pl.pallas_call(
        kernel, grid_spec=grid_spec, out_shape=out_shape, cost_estimate=cost
    )(*args)


def attention(q_local, kv_own, kv_rest, doc_start_q, keep_rows, first_row, window, nkb, slot_of):
    rows_here = q_local.shape[0]
    heads = q_local.shape[1] // HD
    first_blk = first_row // BLOCK
    own_rows = kv_own.shape[0] // 16
    tab, cnt_a, cnt_b, ds_blocks = block_tables(
        doc_start_q, keep_rows, first_blk, nkb, window, slot_of, own_rows
    )
    base = jnp.reshape(first_row, (1,)).astype(jnp.int32)
    keep_i = keep_rows.astype(jnp.int32)
    q_t = q_local
    state = attend_call(
        tab, cnt_a, keep_i, base, ds_blocks, q_t, kv_own, None,
        window=window, first=True, last=False, row_base=0,
    )
    return attend_call(
        tab, cnt_b, keep_i, base, ds_blocks, q_t, kv_rest, state,
        window=window, first=False, last=True, row_base=own_rows,
    )


def shift(x, pairs):
    return lax.ppermute(x, "ctx", pairs)


def local(queries, keys, values, doc_ids, block_keep):
    rows_in = keys.shape[0]
    groups = keys.shape[1] // HD
    kv = jnp.concatenate(
        [keys.reshape(rows_in, groups, HD), values.reshape(rows_in, groups, HD)], axis=2
    ).reshape(rows_in, -1)
    kv_local = lax.all_to_all(kv, "kvh", split_axis=1, concat_axis=0, tiled=True)
    rows_here = kv_local.shape[0]
    per_dev = rows_here // BLOCK
    n_ctx = lax.axis_size("ctx")
    nx = NX
    nz = n_ctx // nx
    reach = n_ctx // 2 // nx
    window = (n_ctx // 2) * rows_here
    ctx = lax.axis_index("ctx")
    first_row = ctx * rows_here
    zq, xq = ctx // nx, ctx % nx

    def x_pairs(d):
        return [(z * nx + x, z * nx + (x + d) % nx) for z in range(nz) for x in range(nx)]

    docs = jnp.arange(N_DOC_IDS, dtype=jnp.int32)
    below = jnp.sum((doc_ids[None, :] < docs[:, None]).astype(jnp.int32), axis=1)
    below_x = jnp.stack(
        [below] + [shift(below, x_pairs(d)) for d in range(1, nx)], axis=0
    ).reshape(-1)
    tail = jnp.zeros((16, kv_local.shape[1]), jnp.float32)
    tail = tail.at[0, :nx * N_DOC_IDS].set((below_x // 32).astype(jnp.float32))
    tail = tail.at[1, :nx * N_DOC_IDS].set((below_x % 32).astype(jnp.float32))
    piece = jnp.concatenate([kv_local, tail.astype(kv_local.dtype)], axis=0)
    prow = piece.shape[0]

    z_step = [(c, (c + nx) % n_ctx) for c in range(n_ctx)]

    col = [piece]
    for _ in range(reach):
        col.append(shift(col[-1], z_step))
    queries, _ = lax.optimization_barrier((queries, col[1]))
    query_local = lax.all_to_all(queries, "kvh", split_axis=1, concat_axis=0, tiled=True)
    half = (reach + 1) // 2
    early = list(range(1, half + 1))
    late = list(range(half + 1, reach))
    parts, tags = list(col), [(a, 0) for a in range(reach + 1)]

    def add(arr, tag_list):
        parts.append(arr)
        tags.extend(tag_list)

    def blocks(idx):
        return jnp.concatenate([col[a] for a in idx], axis=0) if len(idx) > 1 else col[idx[0]]

    e_plus = shift(blocks(early), x_pairs(1))
    e_minus = shift(blocks(early), x_pairs(nx - 1))
    add(e_plus, [(a, 1) for a in early])
    add(e_minus, [(a, nx - 1) for a in early])
    add(shift(e_plus, x_pairs(1)), [(a, 2) for a in early])
    extra = {d: jnp.where(xq + d < nx, col[0], col[reach]) for d in range(1, nx)}
    l_plus = shift(jnp.concatenate([col[a] for a in late] + [extra[1]], axis=0), x_pairs(1))
    l_minus = shift(jnp.concatenate([col[a] for a in late] + [extra[nx - 1]], axis=0), x_pairs(nx - 1))
    add(l_plus, [(a, 1) for a in late] + [("e", 1)])
    add(l_minus, [(a, nx - 1) for a in late] + [("e", nx - 1)])
    if late:
        relay = l_minus[: prow * len(late)]
        add(shift(relay, x_pairs(nx - 1)), [(a, 2) for a in late])
    add(shift(extra[2], x_pairs(2)), [("e", 2)])
    kv_own = jnp.concatenate(parts[:reach + 3], axis=0)
    kv_rest = jnp.concatenate(parts[reach + 3:], axis=0)

    n_slots = len(tags)
    table = np.zeros((reach + 1, nx), np.int32)
    for s, (a, d) in enumerate(tags):
        if a == "e":
            table[0, d] = s
            table[reach, d] = s
        else:
            table[a, d] = s
    tails = kv_own[: (reach + 1) * prow].reshape(reach + 1, prow, -1)
    tails = tails[:, rows_here:rows_here + 2, :nx * N_DOC_IDS]
    tails = tails.astype(jnp.int32)
    below_col = (tails[:, 0, :] * 32 + tails[:, 1, :]).reshape(reach + 1, nx, N_DOC_IDS)
    a_ids = np.arange(reach + 1)[:, None]
    d_ids = np.arange(nx)[None, :]
    src_ctx = (zq - a_ids) * nx + (xq - d_ids) % nx
    floor_ctx = jnp.maximum(ctx - reach * nx, 0)
    use = (src_ctx >= floor_ctx) & (src_ctx <= ctx)
    below_sum = jnp.sum(jnp.where(use[:, :, None], below_col, 0), axis=(0, 1))
    onehot = doc_ids[:, None] == docs[None, :]
    doc_start = floor_ctx * rows_here + jnp.sum(jnp.where(onehot, below_sum[None, :], 0), axis=1)

    def slot_of(kb):
        cp = kb // per_dev
        a = zq - cp // nx
        d = (xq - cp % nx) % nx
        hit = (a[..., None, None] == np.arange(reach + 1)[:, None]) & (
            d[..., None, None] == np.arange(nx)[None, :]
        )
        slot = jnp.sum(jnp.where(hit, table, 0), axis=(-2, -1))
        return (slot * prow + (kb % per_dev) * BLOCK) // 16

    outputs = attention(
        query_local, kv_own, kv_rest, doc_start.astype(jnp.int32), block_keep, first_row,
        window, n_ctx * per_dev, slot_of,
    )
    return lax.all_to_all(outputs, "kvh", split_axis=0, concat_axis=1, tiled=True)


def solution(mesh):
    return jax.shard_map(
        local,
        mesh=mesh,
        in_specs=(
            P(("ctx", "kvh"), None),
            P(("ctx", "kvh"), None),
            P(("ctx", "kvh"), None),
            P("ctx"),
            P("ctx", None),
        ),
        out_specs=P(("ctx", "kvh"), None),
        check_vma=False,
    )
```
